32 devices in a mesh: tile: 8 (over z, y), pat: 4 (over x, core).
Axes of the slice: x: 2, y: 2, z: 4, core: 2. Of those that a mesh axis runs over, the one named last changes fastest.
Arguments:
- amplitudes: bfloat16 [1024, 128, 128], P(('tile', 'pat')), may hold values from 0.5 to 4
- batch_ids: int32 [2, 384], P(None, ('tile', 'pat')), may hold values from 0 to 31
- scan_tile: int32 [2, 384, 1], P(None, ('tile', 'pat')), may hold values from 0 to 7; in each aligned block of 12 rows (0 to 11, 12 to 23, ..., all dimensions but the last counted through in order) at most 3 rows name the same one
- scan_offset: int32 [2, 384, 2], P(None, ('tile', 'pat')), may hold values from 0 to 256
- object_tiles: float32 [2, 8, 384, 384], P(None, 'tile'), may hold values from -6 to 6
- probe: float32 [4, 2, 128, 128], replicated, may hold values from -3 to 3
Outputs:
- object_out: float32 [2, 8, 384, 384], P(None, 'tile')
- probe_out: float32 [4, 2, 128, 128], replicated
The draws below stay inside these ranges and needn't reach their ends.
Inputs may be any that keep to these rules, and one draw needn't show every extreme that they name: `scan_tile`: in each step, the 12 entries of one device name no tile more than 3 times, and some device's entries name one tile exactly 3 times.
All inputs are finite; a program needn't handle non-finite values.
Results may differ from the reference program's by a relative error of at most 0.019.
The reference program's roundings to bfloat16 on the way count: a program that leaves them out, or rounds other values in their place, can miss the bound.
Values may be sent and summed in bfloat16 or wider, within the bound.
No kernel may reach another device: no remote copies, remote signals or barrier semaphores. Data moves between devices by JAX's collectives and lax.ppermute only.
A program may use at most 64 MiB of HBM per device.

```python
import math
import jax
import jax.numpy as jnp
import numpy as np
from jax import lax

K = 128
MODES = 4
S = 384
STEPS = 2
BATCH_DEV = 12
STORE_DEV = 32
TILES = 8
BATCH = 384
PATTERNS = 1024
CAP = 3


def set_ends(entries, own_key, low, high):
    shape = entries.shape
    spot = [jax.random.randint(jax.random.fold_in(own_key, axis), (), 0, shape[axis]) for axis in range(len(shape))]
    entries = entries.at[tuple(spot)].set(low)
    longest = shape.index(max(shape))
    spot[longest] = (spot[longest] + 1) % shape[longest]
    return entries.at[tuple(spot)].set(high)


def level_of(stream_key, shape, cuts, smallest, largest):
    def one(axis_at, parts):
        draws = jax.random.uniform(jax.random.fold_in(jax.random.fold_in(stream_key, 6), axis_at), (parts,), jnp.float32, smallest / len(cuts), largest / len(cuts))
        return jnp.repeat(jnp.exp(draws), shape[axis_at] // parts).reshape((-1,) + (1,) * (len(shape) - axis_at - 1))

    factor_of = one(*cuts[0])
    for cut in cuts[1:]:
        factor_of = factor_of * one(*cut)
    return factor_of


def assign_block(rng, own, number, rows, count, top, reach, slope):
    sequence = jax.random.permutation(rng, count)
    crowded, ordinary = shares(count, rows * top, reach, slope, True), shares(count, rows * top, reach, slope, False)
    places = jnp.arange(count)

    def named(lengths, offset_by):
        used = int((lengths > 0).sum())
        fixed = max(1, used // 4)
        passed = fixed + (places - fixed + offset_by * (used - fixed)) % max(1, count - fixed)
        return jnp.zeros((count,), jnp.int32).at[sequence[jnp.where(places < fixed, places, passed)]].set(jnp.asarray(lengths, jnp.int32))

    lengths = jnp.where(number % 4 == 0, named(crowded, number // 4), named(ordinary, number - number // 4 - 1))
    mixed = jax.random.permutation(jax.random.fold_in(own, 3), count)
    giver, taker = mixed[0:count // 2 * 2:2], mixed[1:count // 2 * 2:2]
    room = jnp.minimum(lengths[giver] - 1, reach - lengths[taker]) // 2
    room = jnp.where((giver == sequence[0]) | (taker == sequence[0]) | (lengths[taker] == 0), 0, jnp.maximum(room, 0))
    passed = jax.random.randint(jax.random.fold_in(own, 4), (count // 2,), 0, 1 << 20) % (room + 1)
    lengths = lengths.at[giver].add(-passed).at[taker].add(passed)
    items = jnp.searchsorted(jnp.cumsum(lengths), jnp.arange(rows * top), side="right").astype(jnp.int32)
    table = items.reshape(top, rows).T
    table = table[jax.random.permutation(jax.random.fold_in(own, 1), rows)]
    offset_by = jax.random.randint(jax.random.fold_in(own, 2), (rows, 1), 0, top)
    return jnp.take_along_axis(table, (jnp.arange(top)[None, :] + offset_by) % top, axis=1)


def shares(count, total, bound, skew, full):
    portions = [(1 << 20) // math.isqrt(rank ** skew) + 1 for rank in range(1, count + 1)]
    largest = bound if full else min(bound, max(-(-total // count), total * portions[0] // sum(portions)))
    least = 1 if total - largest >= count - 1 else 0
    counts, surplus = [largest] + [least] * (count - 1), total - largest - least * (count - 1)
    while surplus > 0:
        free = [i for i in range(1, count) if counts[i] < largest] or [i for i in range(1, count) if counts[i] < bound]
        whole, remaining = sum([portions[i] for i in free]), surplus
        for i in free:
            addition = min(bound - counts[i], max(1, remaining * portions[i] // whole), surplus)
            counts[i] = counts[i] + addition
            surplus = surplus - addition
    return np.array(counts)


def scatter_about(own_key, dims, width, bound, split=(), kind=jnp.bfloat16):
    gain = level_of(own_key, dims, split, -0.22, 0.18) if split else 1.0
    drawn = jax.random.normal(own_key, dims, jnp.float32) * width * gain
    return jnp.minimum(jnp.maximum(drawn, -bound), bound).astype(kind)


def setup_inputs(seed: int = 0) -> dict:
    streams_of = jax.random.split(jax.random.key(seed), 7)
    amplitudes = jnp.clip(jnp.exp(math.log(4.0) - 2.0794415 * jax.random.uniform(streams_of[0], (PATTERNS, K, K), jnp.float32) ** level_of(streams_of[0], (PATTERNS, K, K), ((0, 32),), -0.2, 0.2)), 0.5, 4.0).astype(jnp.bfloat16)
    batch_ids = set_ends(jax.random.randint(streams_of[1], (STEPS, BATCH), 0, STORE_DEV), jax.random.fold_in(streams_of[1], 1), 0, STORE_DEV - 1).astype(jnp.int32)
    scan_tile_keys = jax.random.split(jax.random.fold_in(streams_of[2], 1), STEPS * BATCH // BATCH_DEV)
    scan_tile_turns = jax.random.permutation(jax.random.fold_in(streams_of[2], 3), STEPS * BATCH // BATCH_DEV)
    scan_tile = jax.vmap(lambda own, number: assign_block(jax.random.fold_in(streams_of[2], 2), own, number, BATCH_DEV, TILES, 1, CAP, 2))(scan_tile_keys, scan_tile_turns).reshape((STEPS, BATCH, 1))
    scan_offset = set_ends(jax.random.randint(streams_of[3], (STEPS, BATCH, 2), 0, S - K + 1), jax.random.fold_in(streams_of[3], 1), 0, S - K).astype(jnp.int32)
    object_tiles = scatter_about(streams_of[4], (2, TILES, S, S), 1.0, 6.0, ((1, 8),), jnp.float32)
    probe = scatter_about(streams_of[5], (MODES, 2, K, K), 0.5, 3.0, (), jnp.float32)
    return {"amplitudes": amplitudes, "batch_ids": batch_ids, "scan_tile": scan_tile, "scan_offset": scan_offset, "object_tiles": object_tiles, "probe": probe}


probe_rate = 8.0

def narrow_value(values):
    return lax.optimization_barrier(values.astype(jnp.bfloat16)).astype(jnp.float32)

def dft_tables(length):
    counter = jnp.arange(length, dtype=jnp.int32)
    product = counter[:, None] * counter[None, :] % length
    angle_table = 2.0 * math.pi / length * product.astype(jnp.float32)
    norm_factor = 1.0 / math.sqrt(length)
    table_re = narrow_value(jnp.cos(angle_table) * norm_factor)
    table_im = narrow_value(-jnp.sin(angle_table) * norm_factor)
    return (table_re, table_im)

def transform(src_re, src_im, table_re, table_im):
    half_re = jnp.einsum('kj,bmjc->bmkc', table_re, src_re) - jnp.einsum('kj,bmjc->bmkc', table_im, src_im)
    half_im = jnp.einsum('kj,bmjc->bmkc', table_re, src_im) + jnp.einsum('kj,bmjc->bmkc', table_im, src_re)
    half_re = narrow_value(half_re)
    half_im = narrow_value(half_im)
    out_re = jnp.einsum('bmkc,cl->bmkl', half_re, table_re) - jnp.einsum('bmkc,cl->bmkl', half_im, table_im)
    out_im = jnp.einsum('bmkc,cl->bmkl', half_re, table_im) + jnp.einsum('bmkc,cl->bmkl', half_im, table_re)
    return (out_re, out_im)

def one_step(tiles_now, probe_now, amplitudes, chosen, targets, offsets, table_re, table_im):
    probe_re = probe_now[:, 0]
    probe_im = probe_now[:, 1]
    block_rows = math.gcd(BATCH, 256)
    within = jnp.arange(K, dtype=jnp.int32)

    def block_pass(state_in, pieces_in):
        accum, grad_re, grad_im = state_in
        ids_now, tiles_idx, offs_now = pieces_in
        tile_sel = tiles_idx[:, None, None]
        rows_sel = offs_now[:, 0][:, None, None] + within[None, :, None]
        cols_sel = offs_now[:, 1][:, None, None] + within[None, None, :]
        patch = narrow_value(tiles_now[:, tile_sel, rows_sel, cols_sel])
        patch_re = patch[0][:, None]
        patch_im = patch[1][:, None]
        exit_re = narrow_value(probe_re[None] * patch_re - probe_im[None] * patch_im)
        exit_im = narrow_value(probe_re[None] * patch_im + probe_im[None] * patch_re)
        far_re, far_im = transform(exit_re, exit_im, table_re, table_im)
        intensity = lax.optimization_barrier(jnp.sum(far_re * far_re + far_im * far_im, axis=1))
        measured = amplitudes[ids_now].astype(jnp.float32)
        factor = (measured / jnp.sqrt(jnp.maximum(intensity, 1.0)) - 1.0)[:, None]
        scaled_re = narrow_value(factor * far_re)
        scaled_im = narrow_value(factor * far_im)
        change_re, change_im = transform(scaled_re, scaled_im, table_re, -table_im)
        update_re = narrow_value(lax.optimization_barrier(jnp.sum(probe_re[None] * change_re + probe_im[None] * change_im, axis=1)))
        update_im = narrow_value(lax.optimization_barrier(jnp.sum(probe_re[None] * change_im - probe_im[None] * change_re, axis=1)))
        grad_re = grad_re + lax.optimization_barrier(jnp.sum(patch_re * change_re + patch_im * change_im, axis=0))
        grad_im = grad_im + lax.optimization_barrier(jnp.sum(patch_re * change_im - patch_im * change_re, axis=0))
        accum = accum.at[:, tile_sel, rows_sel, cols_sel].add(jnp.stack([update_re, update_im]))
        return ((accum, grad_re, grad_im), None)
    zero_tiles = jnp.zeros(tiles_now.shape, jnp.float32)
    zero_probe = jnp.zeros(probe_re.shape, jnp.float32)
    blocks = BATCH // block_rows
    holders = jnp.arange(BATCH, dtype=jnp.int32) // BATCH_DEV
    global_ids = (holders * STORE_DEV + chosen).astype(jnp.int32)
    pieces_all = (global_ids.reshape(blocks, block_rows), targets.reshape(blocks, block_rows), offsets.reshape(blocks, block_rows, 2))
    (accum, grad_re, grad_im), unused = lax.scan(block_pass, (zero_tiles, zero_probe, zero_probe), pieces_all)
    peak_power = jnp.max(lax.optimization_barrier(jnp.sum(probe_re * probe_re + probe_im * probe_im, axis=0)))
    tiles_next = tiles_now + accum / peak_power
    probe_next = probe_now + probe_rate * jnp.stack([grad_re, grad_im], axis=1) / BATCH
    return (tiles_next, probe_next)

def reference(amplitudes, batch_ids, scan_tile, scan_offset, object_tiles, probe):
    table_re, table_im = dft_tables(K)
    tiles_now = object_tiles
    probe_now = probe
    for step_no in range(STEPS):
        tiles_now, probe_now = one_step(tiles_now, probe_now, amplitudes, batch_ids[step_no], scan_tile[step_no, :, 0], scan_offset[step_no], table_re, table_im)
    return (tiles_now, probe_now)
```

```python
import math

import jax
import jax.numpy as jnp
from jax import lax
from jax.sharding import PartitionSpec as P

probe_rate = 8.0


def dft_tables(length):
    counter = jnp.arange(length, dtype=jnp.int32)
    product = counter[:, None] * counter[None, :] % length
    angle_table = 2.0 * math.pi / length * product.astype(jnp.float32)
    norm_factor = 1.0 / math.sqrt(length)
    table_re = (jnp.cos(angle_table) * norm_factor).astype(jnp.bfloat16)
    table_im = (-jnp.sin(angle_table) * norm_factor).astype(jnp.bfloat16)
    return (table_re, table_im, -table_im)


def transform(src_re, src_im, table_re, table_im):
    half_re = jnp.einsum(
        "kj,bmjc->bmkc", table_re, src_re, preferred_element_type=jnp.float32
    ) - jnp.einsum("kj,bmjc->bmkc", table_im, src_im, preferred_element_type=jnp.float32)
    half_im = jnp.einsum(
        "kj,bmjc->bmkc", table_re, src_im, preferred_element_type=jnp.float32
    ) + jnp.einsum("kj,bmjc->bmkc", table_im, src_re, preferred_element_type=jnp.float32)
    half_re = half_re.astype(jnp.bfloat16)
    half_im = half_im.astype(jnp.bfloat16)
    out_re = jnp.einsum(
        "bmkc,cl->bmkl", half_re, table_re, preferred_element_type=jnp.float32
    ) - jnp.einsum("bmkc,cl->bmkl", half_im, table_im, preferred_element_type=jnp.float32)
    out_im = jnp.einsum(
        "bmkc,cl->bmkl", half_re, table_im, preferred_element_type=jnp.float32
    ) + jnp.einsum("bmkc,cl->bmkl", half_im, table_re, preferred_element_type=jnp.float32)
    return (out_re, out_im)


def route(amplitudes, batch_ids, scan_tile, scan_offset, tiles_here, size):
    tile_count = lax.axis_size("tile")
    steps, batch_rows = batch_ids.shape
    capacity = max(2, 2 * batch_rows // tile_count)
    slots = tile_count * capacity
    length = amplitudes.shape[-1]
    target = scan_tile[:, :, 0]
    owner = target // tiles_here
    local_tile = target - owner * tiles_here
    onehot = (owner[:, :, None] == jnp.arange(tile_count, dtype=jnp.int32)).astype(jnp.int32)
    place_in = jnp.sum((jnp.cumsum(onehot, axis=1) - 1) * onehot, axis=2)
    slot_of = owner * capacity + place_in
    chosen = slot_of[:, None, :] == jnp.arange(slots, dtype=jnp.int32)[None, :, None]
    valid = jnp.any(chosen, axis=2).astype(jnp.int32)
    entry = jnp.argmax(chosen, axis=2).astype(jnp.int32)
    row_at = local_tile * size + scan_offset[:, :, 0]
    col_at = scan_offset[:, :, 1]
    meta = jnp.stack(
        [
            jnp.take_along_axis(row_at, entry, axis=1),
            jnp.take_along_axis(col_at, entry, axis=1),
            valid,
        ],
        axis=2,
    )
    ids = jnp.take_along_axis(batch_ids, entry, axis=1)
    amp_send = amplitudes[ids.reshape(-1)].reshape(steps, tile_count, capacity, length, length)
    meta_in = lax.all_to_all(
        meta.reshape(steps, tile_count, capacity, 3), "tile", 1, 1, tiled=True
    ).reshape(steps, slots, 3)
    amp_in = lax.all_to_all(amp_send, "tile", 1, 1, tiled=True).reshape(
        steps, slots, length, length
    )
    return amp_in, meta_in


def group_size(axes):
    count = 1
    for axis in axes:
        count *= lax.axis_size(axis)
    return count


def sum_over(value, axes, send_type):
    count = group_size(axes)
    parts = lax.all_to_all(value.astype(send_type).reshape(count, -1), axes, 0, 0, tiled=True)
    total = jnp.sum(parts.astype(jnp.float32), axis=0, keepdims=True).astype(send_type)
    return total, count


def all_sum_a2a(value, axes):
    total, count = sum_over(value, axes, value.dtype)
    spread = lax.all_to_all(jnp.broadcast_to(total, (count, total.shape[1])), axes, 0, 0, tiled=True)
    return spread.reshape(value.shape)


def all_sum_gather(value, axes, send_type):
    total, count = sum_over(value, axes, send_type)
    return lax.all_gather(total, axes, axis=0, tiled=True).reshape(value.shape).astype(jnp.float32)


def entries_pass(stacked, probe_now, amp_in, meta_in, tables):
    table_re, table_im, table_neg = tables
    length = probe_now.shape[-1]
    rows_all, size = stacked.shape[1], stacked.shape[2]
    within = jnp.arange(length, dtype=jnp.int32)
    row_at, col_at, valid = meta_in[:, 0], meta_in[:, 1], meta_in[:, 2]
    pick_rows = (
        (row_at[:, None, None] + within[None, :, None])
        == jnp.arange(rows_all, dtype=jnp.int32)[None, None, :]
    ) & (valid[:, None, None] > 0)
    pick_rows = pick_rows.astype(jnp.bfloat16)
    pick_cols = (
        (col_at[:, None, None] + within[None, None, :])
        == jnp.arange(size, dtype=jnp.int32)[None, :, None]
    ).astype(jnp.bfloat16)
    rows = jnp.einsum(
        "skq,xqc->xskc", pick_rows, stacked, preferred_element_type=jnp.float32
    ).astype(jnp.bfloat16)
    patch = jnp.einsum("xskc,scl->xskl", rows, pick_cols, preferred_element_type=jnp.float32)
    probe_re = probe_now[:, 0]
    probe_im = probe_now[:, 1]
    patch_re = patch[0][:, None]
    patch_im = patch[1][:, None]
    exit_re = (probe_re[None] * patch_re - probe_im[None] * patch_im).astype(jnp.bfloat16)
    exit_im = (probe_re[None] * patch_im + probe_im[None] * patch_re).astype(jnp.bfloat16)
    far_re, far_im = transform(exit_re, exit_im, table_re, table_im)
    intensity = jnp.sum(far_re * far_re + far_im * far_im, axis=1)
    measured = amp_in.astype(jnp.float32)
    factor = (measured / jnp.sqrt(jnp.maximum(intensity, 1.0)) - 1.0)[:, None]
    scaled_re = (factor * far_re).astype(jnp.bfloat16)
    scaled_im = (factor * far_im).astype(jnp.bfloat16)
    change_re, change_im = transform(scaled_re, scaled_im, table_re, table_neg)
    update_re = jnp.sum(probe_re[None] * change_re + probe_im[None] * change_im, axis=1).astype(
        jnp.bfloat16
    )
    update_im = jnp.sum(probe_re[None] * change_im - probe_im[None] * change_re, axis=1).astype(
        jnp.bfloat16
    )
    grad_re = jnp.sum(patch_re * change_re + patch_im * change_im, axis=0)
    grad_im = jnp.sum(patch_re * change_im - patch_im * change_re, axis=0)
    probe_grad = jnp.stack([grad_re, grad_im], axis=1)
    update = jnp.stack([update_re, update_im])
    spread = jnp.einsum(
        "xskl,scl->xskc", update, pick_cols, preferred_element_type=jnp.float32
    ).astype(jnp.bfloat16)
    local_sum = jnp.einsum("skq,xskc->xqc", pick_rows, spread, preferred_element_type=jnp.float32)
    return local_sum, probe_grad


def one_step(tiles_now, probe_now, amp_in, meta_in, tables, batch_total):
    tiles_here, size = tiles_now.shape[1], tiles_now.shape[2]
    slots, length = amp_in.shape[0], amp_in.shape[-1]
    stacked = tiles_now.astype(jnp.bfloat16).reshape(2, tiles_here * size, size)
    chunk = max(d for d in range(1, min(slots, 24) + 1) if slots % d == 0)
    if chunk == slots:
        local_sum, probe_grad = entries_pass(stacked, probe_now, amp_in, meta_in, tables)
    else:

        def body(carry, piece):
            part_sum, part_grad = entries_pass(stacked, probe_now, piece[0], piece[1], tables)
            return (carry[0] + part_sum, carry[1] + part_grad), None

        start = (jnp.zeros(stacked.shape, jnp.float32), jnp.zeros(probe_now.shape, jnp.float32))
        pieces = (
            amp_in.reshape(slots // chunk, chunk, length, length),
            meta_in.reshape(slots // chunk, chunk, 3),
        )
        (local_sum, probe_grad), _ = lax.scan(body, start, pieces)
    local_sum = local_sum.reshape(tiles_now.shape)
    probe_re = probe_now[:, 0]
    probe_im = probe_now[:, 1]
    peak_power = jnp.max(jnp.sum(probe_re * probe_re + probe_im * probe_im, axis=0))
    summed = all_sum_gather(local_sum, ("pat",), jnp.bfloat16)
    tiles_next = tiles_now + summed / peak_power
    grad_sum = all_sum_a2a(probe_grad, ("tile", "pat"))
    probe_next = probe_now + probe_rate * grad_sum / batch_total
    return (tiles_next, probe_next)


def on_device(amplitudes, batch_ids, scan_tile, scan_offset, object_tiles, probe):
    tables = dft_tables(probe.shape[-1])
    tiles_here, size = object_tiles.shape[1], object_tiles.shape[2]
    batch_total = batch_ids.shape[1] * lax.axis_size("tile") * lax.axis_size("pat")
    amp_in, meta_in = route(amplitudes, batch_ids, scan_tile, scan_offset, tiles_here, size)
    tiles_now = object_tiles
    probe_now = probe
    for step_no in range(batch_ids.shape[0]):
        tiles_now, probe_now = one_step(
            tiles_now, probe_now, amp_in[step_no], meta_in[step_no], tables, batch_total
        )
    return (tiles_now, probe_now)


def solution(mesh):
    in_specs = (
        P(("tile", "pat"), None, None),
        P(None, ("tile", "pat")),
        P(None, ("tile", "pat"), None),
        P(None, ("tile", "pat"), None),
        P(None, "tile", None, None),
        P(),
    )
    out_specs = (P(None, "tile", None, None), P())
    return jax.shard_map(
        on_device, mesh=mesh, in_specs=in_specs, out_specs=out_specs, check_vma=False
    )
```

```python
import math

import jax
import jax.numpy as jnp
from jax import lax
from jax.experimental import pallas as pl
from jax.experimental.pallas import tpu as pltpu
from jax.sharding import PartitionSpec as P

probe_rate = 8.0


def dft_tables(length):
    counter = jnp.arange(length, dtype=jnp.int32)
    product = counter[:, None] * counter[None, :] % length
    angle_table = 2.0 * math.pi / length * product.astype(jnp.float32)
    norm_factor = 1.0 / math.sqrt(length)
    table_re = (jnp.cos(angle_table) * norm_factor).astype(jnp.bfloat16)
    table_im = (-jnp.sin(angle_table) * norm_factor).astype(jnp.bfloat16)
    return (table_re, table_im, -table_im)


def transform(src_re, src_im, table_re, table_im):
    half_re = jnp.einsum(
        "kj,bmjc->bmkc", table_re, src_re, preferred_element_type=jnp.float32
    ) - jnp.einsum("kj,bmjc->bmkc", table_im, src_im, preferred_element_type=jnp.float32)
    half_im = jnp.einsum(
        "kj,bmjc->bmkc", table_re, src_im, preferred_element_type=jnp.float32
    ) + jnp.einsum("kj,bmjc->bmkc", table_im, src_re, preferred_element_type=jnp.float32)
    half_re = half_re.astype(jnp.bfloat16)
    half_im = half_im.astype(jnp.bfloat16)
    out_re = jnp.einsum(
        "bmkc,cl->bmkl", half_re, table_re, preferred_element_type=jnp.float32
    ) - jnp.einsum("bmkc,cl->bmkl", half_im, table_im, preferred_element_type=jnp.float32)
    out_im = jnp.einsum(
        "bmkc,cl->bmkl", half_re, table_im, preferred_element_type=jnp.float32
    ) + jnp.einsum("bmkc,cl->bmkl", half_im, table_re, preferred_element_type=jnp.float32)
    return (out_re, out_im)


def block_tables(table_re, table_im):
    left = jnp.concatenate(
        [jnp.concatenate([table_re, -table_im], 1), jnp.concatenate([table_im, table_re], 1)], 0
    )
    right = jnp.concatenate(
        [jnp.concatenate([table_re, table_im], 1), jnp.concatenate([-table_im, table_re], 1)], 0
    )
    return left, right


def entry_kernel(patch_ref, amp_ref, probe_ref, left_ref, right_ref, update_ref, grad_ref):
    modes, length = probe_ref.shape[0], probe_ref.shape[-1]

    @pl.when(pl.program_id(0) == 0)
    def _():
        grad_ref[...] = jnp.zeros(grad_ref.shape, grad_ref.dtype)

    patch_re = patch_ref[0].astype(jnp.float32)
    patch_im = patch_ref[1].astype(jnp.float32)
    left = left_ref[...]
    right = right_ref[...]
    exits_re, exits_im = [], []
    for m in range(modes):
        probe_re = probe_ref[m, 0]
        probe_im = probe_ref[m, 1]
        exits_re.append((probe_re * patch_re - probe_im * patch_im).astype(jnp.bfloat16))
        exits_im.append((probe_re * patch_im + probe_im * patch_re).astype(jnp.bfloat16))
    stacked = jnp.concatenate(
        [jnp.concatenate(exits_re, 1), jnp.concatenate(exits_im, 1)], 0
    )
    half = jnp.dot(left, stacked, preferred_element_type=jnp.float32).astype(jnp.bfloat16)

    def by_mode(wide):
        return jnp.concatenate(
            [
                jnp.concatenate(
                    [
                        wide[:length, m * length : (m + 1) * length],
                        wide[length:, m * length : (m + 1) * length],
                    ],
                    1,
                )
                for m in range(modes)
            ],
            0,
        )

    def by_part(tall):
        return jnp.concatenate(
            [
                jnp.concatenate(
                    [tall[m * length : (m + 1) * length, :length] for m in range(modes)], 1
                ),
                jnp.concatenate(
                    [tall[m * length : (m + 1) * length, length:] for m in range(modes)], 1
                ),
            ],
            0,
        )

    far = jnp.dot(by_mode(half), right, preferred_element_type=jnp.float32)
    intensity = jnp.zeros((length, length), jnp.float32)
    for m in range(modes):
        far_re = far[m * length : (m + 1) * length, :length]
        far_im = far[m * length : (m + 1) * length, length:]
        intensity = intensity + (far_re * far_re + far_im * far_im)
    measured = amp_ref[...].astype(jnp.float32)
    factor = measured / jnp.sqrt(jnp.maximum(intensity, 1.0)) - 1.0
    factor = jnp.concatenate([factor, factor], 1)
    factor = jnp.concatenate([factor] * modes, 0)
    scaled = (factor * far).astype(jnp.bfloat16)
    back = jnp.dot(right, by_part(scaled), preferred_element_type=jnp.float32).astype(
        jnp.bfloat16
    )
    change = jnp.dot(by_mode(back), left, preferred_element_type=jnp.float32)
    update_re = jnp.zeros((length, length), jnp.float32)
    update_im = jnp.zeros((length, length), jnp.float32)
    for m in range(modes):
        change_re = change[m * length : (m + 1) * length, :length]
        change_im = change[m * length : (m + 1) * length, length:]
        probe_re = probe_ref[m, 0]
        probe_im = probe_ref[m, 1]
        update_re = update_re + (probe_re * change_re + probe_im * change_im)
        update_im = update_im + (probe_re * change_im - probe_im * change_re)
        grad_ref[m, 0] += patch_re * change_re + patch_im * change_im
        grad_ref[m, 1] += patch_re * change_im - patch_im * change_re
    update_ref[0] = update_re.astype(update_ref.dtype)
    update_ref[1] = update_im.astype(update_ref.dtype)


def entries_kernel(patch, amp_in, probe_now, left, right):
    slots, length = amp_in.shape[0], amp_in.shape[-1]
    modes = probe_now.shape[0]
    flops = slots * 4 * 2 * (2 * length) * (2 * length) * (modes * length)
    return pl.pallas_call(
        entry_kernel,
        grid=(slots,),
        in_specs=[
            pl.BlockSpec((2, None, length, length), lambda s: (0, s, 0, 0)),
            pl.BlockSpec((None, length, length), lambda s: (s, 0, 0)),
            pl.BlockSpec(probe_now.shape, lambda s: (0, 0, 0, 0)),
            pl.BlockSpec(left.shape, lambda s: (0, 0)),
            pl.BlockSpec(right.shape, lambda s: (0, 0)),
        ],
        out_specs=[
            pl.BlockSpec((2, None, length, length), lambda s: (0, s, 0, 0)),
            pl.BlockSpec(probe_now.shape, lambda s: (0, 0, 0, 0)),
        ],
        out_shape=[
            jax.ShapeDtypeStruct((2, slots, length, length), jnp.bfloat16),
            jax.ShapeDtypeStruct(probe_now.shape, jnp.float32),
        ],
        compiler_params=pltpu.CompilerParams(dimension_semantics=("arbitrary",)),
        cost_estimate=pl.CostEstimate(
            flops=flops,
            transcendentals=slots * length * length,
            bytes_accessed=slots * length * length * 10 + probe_now.size * 8,
        ),
    )(patch, amp_in, probe_now, left, right)


def route(amplitudes, batch_ids, scan_tile, scan_offset, tiles_here, size):
    tile_count = lax.axis_size("tile")
    steps, batch_rows = batch_ids.shape
    capacity = max(2, 2 * batch_rows // tile_count)
    slots = tile_count * capacity
    length = amplitudes.shape[-1]
    target = scan_tile[:, :, 0]
    owner = target // tiles_here
    local_tile = target - owner * tiles_here
    onehot = (owner[:, :, None] == jnp.arange(tile_count, dtype=jnp.int32)).astype(jnp.int32)
    place_in = jnp.sum((jnp.cumsum(onehot, axis=1) - 1) * onehot, axis=2)
    slot_of = owner * capacity + place_in
    chosen = slot_of[:, None, :] == jnp.arange(slots, dtype=jnp.int32)[None, :, None]
    valid = jnp.any(chosen, axis=2).astype(jnp.int32)
    entry = jnp.argmax(chosen, axis=2).astype(jnp.int32)
    row_at = local_tile * size + scan_offset[:, :, 0]
    col_at = scan_offset[:, :, 1]
    meta = jnp.stack(
        [
            jnp.take_along_axis(row_at, entry, axis=1),
            jnp.take_along_axis(col_at, entry, axis=1),
            valid,
        ],
        axis=2,
    )
    ids = jnp.take_along_axis(batch_ids, entry, axis=1)
    amp_send = amplitudes[ids.reshape(-1)].reshape(steps, tile_count, capacity, length, length)
    meta_in = lax.all_to_all(
        meta.reshape(steps, tile_count, capacity, 3), "tile", 1, 1, tiled=True
    ).reshape(steps, slots, 3)
    amp_in = lax.all_to_all(amp_send, "tile", 1, 1, tiled=True).reshape(
        steps, slots, length, length
    )
    return amp_in, meta_in


def group_size(axes):
    count = 1
    for axis in axes:
        count *= lax.axis_size(axis)
    return count


def sum_over(value, axes, send_type):
    count = group_size(axes)
    parts = lax.all_to_all(value.astype(send_type).reshape(count, -1), axes, 0, 0, tiled=True)
    total = jnp.sum(parts.astype(jnp.float32), axis=0, keepdims=True).astype(send_type)
    return total, count


def all_sum_a2a(value, axes):
    total, count = sum_over(value, axes, value.dtype)
    spread = lax.all_to_all(jnp.broadcast_to(total, (count, total.shape[1])), axes, 0, 0, tiled=True)
    return spread.reshape(value.shape)


def all_sum_gather(value, axes, send_type):
    total, count = sum_over(value, axes, send_type)
    return lax.all_gather(total, axes, axis=0, tiled=True).reshape(value.shape).astype(jnp.float32)


def entries_pass(stacked, probe_now, amp_in, meta_in, tables):
    table_re, table_im, table_neg = tables
    length = probe_now.shape[-1]
    rows_all, size = stacked.shape[1], stacked.shape[2]
    within = jnp.arange(length, dtype=jnp.int32)
    row_at, col_at, valid = meta_in[:, 0], meta_in[:, 1], meta_in[:, 2]
    pick_rows = (
        (row_at[:, None, None] + within[None, :, None])
        == jnp.arange(rows_all, dtype=jnp.int32)[None, None, :]
    ) & (valid[:, None, None] > 0)
    pick_rows = pick_rows.astype(jnp.bfloat16)
    pick_cols = (
        (col_at[:, None, None] + within[None, None, :])
        == jnp.arange(size, dtype=jnp.int32)[None, :, None]
    ).astype(jnp.bfloat16)
    rows = jnp.einsum(
        "skq,xqc->xskc", pick_rows, stacked, preferred_element_type=jnp.float32
    ).astype(jnp.bfloat16)
    patch = jnp.einsum("xskc,scl->xskl", rows, pick_cols, preferred_element_type=jnp.float32)
    left, right = block_tables(tables[0], tables[1])
    update, probe_grad = entries_kernel(patch.astype(jnp.bfloat16), amp_in, probe_now, left, right)
    spread = jnp.einsum(
        "xskl,scl->xskc", update, pick_cols, preferred_element_type=jnp.float32
    ).astype(jnp.bfloat16)
    local_sum = jnp.einsum("skq,xskc->xqc", pick_rows, spread, preferred_element_type=jnp.float32)
    return local_sum, probe_grad


def one_step(tiles_now, probe_now, amp_in, meta_in, tables, batch_total):
    tiles_here, size = tiles_now.shape[1], tiles_now.shape[2]
    slots, length = amp_in.shape[0], amp_in.shape[-1]
    stacked = tiles_now.astype(jnp.bfloat16).reshape(2, tiles_here * size, size)
    chunk = max(d for d in range(1, min(slots, 24) + 1) if slots % d == 0)
    if chunk == slots:
        local_sum, probe_grad = entries_pass(stacked, probe_now, amp_in, meta_in, tables)
    else:

        def body(carry, piece):
            part_sum, part_grad = entries_pass(stacked, probe_now, piece[0], piece[1], tables)
            return (carry[0] + part_sum, carry[1] + part_grad), None

        start = (jnp.zeros(stacked.shape, jnp.float32), jnp.zeros(probe_now.shape, jnp.float32))
        pieces = (
            amp_in.reshape(slots // chunk, chunk, length, length),
            meta_in.reshape(slots // chunk, chunk, 3),
        )
        (local_sum, probe_grad), _ = lax.scan(body, start, pieces)
    local_sum = local_sum.reshape(tiles_now.shape)
    probe_re = probe_now[:, 0]
    probe_im = probe_now[:, 1]
    peak_power = jnp.max(jnp.sum(probe_re * probe_re + probe_im * probe_im, axis=0))
    summed = all_sum_gather(local_sum, ("pat",), jnp.bfloat16)
    tiles_next = tiles_now + summed / peak_power
    grad_sum = all_sum_a2a(probe_grad, ("tile", "pat"))
    probe_next = probe_now + probe_rate * grad_sum / batch_total
    return (tiles_next, probe_next)


def on_device(amplitudes, batch_ids, scan_tile, scan_offset, object_tiles, probe):
    tables = dft_tables(probe.shape[-1])
    tiles_here, size = object_tiles.shape[1], object_tiles.shape[2]
    batch_total = batch_ids.shape[1] * lax.axis_size("tile") * lax.axis_size("pat")
    amp_in, meta_in = route(amplitudes, batch_ids, scan_tile, scan_offset, tiles_here, size)
    tiles_now = object_tiles
    probe_now = probe
    for step_no in range(batch_ids.shape[0]):
        tiles_now, probe_now = one_step(
            tiles_now, probe_now, amp_in[step_no], meta_in[step_no], tables, batch_total
        )
    return (tiles_now, probe_now)


def solution(mesh):
    in_specs = (
        P(("tile", "pat"), None, None),
        P(None, ("tile", "pat")),
        P(None, ("tile", "pat"), None),
        P(None, ("tile", "pat"), None),
        P(None, "tile", None, None),
        P(),
    )
    out_specs = (P(None, "tile", None, None), P())
    return jax.shard_map(
        on_device, mesh=mesh, in_specs=in_specs, out_specs=out_specs, check_vma=False
    )
```

```python
import math

import jax
import jax.numpy as jnp
from jax import lax
from jax.experimental import pallas as pl
from jax.experimental.pallas import tpu as pltpu
from jax.sharding import PartitionSpec as P

probe_rate = 8.0


def dft_tables(length):
    counter = jnp.arange(length, dtype=jnp.int32)
    product = counter[:, None] * counter[None, :] % length
    angle_table = 2.0 * math.pi / length * product.astype(jnp.float32)
    norm_factor = 1.0 / math.sqrt(length)
    table_re = (jnp.cos(angle_table) * norm_factor).astype(jnp.bfloat16)
    table_im = (-jnp.sin(angle_table) * norm_factor).astype(jnp.bfloat16)
    return (table_re, table_im, -table_im)


def transform(src_re, src_im, table_re, table_im):
    half_re = jnp.einsum(
        "kj,bmjc->bmkc", table_re, src_re, preferred_element_type=jnp.float32
    ) - jnp.einsum("kj,bmjc->bmkc", table_im, src_im, preferred_element_type=jnp.float32)
    half_im = jnp.einsum(
        "kj,bmjc->bmkc", table_re, src_im, preferred_element_type=jnp.float32
    ) + jnp.einsum("kj,bmjc->bmkc", table_im, src_re, preferred_element_type=jnp.float32)
    half_re = half_re.astype(jnp.bfloat16)
    half_im = half_im.astype(jnp.bfloat16)
    out_re = jnp.einsum(
        "bmkc,cl->bmkl", half_re, table_re, preferred_element_type=jnp.float32
    ) - jnp.einsum("bmkc,cl->bmkl", half_im, table_im, preferred_element_type=jnp.float32)
    out_im = jnp.einsum(
        "bmkc,cl->bmkl", half_re, table_im, preferred_element_type=jnp.float32
    ) + jnp.einsum("bmkc,cl->bmkl", half_im, table_re, preferred_element_type=jnp.float32)
    return (out_re, out_im)


def block_tables(table_re, table_im):
    left = jnp.concatenate(
        [jnp.concatenate([table_re, -table_im], 1), jnp.concatenate([table_im, table_re], 1)], 0
    )
    right = jnp.concatenate(
        [jnp.concatenate([table_re, table_im], 1), jnp.concatenate([-table_im, table_re], 1)], 0
    )
    return left, right


def entry_kernel(patch_ref, amp_ref, probe_ref, left_ref, right_ref, update_ref, grad_ref):
    modes, length = probe_ref.shape[0], probe_ref.shape[-1]

    @pl.when(pl.program_id(0) == 0)
    def _():
        grad_ref[...] = jnp.zeros(grad_ref.shape, grad_ref.dtype)

    patch_re = patch_ref[0].astype(jnp.float32)
    patch_im = patch_ref[1].astype(jnp.float32)
    left = left_ref[...]
    right = right_ref[...]
    exits_re, exits_im = [], []
    for m in range(modes):
        probe_re = probe_ref[m, 0]
        probe_im = probe_ref[m, 1]
        exits_re.append((probe_re * patch_re - probe_im * patch_im).astype(jnp.bfloat16))
        exits_im.append((probe_re * patch_im + probe_im * patch_re).astype(jnp.bfloat16))
    stacked = jnp.concatenate(
        [jnp.concatenate(exits_re, 1), jnp.concatenate(exits_im, 1)], 0
    )
    half = jnp.dot(left, stacked, preferred_element_type=jnp.float32).astype(jnp.bfloat16)

    def by_mode(wide):
        return jnp.concatenate(
            [
                jnp.concatenate(
                    [
                        wide[:length, m * length : (m + 1) * length],
                        wide[length:, m * length : (m + 1) * length],
                    ],
                    1,
                )
                for m in range(modes)
            ],
            0,
        )

    def by_part(tall):
        return jnp.concatenate(
            [
                jnp.concatenate(
                    [tall[m * length : (m + 1) * length, :length] for m in range(modes)], 1
                ),
                jnp.concatenate(
                    [tall[m * length : (m + 1) * length, length:] for m in range(modes)], 1
                ),
            ],
            0,
        )

    far = jnp.dot(by_mode(half), right, preferred_element_type=jnp.float32)
    intensity = jnp.zeros((length, length), jnp.float32)
    for m in range(modes):
        far_re = far[m * length : (m + 1) * length, :length]
        far_im = far[m * length : (m + 1) * length, length:]
        intensity = intensity + (far_re * far_re + far_im * far_im)
    measured = amp_ref[...].astype(jnp.float32)
    factor = measured / jnp.sqrt(jnp.maximum(intensity, 1.0)) - 1.0
    factor = jnp.concatenate([factor, factor], 1)
    factor = jnp.concatenate([factor] * modes, 0)
    scaled = (factor * far).astype(jnp.bfloat16)
    back = jnp.dot(right, by_part(scaled), preferred_element_type=jnp.float32).astype(
        jnp.bfloat16
    )
    change = jnp.dot(by_mode(back), left, preferred_element_type=jnp.float32)
    update_re = jnp.zeros((length, length), jnp.float32)
    update_im = jnp.zeros((length, length), jnp.float32)
    for m in range(modes):
        change_re = change[m * length : (m + 1) * length, :length]
        change_im = change[m * length : (m + 1) * length, length:]
        probe_re = probe_ref[m, 0]
        probe_im = probe_ref[m, 1]
        update_re = update_re + (probe_re * change_re + probe_im * change_im)
        update_im = update_im + (probe_re * change_im - probe_im * change_re)
        grad_ref[m, 0] += patch_re * change_re + patch_im * change_im
        grad_ref[m, 1] += patch_re * change_im - patch_im * change_re
    update_ref[0] = update_re.astype(update_ref.dtype)
    update_ref[1] = update_im.astype(update_ref.dtype)


def entries_kernel(patch, amp_in, probe_now, left, right):
    slots, length = amp_in.shape[0], amp_in.shape[-1]
    modes = probe_now.shape[0]
    flops = slots * 4 * 2 * (2 * length) * (2 * length) * (modes * length)
    return pl.pallas_call(
        entry_kernel,
        grid=(slots,),
        in_specs=[
            pl.BlockSpec((2, None, length, length), lambda s: (0, s, 0, 0)),
            pl.BlockSpec((None, length, length), lambda s: (s, 0, 0)),
            pl.BlockSpec(probe_now.shape, lambda s: (0, 0, 0, 0)),
            pl.BlockSpec(left.shape, lambda s: (0, 0)),
            pl.BlockSpec(right.shape, lambda s: (0, 0)),
        ],
        out_specs=[
            pl.BlockSpec((2, None, length, length), lambda s: (0, s, 0, 0)),
            pl.BlockSpec(probe_now.shape, lambda s: (0, 0, 0, 0)),
        ],
        out_shape=[
            jax.ShapeDtypeStruct((2, slots, length, length), jnp.bfloat16),
            jax.ShapeDtypeStruct(probe_now.shape, jnp.float32),
        ],
        compiler_params=pltpu.CompilerParams(dimension_semantics=("arbitrary",)),
        cost_estimate=pl.CostEstimate(
            flops=flops,
            transcendentals=slots * length * length,
            bytes_accessed=slots * length * length * 10 + probe_now.size * 8,
        ),
    )(patch, amp_in, probe_now, left, right)


def route(amplitudes, batch_ids, scan_tile, scan_offset, tiles_here):
    tile_count = lax.axis_size("tile")
    steps, batch_rows = batch_ids.shape
    capacity = max(2, 2 * batch_rows // tile_count)
    slots = tile_count * capacity
    length = amplitudes.shape[-1]
    target = scan_tile[:, :, 0]
    owner = target // tiles_here
    local_tile = target - owner * tiles_here
    onehot = (owner[:, :, None] == jnp.arange(tile_count, dtype=jnp.int32)).astype(jnp.int32)
    place_in = jnp.sum((jnp.cumsum(onehot, axis=1) - 1) * onehot, axis=2)
    slot_of = owner * capacity + place_in
    chosen = slot_of[:, None, :] == jnp.arange(slots, dtype=jnp.int32)[None, :, None]
    valid = jnp.any(chosen, axis=2).astype(jnp.int32)
    entry = jnp.argmax(chosen, axis=2).astype(jnp.int32)
    meta = jnp.stack(
        [
            jnp.take_along_axis(local_tile, entry, axis=1),
            jnp.take_along_axis(scan_offset[:, :, 0], entry, axis=1),
            jnp.take_along_axis(scan_offset[:, :, 1], entry, axis=1),
            valid,
        ],
        axis=2,
    ).astype(jnp.bfloat16)
    meta = jnp.pad(meta[:, :, None, :], ((0, 0), (0, 0), (0, 7), (0, length - 4)))
    ids = jnp.take_along_axis(batch_ids, entry, axis=1)
    amp_send = amplitudes[ids.reshape(-1)].reshape(steps, slots, length, length)
    payload = jnp.concatenate([amp_send, meta], axis=2)
    return payload.reshape(steps, tile_count, capacity, length + 8, length)


def exchange(payload, size):
    tile_count, capacity, rows, length = payload.shape
    arrived = lax.all_to_all(payload, "tile", 0, 0, tiled=True).reshape(
        tile_count * capacity, rows, length
    )
    meta = arrived[:, length, :4].astype(jnp.int32)
    meta_in = jnp.stack([meta[:, 0] * size + meta[:, 1], meta[:, 2], meta[:, 3]], axis=1)
    return arrived, meta_in


def group_size(axes):
    count = 1
    for axis in axes:
        count *= lax.axis_size(axis)
    return count


def sum_over(value, axes, send_type):
    count = group_size(axes)
    parts = lax.all_to_all(value.astype(send_type).reshape(count, -1), axes, 0, 0, tiled=True)
    total = jnp.sum(parts.astype(jnp.float32), axis=0, keepdims=True).astype(send_type)
    return total, count


def all_sum_a2a(value, axes):
    total, count = sum_over(value, axes, value.dtype)
    spread = lax.all_to_all(jnp.broadcast_to(total, (count, total.shape[1])), axes, 0, 0, tiled=True)
    return spread.reshape(value.shape)


def all_sum_pairs(value, axis, send_type):
    count = lax.axis_size(axis)
    if count & (count - 1):
        return lax.psum(value.astype(send_type), axis).astype(jnp.float32)
    total = value.astype(send_type).astype(jnp.float32)
    step = 1
    while step < count:
        pairs = [(i, i ^ step) for i in range(count)]
        other = lax.ppermute(total.astype(send_type), axis, pairs)
        total = total.astype(send_type).astype(jnp.float32) + other.astype(jnp.float32)
        step *= 2
    return total


def entries_pass(stacked, probe_now, amp_in, meta_in, tables):
    table_re, table_im, table_neg = tables
    length = probe_now.shape[-1]
    rows_all, size = stacked.shape[1], stacked.shape[2]
    within = jnp.arange(length, dtype=jnp.int32)
    row_at, col_at, valid = meta_in[:, 0], meta_in[:, 1], meta_in[:, 2]
    pick_rows = (
        (row_at[:, None, None] + within[None, :, None])
        == jnp.arange(rows_all, dtype=jnp.int32)[None, None, :]
    ) & (valid[:, None, None] > 0)
    pick_rows = pick_rows.astype(jnp.bfloat16)
    pick_cols = (
        (col_at[:, None, None] + within[None, None, :])
        == jnp.arange(size, dtype=jnp.int32)[None, :, None]
    ).astype(jnp.bfloat16)
    rows = jnp.einsum(
        "skq,xqc->xskc", pick_rows, stacked, preferred_element_type=jnp.float32
    ).astype(jnp.bfloat16)
    patch = jnp.einsum("xskc,scl->xskl", rows, pick_cols, preferred_element_type=jnp.float32)
    left, right = block_tables(tables[0], tables[1])
    update, probe_grad = entries_kernel(patch.astype(jnp.bfloat16), amp_in, probe_now, left, right)
    spread = jnp.einsum(
        "xskl,scl->xskc", update, pick_cols, preferred_element_type=jnp.float32
    ).astype(jnp.bfloat16)
    local_sum = jnp.einsum("skq,xskc->xqc", pick_rows, spread, preferred_element_type=jnp.float32)
    return local_sum, probe_grad


def one_step(tiles_now, probe_now, amp_in, meta_in, tables, batch_total):
    tiles_here, size = tiles_now.shape[1], tiles_now.shape[2]
    slots, length = amp_in.shape[0], amp_in.shape[-1]
    stacked = tiles_now.astype(jnp.bfloat16).reshape(2, tiles_here * size, size)
    chunk = max(d for d in range(1, min(slots, 24) + 1) if slots % d == 0)
    if chunk == slots:
        local_sum, probe_grad = entries_pass(stacked, probe_now, amp_in, meta_in, tables)
    else:

        def body(carry, piece):
            part_sum, part_grad = entries_pass(stacked, probe_now, piece[0], piece[1], tables)
            return (carry[0] + part_sum, carry[1] + part_grad), None

        start = (jnp.zeros(stacked.shape, jnp.float32), jnp.zeros(probe_now.shape, jnp.float32))
        pieces = (
            amp_in.reshape(slots // chunk, chunk, length + 8, length),
            meta_in.reshape(slots // chunk, chunk, 3),
        )
        (local_sum, probe_grad), _ = lax.scan(body, start, pieces)
    local_sum = local_sum.reshape(tiles_now.shape)
    probe_re = probe_now[:, 0]
    probe_im = probe_now[:, 1]
    peak_power = jnp.max(jnp.sum(probe_re * probe_re + probe_im * probe_im, axis=0))
    summed = all_sum_pairs(local_sum, "pat", jnp.bfloat16)
    tiles_next = tiles_now + summed / peak_power
    grad_sum = all_sum_a2a(probe_grad, ("tile", "pat"))
    probe_next = probe_now + probe_rate * grad_sum / batch_total
    return (tiles_next, probe_next)


def on_device(amplitudes, batch_ids, scan_tile, scan_offset, object_tiles, probe):
    tables = dft_tables(probe.shape[-1])
    tiles_here, size = object_tiles.shape[1], object_tiles.shape[2]
    batch_total = batch_ids.shape[1] * lax.axis_size("tile") * lax.axis_size("pat")
    payload = route(amplitudes, batch_ids, scan_tile, scan_offset, tiles_here)
    tiles_now = object_tiles
    probe_now = probe
    for step_no in range(batch_ids.shape[0]):
        amp_in, meta_in = exchange(payload[step_no], size)
        tiles_now, probe_now = one_step(tiles_now, probe_now, amp_in, meta_in, tables, batch_total)
    return (tiles_now, probe_now)


def solution(mesh):
    in_specs = (
        P(("tile", "pat"), None, None),
        P(None, ("tile", "pat")),
        P(None, ("tile", "pat"), None),
        P(None, ("tile", "pat"), None),
        P(None, "tile", None, None),
        P(),
    )
    out_specs = (P(None, "tile", None, None), P())
    return jax.shard_map(
        on_device, mesh=mesh, in_specs=in_specs, out_specs=out_specs, check_vma=False
    )
```

```python
import math

import jax
import jax.numpy as jnp
from jax import lax
from jax.experimental import pallas as pl
from jax.experimental.pallas import tpu as pltpu
from jax.sharding import PartitionSpec as P

probe_rate = 8.0


def dft_tables(length):
    counter = jnp.arange(length, dtype=jnp.int32)
    product = counter[:, None] * counter[None, :] % length
    angle_table = 2.0 * math.pi / length * product.astype(jnp.float32)
    norm_factor = 1.0 / math.sqrt(length)
    table_re = (jnp.cos(angle_table) * norm_factor).astype(jnp.bfloat16)
    table_im = (-jnp.sin(angle_table) * norm_factor).astype(jnp.bfloat16)
    return (table_re, table_im, -table_im)


def transform(src_re, src_im, table_re, table_im):
    half_re = jnp.einsum(
        "kj,bmjc->bmkc", table_re, src_re, preferred_element_type=jnp.float32
    ) - jnp.einsum("kj,bmjc->bmkc", table_im, src_im, preferred_element_type=jnp.float32)
    half_im = jnp.einsum(
        "kj,bmjc->bmkc", table_re, src_im, preferred_element_type=jnp.float32
    ) + jnp.einsum("kj,bmjc->bmkc", table_im, src_re, preferred_element_type=jnp.float32)
    half_re = half_re.astype(jnp.bfloat16)
    half_im = half_im.astype(jnp.bfloat16)
    out_re = jnp.einsum(
        "bmkc,cl->bmkl", half_re, table_re, preferred_element_type=jnp.float32
    ) - jnp.einsum("bmkc,cl->bmkl", half_im, table_im, preferred_element_type=jnp.float32)
    out_im = jnp.einsum(
        "bmkc,cl->bmkl", half_re, table_im, preferred_element_type=jnp.float32
    ) + jnp.einsum("bmkc,cl->bmkl", half_im, table_re, preferred_element_type=jnp.float32)
    return (out_re, out_im)


def block_tables(table_re, table_im):
    left = jnp.concatenate(
        [jnp.concatenate([table_re, -table_im], 1), jnp.concatenate([table_im, table_re], 1)], 0
    )
    right = jnp.concatenate(
        [jnp.concatenate([table_re, table_im], 1), jnp.concatenate([-table_im, table_re], 1)], 0
    )
    return left, right


def entry_kernel(valid_ref, patch_ref, amp_ref, probe_ref, left_ref, right_ref, update_ref, grad_ref):
    slot = pl.program_id(0)

    @pl.when(slot == 0)
    def _():
        grad_ref[...] = jnp.zeros(grad_ref.shape, grad_ref.dtype)

    @pl.when(valid_ref[slot] == 0)
    def _():
        update_ref[...] = jnp.zeros(update_ref.shape, update_ref.dtype)

    @pl.when(valid_ref[slot] != 0)
    def _():
        entry_body(patch_ref, amp_ref, probe_ref, left_ref, right_ref, update_ref, grad_ref)


def entry_body(patch_ref, amp_ref, probe_ref, left_ref, right_ref, update_ref, grad_ref):
    modes, length = probe_ref.shape[0], probe_ref.shape[-1]

    patch_re = patch_ref[0].astype(jnp.float32)
    patch_im = patch_ref[1].astype(jnp.float32)
    left = left_ref[...]
    right = right_ref[...]
    exits_re, exits_im = [], []
    for m in range(modes):
        probe_re = probe_ref[m, 0]
        probe_im = probe_ref[m, 1]
        exits_re.append((probe_re * patch_re - probe_im * patch_im).astype(jnp.bfloat16))
        exits_im.append((probe_re * patch_im + probe_im * patch_re).astype(jnp.bfloat16))
    stacked = jnp.concatenate(
        [jnp.concatenate(exits_re, 1), jnp.concatenate(exits_im, 1)], 0
    )
    half = jnp.dot(left, stacked, preferred_element_type=jnp.float32).astype(jnp.bfloat16)

    def by_mode(wide):
        return jnp.concatenate(
            [
                jnp.concatenate(
                    [
                        wide[:length, m * length : (m + 1) * length],
                        wide[length:, m * length : (m + 1) * length],
                    ],
                    1,
                )
                for m in range(modes)
            ],
            0,
        )

    def by_part(tall):
        return jnp.concatenate(
            [
                jnp.concatenate(
                    [tall[m * length : (m + 1) * length, :length] for m in range(modes)], 1
                ),
                jnp.concatenate(
                    [tall[m * length : (m + 1) * length, length:] for m in range(modes)], 1
                ),
            ],
            0,
        )

    far = jnp.dot(by_mode(half), right, preferred_element_type=jnp.float32)
    intensity = jnp.zeros((length, length), jnp.float32)
    for m in range(modes):
        far_re = far[m * length : (m + 1) * length, :length]
        far_im = far[m * length : (m + 1) * length, length:]
        intensity = intensity + (far_re * far_re + far_im * far_im)
    measured = amp_ref[...].astype(jnp.float32)
    factor = measured / jnp.sqrt(jnp.maximum(intensity, 1.0)) - 1.0
    factor = jnp.concatenate([factor, factor], 1)
    factor = jnp.concatenate([factor] * modes, 0)
    scaled = (factor * far).astype(jnp.bfloat16)
    back = jnp.dot(right, by_part(scaled), preferred_element_type=jnp.float32).astype(
        jnp.bfloat16
    )
    change = jnp.dot(by_mode(back), left, preferred_element_type=jnp.float32)
    update_re = jnp.zeros((length, length), jnp.float32)
    update_im = jnp.zeros((length, length), jnp.float32)
    for m in range(modes):
        change_re = change[m * length : (m + 1) * length, :length]
        change_im = change[m * length : (m + 1) * length, length:]
        probe_re = probe_ref[m, 0]
        probe_im = probe_ref[m, 1]
        update_re = update_re + (probe_re * change_re + probe_im * change_im)
        update_im = update_im + (probe_re * change_im - probe_im * change_re)
        grad_ref[m, 0] += patch_re * change_re + patch_im * change_im
        grad_ref[m, 1] += patch_re * change_im - patch_im * change_re
    update_ref[0] = update_re.astype(update_ref.dtype)
    update_ref[1] = update_im.astype(update_ref.dtype)


def entries_kernel(valid, patch, amp_in, probe_now, left, right):
    slots, length = amp_in.shape[0], amp_in.shape[-1]
    modes = probe_now.shape[0]
    flops = slots * 4 * 2 * (2 * length) * (2 * length) * (modes * length)
    grid_spec = pltpu.PrefetchScalarGridSpec(
        num_scalar_prefetch=1,
        grid=(slots,),
        in_specs=[
            pl.BlockSpec((2, None, length, length), lambda s, v: (0, s, 0, 0)),
            pl.BlockSpec((None, length, length), lambda s, v: (s, 0, 0)),
            pl.BlockSpec(probe_now.shape, lambda s, v: (0, 0, 0, 0)),
            pl.BlockSpec(left.shape, lambda s, v: (0, 0)),
            pl.BlockSpec(right.shape, lambda s, v: (0, 0)),
        ],
        out_specs=[
            pl.BlockSpec((2, None, length, length), lambda s, v: (0, s, 0, 0)),
            pl.BlockSpec(probe_now.shape, lambda s, v: (0, 0, 0, 0)),
        ],
    )
    return pl.pallas_call(
        entry_kernel,
        grid_spec=grid_spec,
        out_shape=[
            jax.ShapeDtypeStruct((2, slots, length, length), jnp.bfloat16),
            jax.ShapeDtypeStruct(probe_now.shape, jnp.float32),
        ],
        compiler_params=pltpu.CompilerParams(dimension_semantics=("arbitrary",)),
        cost_estimate=pl.CostEstimate(
            flops=flops,
            transcendentals=slots * length * length,
            bytes_accessed=slots * length * length * 10 + probe_now.size * 8,
        ),
    )(valid, patch, amp_in, probe_now, left, right)


def route(amplitudes, batch_ids, scan_tile, scan_offset, tiles_here):
    tile_count = lax.axis_size("tile")
    steps, batch_rows = batch_ids.shape
    capacity = max(2, 2 * batch_rows // tile_count)
    slots = tile_count * capacity
    length = amplitudes.shape[-1]
    target = scan_tile[:, :, 0]
    owner = target // tiles_here
    local_tile = target - owner * tiles_here
    onehot = (owner[:, :, None] == jnp.arange(tile_count, dtype=jnp.int32)).astype(jnp.int32)
    place_in = jnp.sum((jnp.cumsum(onehot, axis=1) - 1) * onehot, axis=2)
    slot_of = owner * capacity + place_in
    chosen = slot_of[:, None, :] == jnp.arange(slots, dtype=jnp.int32)[None, :, None]
    valid = jnp.any(chosen, axis=2).astype(jnp.int32)
    entry = jnp.argmax(chosen, axis=2).astype(jnp.int32)
    meta = jnp.stack(
        [
            jnp.take_along_axis(local_tile, entry, axis=1),
            jnp.take_along_axis(scan_offset[:, :, 0], entry, axis=1),
            jnp.take_along_axis(scan_offset[:, :, 1], entry, axis=1),
            valid,
        ],
        axis=2,
    ).astype(jnp.bfloat16)
    meta = jnp.pad(meta[:, :, None, :], ((0, 0), (0, 0), (0, 7), (0, length - 4)))
    ids = jnp.take_along_axis(batch_ids, entry, axis=1)
    amp_send = amplitudes[ids.reshape(-1)].reshape(steps, slots, length, length)
    payload = jnp.concatenate([amp_send, meta], axis=2)
    return payload.reshape(steps, tile_count, capacity, length + 8, length)


def exchange(payload, size):
    tile_count, capacity, rows, length = payload.shape
    arrived = lax.all_to_all(payload, "tile", 0, 0, tiled=True).reshape(
        tile_count * capacity, rows, length
    )
    meta = arrived[:, length, :4].astype(jnp.int32)
    meta_in = jnp.stack([meta[:, 0] * size + meta[:, 1], meta[:, 2], meta[:, 3]], axis=1)
    return arrived, meta_in


def group_size(axes):
    count = 1
    for axis in axes:
        count *= lax.axis_size(axis)
    return count


def sum_over(value, axes, send_type):
    count = group_size(axes)
    parts = lax.all_to_all(value.astype(send_type).reshape(count, -1), axes, 0, 0, tiled=True)
    total = jnp.sum(parts.astype(jnp.float32), axis=0, keepdims=True).astype(send_type)
    return total, count


def all_sum_a2a(value, axes):
    total, count = sum_over(value, axes, value.dtype)
    spread = lax.all_to_all(jnp.broadcast_to(total, (count, total.shape[1])), axes, 0, 0, tiled=True)
    return spread.reshape(value.shape)


def all_sum_pairs(value, axis, send_type):
    count = lax.axis_size(axis)
    if count & (count - 1):
        return lax.psum(value.astype(send_type), axis).astype(jnp.float32)
    total = value.astype(send_type).astype(jnp.float32)
    step = 1
    while step < count:
        pairs = [(i, i ^ step) for i in range(count)]
        other = lax.ppermute(total.astype(send_type), axis, pairs)
        total = total.astype(send_type).astype(jnp.float32) + other.astype(jnp.float32)
        step *= 2
    return total


def entries_pass(stacked, probe_now, amp_in, meta_in, tables):
    table_re, table_im, table_neg = tables
    length = probe_now.shape[-1]
    rows_all, size = stacked.shape[1], stacked.shape[2]
    within = jnp.arange(length, dtype=jnp.int32)
    row_at, col_at, valid = meta_in[:, 0], meta_in[:, 1], meta_in[:, 2]
    pick_rows = (
        (row_at[:, None, None] + within[None, :, None])
        == jnp.arange(rows_all, dtype=jnp.int32)[None, None, :]
    ) & (valid[:, None, None] > 0)
    pick_rows = pick_rows.astype(jnp.bfloat16)
    pick_cols = (
        (col_at[:, None, None] + within[None, None, :])
        == jnp.arange(size, dtype=jnp.int32)[None, :, None]
    ).astype(jnp.bfloat16)
    rows = jnp.einsum(
        "skq,xqc->xskc", pick_rows, stacked, preferred_element_type=jnp.float32
    ).astype(jnp.bfloat16)
    patch = jnp.einsum("xskc,scl->xskl", rows, pick_cols, preferred_element_type=jnp.float32)
    left, right = block_tables(tables[0], tables[1])
    update, probe_grad = entries_kernel(
        valid, patch.astype(jnp.bfloat16), amp_in, probe_now, left, right
    )
    spread = jnp.einsum(
        "xskl,scl->xskc", update, pick_cols, preferred_element_type=jnp.float32
    ).astype(jnp.bfloat16)
    local_sum = jnp.einsum("skq,xskc->xqc", pick_rows, spread, preferred_element_type=jnp.float32)
    return local_sum, probe_grad


def one_step(tiles_now, probe_now, amp_in, meta_in, tables, batch_total):
    tiles_here, size = tiles_now.shape[1], tiles_now.shape[2]
    slots, length = amp_in.shape[0], amp_in.shape[-1]
    stacked = tiles_now.astype(jnp.bfloat16).reshape(2, tiles_here * size, size)
    chunk = max(d for d in range(1, min(slots, 24) + 1) if slots % d == 0)
    if chunk == slots:
        local_sum, probe_grad = entries_pass(stacked, probe_now, amp_in, meta_in, tables)
    else:

        def body(carry, piece):
            part_sum, part_grad = entries_pass(stacked, probe_now, piece[0], piece[1], tables)
            return (carry[0] + part_sum, carry[1] + part_grad), None

        start = (jnp.zeros(stacked.shape, jnp.float32), jnp.zeros(probe_now.shape, jnp.float32))
        pieces = (
            amp_in.reshape(slots // chunk, chunk, length + 8, length),
            meta_in.reshape(slots // chunk, chunk, 3),
        )
        (local_sum, probe_grad), _ = lax.scan(body, start, pieces)
    local_sum = local_sum.reshape(tiles_now.shape)
    probe_re = probe_now[:, 0]
    probe_im = probe_now[:, 1]
    peak_power = jnp.max(jnp.sum(probe_re * probe_re + probe_im * probe_im, axis=0))
    summed = all_sum_pairs(local_sum, "pat", jnp.bfloat16)
    tiles_next = tiles_now + summed / peak_power
    grad_sum = all_sum_a2a(probe_grad, ("tile", "pat"))
    probe_next = probe_now + probe_rate * grad_sum / batch_total
    return (tiles_next, probe_next)


def on_device(amplitudes, batch_ids, scan_tile, scan_offset, object_tiles, probe):
    tables = dft_tables(probe.shape[-1])
    tiles_here, size = object_tiles.shape[1], object_tiles.shape[2]
    batch_total = batch_ids.shape[1] * lax.axis_size("tile") * lax.axis_size("pat")
    payload = route(amplitudes, batch_ids, scan_tile, scan_offset, tiles_here)
    tiles_now = object_tiles
    probe_now = probe
    for step_no in range(batch_ids.shape[0]):
        amp_in, meta_in = exchange(payload[step_no], size)
        tiles_now, probe_now = one_step(tiles_now, probe_now, amp_in, meta_in, tables, batch_total)
    return (tiles_now, probe_now)


def solution(mesh):
    in_specs = (
        P(("tile", "pat"), None, None),
        P(None, ("tile", "pat")),
        P(None, ("tile", "pat"), None),
        P(None, ("tile", "pat"), None),
        P(None, "tile", None, None),
        P(),
    )
    out_specs = (P(None, "tile", None, None), P())
    return jax.shard_map(
        on_device, mesh=mesh, in_specs=in_specs, out_specs=out_specs, check_vma=False
    )
```

```python
import math

import jax
import jax.numpy as jnp
from jax import lax
from jax.experimental import pallas as pl
from jax.experimental.pallas import tpu as pltpu
from jax.sharding import PartitionSpec as P

probe_rate = 8.0


def dft_tables(length):
    counter = jnp.arange(length, dtype=jnp.int32)
    product = counter[:, None] * counter[None, :] % length
    angle_table = 2.0 * math.pi / length * product.astype(jnp.float32)
    norm_factor = 1.0 / math.sqrt(length)
    table_re = (jnp.cos(angle_table) * norm_factor).astype(jnp.bfloat16)
    table_im = (-jnp.sin(angle_table) * norm_factor).astype(jnp.bfloat16)
    return (table_re, table_im, -table_im)


def transform(src_re, src_im, table_re, table_im):
    half_re = jnp.einsum(
        "kj,bmjc->bmkc", table_re, src_re, preferred_element_type=jnp.float32
    ) - jnp.einsum("kj,bmjc->bmkc", table_im, src_im, preferred_element_type=jnp.float32)
    half_im = jnp.einsum(
        "kj,bmjc->bmkc", table_re, src_im, preferred_element_type=jnp.float32
    ) + jnp.einsum("kj,bmjc->bmkc", table_im, src_re, preferred_element_type=jnp.float32)
    half_re = half_re.astype(jnp.bfloat16)
    half_im = half_im.astype(jnp.bfloat16)
    out_re = jnp.einsum(
        "bmkc,cl->bmkl", half_re, table_re, preferred_element_type=jnp.float32
    ) - jnp.einsum("bmkc,cl->bmkl", half_im, table_im, preferred_element_type=jnp.float32)
    out_im = jnp.einsum(
        "bmkc,cl->bmkl", half_re, table_im, preferred_element_type=jnp.float32
    ) + jnp.einsum("bmkc,cl->bmkl", half_im, table_re, preferred_element_type=jnp.float32)
    return (out_re, out_im)


def block_tables(table_re, table_im):
    left = jnp.concatenate(
        [jnp.concatenate([table_re, -table_im], 1), jnp.concatenate([table_im, table_re], 1)], 0
    )
    right = jnp.concatenate(
        [jnp.concatenate([table_re, table_im], 1), jnp.concatenate([-table_im, table_re], 1)], 0
    )
    return left, right


def entry_kernel(valid_ref, patch_ref, amp_ref, probe_ref, left_ref, right_ref, update_ref, grad_ref):
    grad_ref[...] = jnp.zeros(grad_ref.shape, grad_ref.dtype)

    def one_slot(slot, carry):
        @pl.when(valid_ref[slot] == 0)
        def _():
            update_ref[:, slot] = jnp.zeros((2,) + update_ref.shape[2:], update_ref.dtype)

        @pl.when(valid_ref[slot] != 0)
        def _():
            entry_body(slot, patch_ref, amp_ref, probe_ref, left_ref, right_ref, update_ref, grad_ref)

        return carry

    lax.fori_loop(0, valid_ref.shape[0], one_slot, 0)


def entry_body(slot, patch_ref, amp_ref, probe_ref, left_ref, right_ref, update_ref, grad_ref):
    modes, length = probe_ref.shape[0], probe_ref.shape[-1]

    patch_re = patch_ref[0, slot].astype(jnp.float32)
    patch_im = patch_ref[1, slot].astype(jnp.float32)
    left = left_ref[...]
    right = right_ref[...]
    exits_re, exits_im = [], []
    for m in range(modes):
        probe_re = probe_ref[m, 0]
        probe_im = probe_ref[m, 1]
        exits_re.append((probe_re * patch_re - probe_im * patch_im).astype(jnp.bfloat16))
        exits_im.append((probe_re * patch_im + probe_im * patch_re).astype(jnp.bfloat16))
    stacked = jnp.concatenate(
        [jnp.concatenate(exits_re, 1), jnp.concatenate(exits_im, 1)], 0
    )
    half = jnp.dot(left, stacked, preferred_element_type=jnp.float32).astype(jnp.bfloat16)

    def by_mode(wide):
        return jnp.concatenate(
            [
                jnp.concatenate(
                    [
                        wide[:length, m * length : (m + 1) * length],
                        wide[length:, m * length : (m + 1) * length],
                    ],
                    1,
                )
                for m in range(modes)
            ],
            0,
        )

    def by_part(tall):
        return jnp.concatenate(
            [
                jnp.concatenate(
                    [tall[m * length : (m + 1) * length, :length] for m in range(modes)], 1
                ),
                jnp.concatenate(
                    [tall[m * length : (m + 1) * length, length:] for m in range(modes)], 1
                ),
            ],
            0,
        )

    far = jnp.dot(by_mode(half), right, preferred_element_type=jnp.float32)
    intensity = jnp.zeros((length, length), jnp.float32)
    for m in range(modes):
        far_re = far[m * length : (m + 1) * length, :length]
        far_im = far[m * length : (m + 1) * length, length:]
        intensity = intensity + (far_re * far_re + far_im * far_im)
    measured = amp_ref[slot, :length, :].astype(jnp.float32)
    factor = measured / jnp.sqrt(jnp.maximum(intensity, 1.0)) - 1.0
    factor = jnp.concatenate([factor, factor], 1)
    factor = jnp.concatenate([factor] * modes, 0)
    scaled = (factor * far).astype(jnp.bfloat16)
    back = jnp.dot(right, by_part(scaled), preferred_element_type=jnp.float32).astype(
        jnp.bfloat16
    )
    change = jnp.dot(by_mode(back), left, preferred_element_type=jnp.float32)
    update_re = jnp.zeros((length, length), jnp.float32)
    update_im = jnp.zeros((length, length), jnp.float32)
    for m in range(modes):
        change_re = change[m * length : (m + 1) * length, :length]
        change_im = change[m * length : (m + 1) * length, length:]
        probe_re = probe_ref[m, 0]
        probe_im = probe_ref[m, 1]
        update_re = update_re + (probe_re * change_re + probe_im * change_im)
        update_im = update_im + (probe_re * change_im - probe_im * change_re)
        grad_ref[m, 0] += patch_re * change_re + patch_im * change_im
        grad_ref[m, 1] += patch_re * change_im - patch_im * change_re
    update_ref[0, slot] = update_re.astype(update_ref.dtype)
    update_ref[1, slot] = update_im.astype(update_ref.dtype)


def entries_kernel(valid, patch, amp_in, probe_now, left, right):
    slots, length = amp_in.shape[0], amp_in.shape[-1]
    modes = probe_now.shape[0]
    flops = slots * 4 * 2 * (2 * length) * (2 * length) * (modes * length)
    whole = pl.BlockSpec(memory_space=pltpu.VMEM)
    grid_spec = pltpu.PrefetchScalarGridSpec(
        num_scalar_prefetch=1,
        grid=(1,),
        in_specs=[whole] * 5,
        out_specs=[whole] * 2,
    )
    return pl.pallas_call(
        entry_kernel,
        grid_spec=grid_spec,
        out_shape=[
            jax.ShapeDtypeStruct((2, slots, length, length), jnp.bfloat16),
            jax.ShapeDtypeStruct(probe_now.shape, jnp.float32),
        ],
        compiler_params=pltpu.CompilerParams(dimension_semantics=("arbitrary",)),
        cost_estimate=pl.CostEstimate(
            flops=flops,
            transcendentals=slots * length * length,
            bytes_accessed=slots * length * length * 10 + probe_now.size * 8,
        ),
    )(valid, patch, amp_in, probe_now, left, right)


def route(amplitudes, batch_ids, scan_tile, scan_offset, tiles_here):
    tile_count = lax.axis_size("tile")
    steps, batch_rows = batch_ids.shape
    capacity = max(2, 2 * batch_rows // tile_count)
    slots = tile_count * capacity
    length = amplitudes.shape[-1]
    target = scan_tile[:, :, 0]
    owner = target // tiles_here
    local_tile = target - owner * tiles_here
    onehot = (owner[:, :, None] == jnp.arange(tile_count, dtype=jnp.int32)).astype(jnp.int32)
    place_in = jnp.sum((jnp.cumsum(onehot, axis=1) - 1) * onehot, axis=2)
    slot_of = owner * capacity + place_in
    chosen = slot_of[:, None, :] == jnp.arange(slots, dtype=jnp.int32)[None, :, None]
    valid = jnp.any(chosen, axis=2).astype(jnp.int32)
    entry = jnp.argmax(chosen, axis=2).astype(jnp.int32)
    meta = jnp.stack(
        [
            jnp.take_along_axis(local_tile, entry, axis=1),
            jnp.take_along_axis(scan_offset[:, :, 0], entry, axis=1),
            jnp.take_along_axis(scan_offset[:, :, 1], entry, axis=1),
            valid,
        ],
        axis=2,
    ).astype(jnp.bfloat16)
    meta = jnp.pad(meta[:, :, None, :], ((0, 0), (0, 0), (0, 7), (0, length - 4)))
    ids = jnp.take_along_axis(batch_ids, entry, axis=1)
    amp_send = amplitudes[ids.reshape(-1)].reshape(steps, slots, length, length)
    payload = jnp.concatenate([amp_send, meta], axis=2)
    return payload.reshape(steps, tile_count, capacity, length + 8, length)


def exchange(payload, size):
    tile_count, capacity, rows, length = payload.shape
    arrived = lax.all_to_all(payload, "tile", 0, 0, tiled=True).reshape(
        tile_count * capacity, rows, length
    )
    meta = arrived[:, length, :4].astype(jnp.int32)
    meta_in = jnp.stack([meta[:, 0] * size + meta[:, 1], meta[:, 2], meta[:, 3]], axis=1)
    return arrived, meta_in


def group_size(axes):
    count = 1
    for axis in axes:
        count *= lax.axis_size(axis)
    return count


def sum_over(value, axes, send_type):
    count = group_size(axes)
    parts = lax.all_to_all(value.astype(send_type).reshape(count, -1), axes, 0, 0, tiled=True)
    total = jnp.sum(parts.astype(jnp.float32), axis=0, keepdims=True).astype(send_type)
    return total, count


def all_sum_a2a(value, axes):
    total, count = sum_over(value, axes, value.dtype)
    spread = lax.all_to_all(jnp.broadcast_to(total, (count, total.shape[1])), axes, 0, 0, tiled=True)
    return spread.reshape(value.shape)


def all_sum_pairs(value, axis, send_type):
    count = lax.axis_size(axis)
    if count & (count - 1):
        return lax.psum(value.astype(send_type), axis).astype(jnp.float32)
    total = value.astype(send_type).astype(jnp.float32)
    step = 1
    while step < count:
        pairs = [(i, i ^ step) for i in range(count)]
        other = lax.ppermute(total.astype(send_type), axis, pairs)
        total = total.astype(send_type).astype(jnp.float32) + other.astype(jnp.float32)
        step *= 2
    return total


def entries_pass(stacked, probe_now, amp_in, meta_in, tables):
    table_re, table_im, table_neg = tables
    length = probe_now.shape[-1]
    rows_all, size = stacked.shape[1], stacked.shape[2]
    within = jnp.arange(length, dtype=jnp.int32)
    row_at, col_at, valid = meta_in[:, 0], meta_in[:, 1], meta_in[:, 2]
    pick_rows = (
        (row_at[:, None, None] + within[None, :, None])
        == jnp.arange(rows_all, dtype=jnp.int32)[None, None, :]
    ) & (valid[:, None, None] > 0)
    pick_rows = pick_rows.astype(jnp.bfloat16)
    pick_cols = (
        (col_at[:, None, None] + within[None, None, :])
        == jnp.arange(size, dtype=jnp.int32)[None, :, None]
    ).astype(jnp.bfloat16)
    rows = jnp.einsum(
        "skq,xqc->xskc", pick_rows, stacked, preferred_element_type=jnp.float32
    ).astype(jnp.bfloat16)
    patch = jnp.einsum("xskc,scl->xskl", rows, pick_cols, preferred_element_type=jnp.float32)
    left, right = block_tables(tables[0], tables[1])
    update, probe_grad = entries_kernel(
        valid, patch.astype(jnp.bfloat16), amp_in, probe_now, left, right
    )
    spread = jnp.einsum(
        "xskl,scl->xskc", update, pick_cols, preferred_element_type=jnp.float32
    ).astype(jnp.bfloat16)
    local_sum = jnp.einsum("skq,xskc->xqc", pick_rows, spread, preferred_element_type=jnp.float32)
    return local_sum, probe_grad


def one_step(tiles_now, probe_now, amp_in, meta_in, tables, batch_total):
    tiles_here, size = tiles_now.shape[1], tiles_now.shape[2]
    slots, length = amp_in.shape[0], amp_in.shape[-1]
    stacked = tiles_now.astype(jnp.bfloat16).reshape(2, tiles_here * size, size)
    chunk = max(d for d in range(1, min(slots, 24) + 1) if slots % d == 0)
    if chunk == slots:
        local_sum, probe_grad = entries_pass(stacked, probe_now, amp_in, meta_in, tables)
    else:

        def body(carry, piece):
            part_sum, part_grad = entries_pass(stacked, probe_now, piece[0], piece[1], tables)
            return (carry[0] + part_sum, carry[1] + part_grad), None

        start = (jnp.zeros(stacked.shape, jnp.float32), jnp.zeros(probe_now.shape, jnp.float32))
        pieces = (
            amp_in.reshape(slots // chunk, chunk, length + 8, length),
            meta_in.reshape(slots // chunk, chunk, 3),
        )
        (local_sum, probe_grad), _ = lax.scan(body, start, pieces)
    local_sum = local_sum.reshape(tiles_now.shape)
    probe_re = probe_now[:, 0]
    probe_im = probe_now[:, 1]
    peak_power = jnp.max(jnp.sum(probe_re * probe_re + probe_im * probe_im, axis=0))
    summed = all_sum_pairs(local_sum, "pat", jnp.bfloat16)
    tiles_next = tiles_now + summed / peak_power
    grad_sum = all_sum_a2a(probe_grad, ("tile", "pat"))
    probe_next = probe_now + probe_rate * grad_sum / batch_total
    return (tiles_next, probe_next)


def on_device(amplitudes, batch_ids, scan_tile, scan_offset, object_tiles, probe):
    tables = dft_tables(probe.shape[-1])
    tiles_here, size = object_tiles.shape[1], object_tiles.shape[2]
    batch_total = batch_ids.shape[1] * lax.axis_size("tile") * lax.axis_size("pat")
    payload = route(amplitudes, batch_ids, scan_tile, scan_offset, tiles_here)
    tiles_now = object_tiles
    probe_now = probe
    for step_no in range(batch_ids.shape[0]):
        amp_in, meta_in = exchange(payload[step_no], size)
        tiles_now, probe_now = one_step(tiles_now, probe_now, amp_in, meta_in, tables, batch_total)
    return (tiles_now, probe_now)


def solution(mesh):
    in_specs = (
        P(("tile", "pat"), None, None),
        P(None, ("tile", "pat")),
        P(None, ("tile", "pat"), None),
        P(None, ("tile", "pat"), None),
        P(None, "tile", None, None),
        P(),
    )
    out_specs = (P(None, "tile", None, None), P())
    return jax.shard_map(
        on_device, mesh=mesh, in_specs=in_specs, out_specs=out_specs, check_vma=False
    )
```

```python
import math

import jax
import jax.numpy as jnp
from jax import lax
from jax.experimental import pallas as pl
from jax.experimental.pallas import tpu as pltpu
from jax.sharding import PartitionSpec as P

probe_rate = 8.0


def dft_tables(length):
    counter = jnp.arange(length, dtype=jnp.int32)
    product = counter[:, None] * counter[None, :] % length
    angle_table = 2.0 * math.pi / length * product.astype(jnp.float32)
    norm_factor = 1.0 / math.sqrt(length)
    table_re = (jnp.cos(angle_table) * norm_factor).astype(jnp.bfloat16)
    table_im = (-jnp.sin(angle_table) * norm_factor).astype(jnp.bfloat16)
    return (table_re, table_im, -table_im)


def transform(src_re, src_im, table_re, table_im):
    half_re = jnp.einsum(
        "kj,bmjc->bmkc", table_re, src_re, preferred_element_type=jnp.float32
    ) - jnp.einsum("kj,bmjc->bmkc", table_im, src_im, preferred_element_type=jnp.float32)
    half_im = jnp.einsum(
        "kj,bmjc->bmkc", table_re, src_im, preferred_element_type=jnp.float32
    ) + jnp.einsum("kj,bmjc->bmkc", table_im, src_re, preferred_element_type=jnp.float32)
    half_re = half_re.astype(jnp.bfloat16)
    half_im = half_im.astype(jnp.bfloat16)
    out_re = jnp.einsum(
        "bmkc,cl->bmkl", half_re, table_re, preferred_element_type=jnp.float32
    ) - jnp.einsum("bmkc,cl->bmkl", half_im, table_im, preferred_element_type=jnp.float32)
    out_im = jnp.einsum(
        "bmkc,cl->bmkl", half_re, table_im, preferred_element_type=jnp.float32
    ) + jnp.einsum("bmkc,cl->bmkl", half_im, table_re, preferred_element_type=jnp.float32)
    return (out_re, out_im)


def block_tables(table_re, table_im):
    left = jnp.concatenate(
        [jnp.concatenate([table_re, -table_im], 1), jnp.concatenate([table_im, table_re], 1)], 0
    )
    right = jnp.concatenate(
        [jnp.concatenate([table_re, table_im], 1), jnp.concatenate([-table_im, table_re], 1)], 0
    )
    return left, right


def entry_kernel(valid_ref, patch_ref, amp_ref, probe_ref, left_ref, right_ref, update_ref, grad_ref):
    grad_ref[...] = jnp.zeros(grad_ref.shape, grad_ref.dtype)

    def one_slot(slot, carry):
        @pl.when(valid_ref[slot] == 0)
        def _():
            update_ref[:, slot] = jnp.zeros((2,) + update_ref.shape[2:], update_ref.dtype)

        @pl.when(valid_ref[slot] != 0)
        def _():
            entry_body(slot, patch_ref, amp_ref, probe_ref, left_ref, right_ref, update_ref, grad_ref)

        return carry

    lax.fori_loop(0, valid_ref.shape[0], one_slot, 0)


def entry_body(slot, patch_ref, amp_ref, probe_ref, left_ref, right_ref, update_ref, grad_ref):
    modes, length = probe_ref.shape[0], probe_ref.shape[-1]

    patch_re = patch_ref[0, slot].astype(jnp.float32)
    patch_im = patch_ref[1, slot].astype(jnp.float32)
    left = left_ref[...]
    right = right_ref[...]
    exits_re, exits_im = [], []
    for m in range(modes):
        probe_re = probe_ref[m, 0]
        probe_im = probe_ref[m, 1]
        exits_re.append((probe_re * patch_re - probe_im * patch_im).astype(jnp.bfloat16))
        exits_im.append((probe_re * patch_im + probe_im * patch_re).astype(jnp.bfloat16))
    stacked = jnp.concatenate(
        [jnp.concatenate(exits_re, 1), jnp.concatenate(exits_im, 1)], 0
    )
    half = jnp.dot(left, stacked, preferred_element_type=jnp.float32).astype(jnp.bfloat16)

    def by_mode(wide):
        return jnp.concatenate(
            [
                jnp.concatenate(
                    [
                        wide[:length, m * length : (m + 1) * length],
                        wide[length:, m * length : (m + 1) * length],
                    ],
                    1,
                )
                for m in range(modes)
            ],
            0,
        )

    def by_part(tall):
        return jnp.concatenate(
            [
                jnp.concatenate(
                    [tall[m * length : (m + 1) * length, :length] for m in range(modes)], 1
                ),
                jnp.concatenate(
                    [tall[m * length : (m + 1) * length, length:] for m in range(modes)], 1
                ),
            ],
            0,
        )

    far = jnp.dot(by_mode(half), right, preferred_element_type=jnp.float32)
    intensity = jnp.zeros((length, length), jnp.float32)
    for m in range(modes):
        far_re = far[m * length : (m + 1) * length, :length]
        far_im = far[m * length : (m + 1) * length, length:]
        intensity = intensity + (far_re * far_re + far_im * far_im)
    measured = amp_ref[slot, :length, :].astype(jnp.float32)
    factor = measured / jnp.sqrt(jnp.maximum(intensity, 1.0)) - 1.0
    factor = jnp.concatenate([factor, factor], 1)
    factor = jnp.concatenate([factor] * modes, 0)
    scaled = (factor * far).astype(jnp.bfloat16)
    back = jnp.dot(right, by_part(scaled), preferred_element_type=jnp.float32).astype(
        jnp.bfloat16
    )
    change = jnp.dot(by_mode(back), left, preferred_element_type=jnp.float32)
    update_re = jnp.zeros((length, length), jnp.float32)
    update_im = jnp.zeros((length, length), jnp.float32)
    for m in range(modes):
        change_re = change[m * length : (m + 1) * length, :length]
        change_im = change[m * length : (m + 1) * length, length:]
        probe_re = probe_ref[m, 0]
        probe_im = probe_ref[m, 1]
        update_re = update_re + (probe_re * change_re + probe_im * change_im)
        update_im = update_im + (probe_re * change_im - probe_im * change_re)
        grad_ref[m, 0] += patch_re * change_re + patch_im * change_im
        grad_ref[m, 1] += patch_re * change_im - patch_im * change_re
    update_ref[0, slot] = update_re.astype(update_ref.dtype)
    update_ref[1, slot] = update_im.astype(update_ref.dtype)


def entries_kernel(valid, patch, amp_in, probe_now, left, right):
    slots, length = amp_in.shape[0], amp_in.shape[-1]
    modes = probe_now.shape[0]
    flops = slots * 4 * 2 * (2 * length) * (2 * length) * (modes * length)
    whole = pl.BlockSpec(memory_space=pltpu.VMEM)
    grid_spec = pltpu.PrefetchScalarGridSpec(
        num_scalar_prefetch=1,
        grid=(1,),
        in_specs=[whole] * 5,
        out_specs=[whole] * 2,
    )
    return pl.pallas_call(
        entry_kernel,
        grid_spec=grid_spec,
        out_shape=[
            jax.ShapeDtypeStruct((2, slots, length, length), jnp.bfloat16),
            jax.ShapeDtypeStruct(probe_now.shape, jnp.float32),
        ],
        compiler_params=pltpu.CompilerParams(dimension_semantics=("arbitrary",)),
        cost_estimate=pl.CostEstimate(
            flops=flops,
            transcendentals=slots * length * length,
            bytes_accessed=slots * length * length * 10 + probe_now.size * 8,
        ),
    )(valid, patch, amp_in, probe_now, left, right)


def route(amplitudes, batch_ids, scan_tile, scan_offset, tiles_here):
    tile_count = lax.axis_size("tile")
    steps, batch_rows = batch_ids.shape
    capacity = max(2, 2 * batch_rows // tile_count)
    slots = tile_count * capacity
    length = amplitudes.shape[-1]
    target = scan_tile[:, :, 0]
    owner = target // tiles_here
    local_tile = target - owner * tiles_here
    onehot = (owner[:, :, None] == jnp.arange(tile_count, dtype=jnp.int32)).astype(jnp.int32)
    place_in = jnp.sum((jnp.cumsum(onehot, axis=1) - 1) * onehot, axis=2)
    slot_of = owner * capacity + place_in
    chosen = (slot_of[:, None, :] == jnp.arange(slots, dtype=jnp.int32)[None, :, None]).astype(
        jnp.int32
    )
    fields = jnp.stack(
        [local_tile, scan_offset[:, :, 0], scan_offset[:, :, 1], jnp.ones_like(local_tile)], axis=2
    )
    meta = jnp.sum(chosen[:, :, :, None] * fields[:, None, :, :], axis=2).astype(jnp.bfloat16)
    meta = jnp.pad(meta[:, :, None, :], ((0, 0), (0, 0), (0, 7), (0, length - 4)))
    ids = jnp.sum(chosen * batch_ids[:, None, :], axis=2)
    amp_send = amplitudes[ids.reshape(-1)].reshape(steps, slots, length, length)
    payload = jnp.concatenate([amp_send, meta], axis=2)
    return payload.reshape(steps, tile_count, capacity, length + 8, length)


def exchange(payload, size):
    tile_count, capacity, rows, length = payload.shape
    arrived = lax.all_to_all(payload, "tile", 0, 0, tiled=True).reshape(
        tile_count * capacity, rows, length
    )
    meta = arrived[:, length, :4].astype(jnp.int32)
    meta_in = jnp.stack([meta[:, 0] * size + meta[:, 1], meta[:, 2], meta[:, 3]], axis=1)
    return arrived, meta_in


def group_size(axes):
    count = 1
    for axis in axes:
        count *= lax.axis_size(axis)
    return count


def sum_over(value, axes, send_type):
    count = group_size(axes)
    parts = lax.all_to_all(value.astype(send_type).reshape(count, -1), axes, 0, 0, tiled=True)
    total = jnp.sum(parts.astype(jnp.float32), axis=0, keepdims=True).astype(send_type)
    return total, count


def all_sum_a2a(value, axes):
    total, count = sum_over(value, axes, value.dtype)
    spread = lax.all_to_all(jnp.broadcast_to(total, (count, total.shape[1])), axes, 0, 0, tiled=True)
    return spread.reshape(value.shape)


def all_sum_pairs(value, axis, send_type):
    count = lax.axis_size(axis)
    if count & (count - 1):
        return lax.psum(value.astype(send_type), axis).astype(jnp.float32)
    total = value.astype(send_type).astype(jnp.float32)
    step = 1
    while step < count:
        pairs = [(i, i ^ step) for i in range(count)]
        other = lax.ppermute(total.astype(send_type), axis, pairs)
        total = total.astype(send_type).astype(jnp.float32) + other.astype(jnp.float32)
        step *= 2
    return total


def entries_pass(stacked, probe_now, amp_in, meta_in, tables):
    table_re, table_im, table_neg = tables
    length = probe_now.shape[-1]
    rows_all, size = stacked.shape[1], stacked.shape[2]
    within = jnp.arange(length, dtype=jnp.int32)
    row_at, col_at, valid = meta_in[:, 0], meta_in[:, 1], meta_in[:, 2]
    pick_rows = (
        (row_at[:, None, None] + within[None, :, None])
        == jnp.arange(rows_all, dtype=jnp.int32)[None, None, :]
    ) & (valid[:, None, None] > 0)
    pick_rows = pick_rows.astype(jnp.bfloat16)
    pick_cols = (
        (col_at[:, None, None] + within[None, None, :])
        == jnp.arange(size, dtype=jnp.int32)[None, :, None]
    ).astype(jnp.bfloat16)
    rows = jnp.einsum(
        "skq,xqc->xskc", pick_rows, stacked, preferred_element_type=jnp.float32
    ).astype(jnp.bfloat16)
    patch = jnp.einsum("xskc,scl->xskl", rows, pick_cols, preferred_element_type=jnp.float32)
    left, right = block_tables(tables[0], tables[1])
    update, probe_grad = entries_kernel(
        valid, patch.astype(jnp.bfloat16), amp_in, probe_now, left, right
    )
    spread = jnp.einsum(
        "xskl,scl->xskc", update, pick_cols, preferred_element_type=jnp.float32
    ).astype(jnp.bfloat16)
    local_sum = jnp.einsum("skq,xskc->xqc", pick_rows, spread, preferred_element_type=jnp.float32)
    return local_sum, probe_grad


def one_step(tiles_now, probe_now, amp_in, meta_in, tables, batch_total):
    tiles_here, size = tiles_now.shape[1], tiles_now.shape[2]
    slots, length = amp_in.shape[0], amp_in.shape[-1]
    stacked = tiles_now.astype(jnp.bfloat16).reshape(2, tiles_here * size, size)
    chunk = max(d for d in range(1, min(slots, 24) + 1) if slots % d == 0)
    if chunk == slots:
        local_sum, probe_grad = entries_pass(stacked, probe_now, amp_in, meta_in, tables)
    else:

        def body(carry, piece):
            part_sum, part_grad = entries_pass(stacked, probe_now, piece[0], piece[1], tables)
            return (carry[0] + part_sum, carry[1] + part_grad), None

        start = (jnp.zeros(stacked.shape, jnp.float32), jnp.zeros(probe_now.shape, jnp.float32))
        pieces = (
            amp_in.reshape(slots // chunk, chunk, length + 8, length),
            meta_in.reshape(slots // chunk, chunk, 3),
        )
        (local_sum, probe_grad), _ = lax.scan(body, start, pieces)
    local_sum = local_sum.reshape(tiles_now.shape)
    probe_re = probe_now[:, 0]
    probe_im = probe_now[:, 1]
    peak_power = jnp.max(jnp.sum(probe_re * probe_re + probe_im * probe_im, axis=0))
    summed = all_sum_pairs(local_sum, "pat", jnp.bfloat16)
    tiles_next = tiles_now + summed / peak_power
    grad_sum = all_sum_a2a(probe_grad, ("tile", "pat"))
    probe_next = probe_now + probe_rate * grad_sum / batch_total
    return (tiles_next, probe_next, probe_grad)


def on_device(amplitudes, batch_ids, scan_tile, scan_offset, object_tiles, probe):
    tables = dft_tables(probe.shape[-1])
    tiles_here, size = object_tiles.shape[1], object_tiles.shape[2]
    batch_total = batch_ids.shape[1] * lax.axis_size("tile") * lax.axis_size("pat")
    payload = route(amplitudes, batch_ids, scan_tile, scan_offset, tiles_here)
    tiles_now = object_tiles
    probe_now = probe
    for step_no in range(batch_ids.shape[0]):
        sending = payload[step_no]
        if step_no > 0:
            sending, _ = lax.optimization_barrier((sending, local_grad))
        amp_in, meta_in = exchange(sending, size)
        tiles_now, probe_now, local_grad = one_step(
            tiles_now, probe_now, amp_in, meta_in, tables, batch_total
        )
    return (tiles_now, probe_now)


def solution(mesh):
    in_specs = (
        P(("tile", "pat"), None, None),
        P(None, ("tile", "pat")),
        P(None, ("tile", "pat"), None),
        P(None, ("tile", "pat"), None),
        P(None, "tile", None, None),
        P(),
    )
    out_specs = (P(None, "tile", None, None), P())
    return jax.shard_map(
        on_device, mesh=mesh, in_specs=in_specs, out_specs=out_specs, check_vma=False
    )
```

```python
import math

import jax
import jax.numpy as jnp
from jax import lax
from jax.experimental import pallas as pl
from jax.experimental.pallas import tpu as pltpu
from jax.sharding import PartitionSpec as P

probe_rate = 8.0


def dft_tables(length):
    counter = jnp.arange(length, dtype=jnp.int32)
    product = counter[:, None] * counter[None, :] % length
    angle_table = 2.0 * math.pi / length * product.astype(jnp.float32)
    norm_factor = 1.0 / math.sqrt(length)
    table_re = (jnp.cos(angle_table) * norm_factor).astype(jnp.bfloat16)
    table_im = (-jnp.sin(angle_table) * norm_factor).astype(jnp.bfloat16)
    return (table_re, table_im, -table_im)


def transform(src_re, src_im, table_re, table_im):
    half_re = jnp.einsum(
        "kj,bmjc->bmkc", table_re, src_re, preferred_element_type=jnp.float32
    ) - jnp.einsum("kj,bmjc->bmkc", table_im, src_im, preferred_element_type=jnp.float32)
    half_im = jnp.einsum(
        "kj,bmjc->bmkc", table_re, src_im, preferred_element_type=jnp.float32
    ) + jnp.einsum("kj,bmjc->bmkc", table_im, src_re, preferred_element_type=jnp.float32)
    half_re = half_re.astype(jnp.bfloat16)
    half_im = half_im.astype(jnp.bfloat16)
    out_re = jnp.einsum(
        "bmkc,cl->bmkl", half_re, table_re, preferred_element_type=jnp.float32
    ) - jnp.einsum("bmkc,cl->bmkl", half_im, table_im, preferred_element_type=jnp.float32)
    out_im = jnp.einsum(
        "bmkc,cl->bmkl", half_re, table_im, preferred_element_type=jnp.float32
    ) + jnp.einsum("bmkc,cl->bmkl", half_im, table_re, preferred_element_type=jnp.float32)
    return (out_re, out_im)


def block_tables(table_re, table_im):
    left = jnp.concatenate(
        [jnp.concatenate([table_re, -table_im], 1), jnp.concatenate([table_im, table_re], 1)], 0
    )
    right = jnp.concatenate(
        [jnp.concatenate([table_re, table_im], 1), jnp.concatenate([-table_im, table_re], 1)], 0
    )
    return left, right


def entry_kernel(valid_ref, patch_ref, amp_ref, probe_ref, left_ref, right_ref, update_ref, grad_ref):
    grad_ref[...] = jnp.zeros(grad_ref.shape, grad_ref.dtype)

    def one_slot(slot, carry):
        @pl.when(valid_ref[slot] == 0)
        def _():
            update_ref[:, slot] = jnp.zeros((2,) + update_ref.shape[2:], update_ref.dtype)

        @pl.when(valid_ref[slot] != 0)
        def _():
            entry_body(slot, patch_ref, amp_ref, probe_ref, left_ref, right_ref, update_ref, grad_ref)

        return carry

    lax.fori_loop(0, valid_ref.shape[0], one_slot, 0)


def entry_body(slot, patch_ref, amp_ref, probe_ref, left_ref, right_ref, update_ref, grad_ref):
    modes, length = probe_ref.shape[0], probe_ref.shape[-1]

    patch_re = patch_ref[0, slot].astype(jnp.float32)
    patch_im = patch_ref[1, slot].astype(jnp.float32)
    left = left_ref[...]
    right = right_ref[...]
    exits_re, exits_im = [], []
    for m in range(modes):
        probe_re = probe_ref[m, 0]
        probe_im = probe_ref[m, 1]
        exits_re.append((probe_re * patch_re - probe_im * patch_im).astype(jnp.bfloat16))
        exits_im.append((probe_re * patch_im + probe_im * patch_re).astype(jnp.bfloat16))
    stacked = jnp.concatenate(
        [jnp.concatenate(exits_re, 1), jnp.concatenate(exits_im, 1)], 0
    )
    half = jnp.dot(left, stacked, preferred_element_type=jnp.float32).astype(jnp.bfloat16)

    def by_mode(wide):
        return jnp.concatenate(
            [
                jnp.concatenate(
                    [
                        wide[:length, m * length : (m + 1) * length],
                        wide[length:, m * length : (m + 1) * length],
                    ],
                    1,
                )
                for m in range(modes)
            ],
            0,
        )

    def by_part(tall):
        return jnp.concatenate(
            [
                jnp.concatenate(
                    [tall[m * length : (m + 1) * length, :length] for m in range(modes)], 1
                ),
                jnp.concatenate(
                    [tall[m * length : (m + 1) * length, length:] for m in range(modes)], 1
                ),
            ],
            0,
        )

    far = jnp.dot(by_mode(half), right, preferred_element_type=jnp.float32)
    intensity = jnp.zeros((length, length), jnp.float32)
    for m in range(modes):
        far_re = far[m * length : (m + 1) * length, :length]
        far_im = far[m * length : (m + 1) * length, length:]
        intensity = intensity + (far_re * far_re + far_im * far_im)
    measured = amp_ref[slot, :length, :].astype(jnp.float32)
    factor = measured / jnp.sqrt(jnp.maximum(intensity, 1.0)) - 1.0
    factor = jnp.concatenate([factor, factor], 1)
    factor = jnp.concatenate([factor] * modes, 0)
    scaled = (factor * far).astype(jnp.bfloat16)
    back = jnp.dot(right, by_part(scaled), preferred_element_type=jnp.float32).astype(
        jnp.bfloat16
    )
    change = jnp.dot(by_mode(back), left, preferred_element_type=jnp.float32)
    update_re = jnp.zeros((length, length), jnp.float32)
    update_im = jnp.zeros((length, length), jnp.float32)
    for m in range(modes):
        change_re = change[m * length : (m + 1) * length, :length]
        change_im = change[m * length : (m + 1) * length, length:]
        probe_re = probe_ref[m, 0]
        probe_im = probe_ref[m, 1]
        update_re = update_re + (probe_re * change_re + probe_im * change_im)
        update_im = update_im + (probe_re * change_im - probe_im * change_re)
        grad_ref[m, 0] += patch_re * change_re + patch_im * change_im
        grad_ref[m, 1] += patch_re * change_im - patch_im * change_re
    update_ref[0, slot] = update_re.astype(update_ref.dtype)
    update_ref[1, slot] = update_im.astype(update_ref.dtype)


def entries_kernel(valid, patch, amp_in, probe_now, left, right):
    slots, length = amp_in.shape[0], amp_in.shape[-1]
    modes = probe_now.shape[0]
    flops = slots * 4 * 2 * (2 * length) * (2 * length) * (modes * length)
    whole = pl.BlockSpec(memory_space=pltpu.VMEM)
    grid_spec = pltpu.PrefetchScalarGridSpec(
        num_scalar_prefetch=1,
        grid=(1,),
        in_specs=[whole] * 5,
        out_specs=[whole] * 2,
    )
    return pl.pallas_call(
        entry_kernel,
        grid_spec=grid_spec,
        out_shape=[
            jax.ShapeDtypeStruct((2, slots, length, length), jnp.bfloat16),
            jax.ShapeDtypeStruct(probe_now.shape, jnp.float32),
        ],
        compiler_params=pltpu.CompilerParams(dimension_semantics=("arbitrary",)),
        cost_estimate=pl.CostEstimate(
            flops=flops,
            transcendentals=slots * length * length,
            bytes_accessed=slots * length * length * 10 + probe_now.size * 8,
        ),
    )(valid, patch, amp_in, probe_now, left, right)


def route(amplitudes, batch_ids, scan_tile, scan_offset, tiles_here):
    tile_count = lax.axis_size("tile")
    steps, batch_rows = batch_ids.shape
    capacity = max(2, 2 * batch_rows // tile_count)
    slots = tile_count * capacity
    length = amplitudes.shape[-1]
    target = scan_tile[:, :, 0]
    owner = target // tiles_here
    local_tile = target - owner * tiles_here
    onehot = (owner[:, :, None] == jnp.arange(tile_count, dtype=jnp.int32)).astype(jnp.int32)
    place_in = jnp.sum((jnp.cumsum(onehot, axis=1) - 1) * onehot, axis=2)
    slot_of = owner * capacity + place_in
    chosen = (slot_of[:, None, :] == jnp.arange(slots, dtype=jnp.int32)[None, :, None]).astype(
        jnp.int32
    )
    fields = jnp.stack(
        [local_tile, scan_offset[:, :, 0], scan_offset[:, :, 1], jnp.ones_like(local_tile)], axis=2
    )
    meta = jnp.sum(chosen[:, :, :, None] * fields[:, None, :, :], axis=2).astype(jnp.bfloat16)
    meta = jnp.pad(meta[:, :, None, :], ((0, 0), (0, 0), (0, 7), (0, length - 4)))
    ids = jnp.sum(chosen * batch_ids[:, None, :], axis=2)
    amp_send = amplitudes[ids.reshape(-1)].reshape(steps, slots, length, length)
    payload = jnp.concatenate([amp_send, meta], axis=2)
    return payload.reshape(steps, tile_count, capacity, length + 8, length)


def exchange(payload, size):
    tile_count, capacity, rows, length = payload.shape
    arrived = lax.all_to_all(payload, "tile", 0, 0, tiled=True).reshape(
        tile_count * capacity, rows, length
    )
    meta = arrived[:, length, :4].astype(jnp.int32)
    meta_in = jnp.stack([meta[:, 0] * size + meta[:, 1], meta[:, 2], meta[:, 3]], axis=1)
    return arrived, meta_in


def group_size(axes):
    count = 1
    for axis in axes:
        count *= lax.axis_size(axis)
    return count


def sum_over(value, axes, send_type):
    count = group_size(axes)
    parts = lax.all_to_all(value.astype(send_type).reshape(count, -1), axes, 0, 0, tiled=True)
    total = jnp.sum(parts.astype(jnp.float32), axis=0, keepdims=True).astype(send_type)
    return total, count


def all_sum_a2a(value, axes):
    total, count = sum_over(value, axes, value.dtype)
    spread = lax.all_to_all(jnp.broadcast_to(total, (count, total.shape[1])), axes, 0, 0, tiled=True)
    return spread.reshape(value.shape)


def all_sum_pairs(value, axis, send_type):
    count = lax.axis_size(axis)
    if count & (count - 1):
        return lax.psum(value.astype(send_type), axis).astype(jnp.float32)
    total = value.astype(send_type).astype(jnp.float32)
    step = 1
    while step < count:
        pairs = [(i, i ^ step) for i in range(count)]
        other = lax.ppermute(total.astype(send_type), axis, pairs)
        total = total.astype(send_type).astype(jnp.float32) + other.astype(jnp.float32)
        step *= 2
    return total


def entries_pass(stacked, probe_now, amp_in, meta_in, tables):
    table_re, table_im, table_neg = tables
    length = probe_now.shape[-1]
    rows_all, size = stacked.shape[1], stacked.shape[2]
    within = jnp.arange(length, dtype=jnp.int32)
    row_at, col_at, valid = meta_in[:, 0], meta_in[:, 1], meta_in[:, 2]
    pick_rows = (
        (row_at[:, None, None] + within[None, :, None])
        == jnp.arange(rows_all, dtype=jnp.int32)[None, None, :]
    ) & (valid[:, None, None] > 0)
    pick_rows = pick_rows.astype(jnp.bfloat16)
    pick_cols = (
        (col_at[:, None, None] + within[None, None, :])
        == jnp.arange(size, dtype=jnp.int32)[None, :, None]
    ).astype(jnp.bfloat16)
    rows = jnp.einsum(
        "skq,xqc->xskc", pick_rows, stacked, preferred_element_type=jnp.float32
    ).astype(jnp.bfloat16)
    patch = jnp.einsum("xskc,scl->xskl", rows, pick_cols, preferred_element_type=jnp.float32)
    left, right = block_tables(tables[0], tables[1])
    update, probe_grad = entries_kernel(
        valid, patch.astype(jnp.bfloat16), amp_in, probe_now, left, right
    )
    spread = jnp.einsum(
        "xskl,scl->xskc", update, pick_cols, preferred_element_type=jnp.float32
    ).astype(jnp.bfloat16)
    local_sum = jnp.einsum("skq,xskc->xqc", pick_rows, spread, preferred_element_type=jnp.float32)
    return local_sum, probe_grad


def one_step(tiles_now, probe_now, amp_in, meta_in, tables, batch_total):
    tiles_here, size = tiles_now.shape[1], tiles_now.shape[2]
    slots, length = amp_in.shape[0], amp_in.shape[-1]
    stacked = tiles_now.astype(jnp.bfloat16).reshape(2, tiles_here * size, size)
    chunk = max(d for d in range(1, min(slots, 24) + 1) if slots % d == 0)
    if chunk == slots:
        local_sum, probe_grad = entries_pass(stacked, probe_now, amp_in, meta_in, tables)
    else:

        def body(carry, piece):
            part_sum, part_grad = entries_pass(stacked, probe_now, piece[0], piece[1], tables)
            return (carry[0] + part_sum, carry[1] + part_grad), None

        start = (jnp.zeros(stacked.shape, jnp.float32), jnp.zeros(probe_now.shape, jnp.float32))
        pieces = (
            amp_in.reshape(slots // chunk, chunk, length + 8, length),
            meta_in.reshape(slots // chunk, chunk, 3),
        )
        (local_sum, probe_grad), _ = lax.scan(body, start, pieces)
    local_sum = local_sum.reshape(tiles_now.shape)
    probe_re = probe_now[:, 0]
    probe_im = probe_now[:, 1]
    peak_power = jnp.max(jnp.sum(probe_re * probe_re + probe_im * probe_im, axis=0))
    summed = all_sum_pairs(local_sum, "pat", jnp.bfloat16)
    tiles_next = tiles_now + summed / peak_power
    grad_sum = all_sum_a2a(probe_grad, ("tile", "pat"))
    probe_next = probe_now + probe_rate * grad_sum / batch_total
    return (tiles_next, probe_next, probe_grad)


def on_device(amplitudes, batch_ids, scan_tile, scan_offset, object_tiles, probe):
    tables = dft_tables(probe.shape[-1])
    tiles_here, size = object_tiles.shape[1], object_tiles.shape[2]
    batch_total = batch_ids.shape[1] * lax.axis_size("tile") * lax.axis_size("pat")
    payload = route(amplitudes, batch_ids, scan_tile, scan_offset, tiles_here)
    tiles_now = object_tiles
    probe_now = probe
    for step_no in range(batch_ids.shape[0]):
        amp_in, meta_in = exchange(payload[step_no], size)
        tiles_now, probe_now, _ = one_step(tiles_now, probe_now, amp_in, meta_in, tables, batch_total)
    return (tiles_now, probe_now)


def solution(mesh):
    in_specs = (
        P(("tile", "pat"), None, None),
        P(None, ("tile", "pat")),
        P(None, ("tile", "pat"), None),
        P(None, ("tile", "pat"), None),
        P(None, "tile", None, None),
        P(),
    )
    out_specs = (P(None, "tile", None, None), P())
    return jax.shard_map(
        on_device, mesh=mesh, in_specs=in_specs, out_specs=out_specs, check_vma=False
    )
```

```python
import math

import jax
import jax.numpy as jnp
from jax import lax
from jax.experimental import pallas as pl
from jax.experimental.pallas import tpu as pltpu
from jax.sharding import PartitionSpec as P

probe_rate = 8.0


def dft_tables(length):
    counter = jnp.arange(length, dtype=jnp.int32)
    product = counter[:, None] * counter[None, :] % length
    angle_table = 2.0 * math.pi / length * product.astype(jnp.float32)
    norm_factor = 1.0 / math.sqrt(length)
    table_re = (jnp.cos(angle_table) * norm_factor).astype(jnp.bfloat16)
    table_im = (-jnp.sin(angle_table) * norm_factor).astype(jnp.bfloat16)
    return (table_re, table_im, -table_im)


def transform(src_re, src_im, table_re, table_im):
    half_re = jnp.einsum(
        "kj,bmjc->bmkc", table_re, src_re, preferred_element_type=jnp.float32
    ) - jnp.einsum("kj,bmjc->bmkc", table_im, src_im, preferred_element_type=jnp.float32)
    half_im = jnp.einsum(
        "kj,bmjc->bmkc", table_re, src_im, preferred_element_type=jnp.float32
    ) + jnp.einsum("kj,bmjc->bmkc", table_im, src_re, preferred_element_type=jnp.float32)
    half_re = half_re.astype(jnp.bfloat16)
    half_im = half_im.astype(jnp.bfloat16)
    out_re = jnp.einsum(
        "bmkc,cl->bmkl", half_re, table_re, preferred_element_type=jnp.float32
    ) - jnp.einsum("bmkc,cl->bmkl", half_im, table_im, preferred_element_type=jnp.float32)
    out_im = jnp.einsum(
        "bmkc,cl->bmkl", half_re, table_im, preferred_element_type=jnp.float32
    ) + jnp.einsum("bmkc,cl->bmkl", half_im, table_re, preferred_element_type=jnp.float32)
    return (out_re, out_im)


def block_tables(table_re, table_im):
    left = jnp.concatenate(
        [jnp.concatenate([table_re, -table_im], 1), jnp.concatenate([table_im, table_re], 1)], 0
    )
    right = jnp.concatenate(
        [jnp.concatenate([table_re, table_im], 1), jnp.concatenate([-table_im, table_re], 1)], 0
    )
    return left, right


def entry_kernel(order_ref, patch_ref, amp_ref, probe_ref, left_ref, right_ref, update_ref, grad_ref):
    slots = order_ref.shape[0] - 1
    count = order_ref[slots]
    group = 2 if slots % 2 == 0 else 1
    grad_ref[...] = jnp.zeros(grad_ref.shape, grad_ref.dtype)
    update_ref[...] = jnp.zeros(update_ref.shape, update_ref.dtype)

    def one_group(index, carry):
        chosen = [order_ref[index * group + g] for g in range(group)]
        entry_body(chosen, patch_ref, amp_ref, probe_ref, left_ref, right_ref, update_ref, grad_ref)
        return carry

    lax.fori_loop(0, (count + group - 1) // group, one_group, 0)


def entry_body(chosen, patch_ref, amp_ref, probe_ref, left_ref, right_ref, update_ref, grad_ref):
    modes, length = probe_ref.shape[0], probe_ref.shape[-1]
    blocks = len(chosen) * modes
    patches = [
        (patch_ref[0, slot].astype(jnp.float32), patch_ref[1, slot].astype(jnp.float32))
        for slot in chosen
    ]
    left = left_ref[...]
    right = right_ref[...]
    exits_re, exits_im = [], []
    for patch_re, patch_im in patches:
        for m in range(modes):
            probe_re = probe_ref[m, 0]
            probe_im = probe_ref[m, 1]
            exits_re.append((probe_re * patch_re - probe_im * patch_im).astype(jnp.bfloat16))
            exits_im.append((probe_re * patch_im + probe_im * patch_re).astype(jnp.bfloat16))
    stacked = jnp.concatenate(
        [jnp.concatenate(exits_re, 1), jnp.concatenate(exits_im, 1)], 0
    )
    half = jnp.dot(left, stacked, preferred_element_type=jnp.float32).astype(jnp.bfloat16)

    def by_mode(wide):
        return jnp.concatenate(
            [
                jnp.concatenate(
                    [
                        wide[:length, j * length : (j + 1) * length],
                        wide[length:, j * length : (j + 1) * length],
                    ],
                    1,
                )
                for j in range(blocks)
            ],
            0,
        )

    def by_part(tall):
        return jnp.concatenate(
            [
                jnp.concatenate(
                    [tall[j * length : (j + 1) * length, :length] for j in range(blocks)], 1
                ),
                jnp.concatenate(
                    [tall[j * length : (j + 1) * length, length:] for j in range(blocks)], 1
                ),
            ],
            0,
        )

    far = jnp.dot(by_mode(half), right, preferred_element_type=jnp.float32)
    factors = []
    for g, slot in enumerate(chosen):
        intensity = jnp.zeros((length, length), jnp.float32)
        for m in range(modes):
            j = g * modes + m
            far_re = far[j * length : (j + 1) * length, :length]
            far_im = far[j * length : (j + 1) * length, length:]
            intensity = intensity + (far_re * far_re + far_im * far_im)
        measured = amp_ref[slot, :length, :].astype(jnp.float32)
        factor = measured / jnp.sqrt(jnp.maximum(intensity, 1.0)) - 1.0
        factors.extend([jnp.concatenate([factor, factor], 1)] * modes)
    scaled = (jnp.concatenate(factors, 0) * far).astype(jnp.bfloat16)
    back = jnp.dot(right, by_part(scaled), preferred_element_type=jnp.float32).astype(
        jnp.bfloat16
    )
    change = jnp.dot(by_mode(back), left, preferred_element_type=jnp.float32)
    grads = [[None, None] for _ in range(modes)]
    for g, slot in enumerate(chosen):
        patch_re, patch_im = patches[g]
        update_re = jnp.zeros((length, length), jnp.float32)
        update_im = jnp.zeros((length, length), jnp.float32)
        for m in range(modes):
            j = g * modes + m
            change_re = change[j * length : (j + 1) * length, :length]
            change_im = change[j * length : (j + 1) * length, length:]
            probe_re = probe_ref[m, 0]
            probe_im = probe_ref[m, 1]
            update_re = update_re + (probe_re * change_re + probe_im * change_im)
            update_im = update_im + (probe_re * change_im - probe_im * change_re)
            grad_re = patch_re * change_re + patch_im * change_im
            grad_im = patch_re * change_im - patch_im * change_re
            if g == 0:
                grads[m] = [grad_re, grad_im]
            else:
                grads[m] = [grads[m][0] + grad_re, grads[m][1] + grad_im]
        update_ref[0, slot] = update_re.astype(update_ref.dtype)
        update_ref[1, slot] = update_im.astype(update_ref.dtype)
    for m in range(modes):
        grad_ref[m, 0] += grads[m][0]
        grad_ref[m, 1] += grads[m][1]


def entries_kernel(order, patch, amp_in, probe_now, left, right):
    slots, length = amp_in.shape[0], amp_in.shape[-1]
    modes = probe_now.shape[0]
    flops = slots * 4 * 2 * (2 * length) * (2 * length) * (modes * length)
    whole = pl.BlockSpec(memory_space=pltpu.VMEM)
    grid_spec = pltpu.PrefetchScalarGridSpec(
        num_scalar_prefetch=1,
        grid=(1,),
        in_specs=[whole] * 5,
        out_specs=[whole] * 2,
    )
    return pl.pallas_call(
        entry_kernel,
        grid_spec=grid_spec,
        out_shape=[
            jax.ShapeDtypeStruct((2, slots, length, length), jnp.bfloat16),
            jax.ShapeDtypeStruct(probe_now.shape, jnp.float32),
        ],
        compiler_params=pltpu.CompilerParams(dimension_semantics=("arbitrary",)),
        cost_estimate=pl.CostEstimate(
            flops=flops,
            transcendentals=slots * length * length,
            bytes_accessed=slots * length * length * 10 + probe_now.size * 8,
        ),
    )(order, patch, amp_in, probe_now, left, right)


def route(amplitudes, batch_ids, scan_tile, scan_offset, tiles_here):
    tile_count = lax.axis_size("tile")
    steps, batch_rows = batch_ids.shape
    capacity = max(2, 2 * batch_rows // tile_count)
    slots = tile_count * capacity
    length = amplitudes.shape[-1]
    target = scan_tile[:, :, 0]
    owner = target // tiles_here
    local_tile = target - owner * tiles_here
    onehot = (owner[:, :, None] == jnp.arange(tile_count, dtype=jnp.int32)).astype(jnp.int32)
    place_in = jnp.sum((jnp.cumsum(onehot, axis=1) - 1) * onehot, axis=2)
    slot_of = owner * capacity + place_in
    chosen = (slot_of[:, None, :] == jnp.arange(slots, dtype=jnp.int32)[None, :, None]).astype(
        jnp.int32
    )
    fields = jnp.stack(
        [local_tile, scan_offset[:, :, 0], scan_offset[:, :, 1], jnp.ones_like(local_tile)], axis=2
    )
    meta = jnp.sum(chosen[:, :, :, None] * fields[:, None, :, :], axis=2).astype(jnp.bfloat16)
    meta = jnp.pad(meta[:, :, None, :], ((0, 0), (0, 0), (0, 7), (0, length - 4)))
    ids = jnp.sum(chosen * batch_ids[:, None, :], axis=2)
    amp_send = amplitudes[ids.reshape(-1)].reshape(steps, slots, length, length)
    payload = jnp.concatenate([amp_send, meta], axis=2)
    return payload.reshape(steps, tile_count, capacity, length + 8, length)


def exchange(payload, size):
    tile_count, capacity, rows, length = payload.shape
    arrived = lax.all_to_all(payload, "tile", 0, 0, tiled=True).reshape(
        tile_count * capacity, rows, length
    )
    meta = arrived[:, length, :4].astype(jnp.int32)
    meta_in = jnp.stack([meta[:, 0] * size + meta[:, 1], meta[:, 2], meta[:, 3]], axis=1)
    return arrived, meta_in


def group_size(axes):
    count = 1
    for axis in axes:
        count *= lax.axis_size(axis)
    return count


def sum_over(value, axes, send_type):
    count = group_size(axes)
    parts = lax.all_to_all(value.astype(send_type).reshape(count, -1), axes, 0, 0, tiled=True)
    total = jnp.sum(parts.astype(jnp.float32), axis=0, keepdims=True).astype(send_type)
    return total, count


def all_sum_a2a(value, axes):
    total, count = sum_over(value, axes, value.dtype)
    spread = lax.all_to_all(jnp.broadcast_to(total, (count, total.shape[1])), axes, 0, 0, tiled=True)
    return spread.reshape(value.shape)


def all_sum_pairs(value, axis, send_type):
    count = lax.axis_size(axis)
    if count & (count - 1):
        return lax.psum(value.astype(send_type), axis).astype(jnp.float32)
    total = value.astype(send_type).astype(jnp.float32)
    step = 1
    while step < count:
        pairs = [(i, i ^ step) for i in range(count)]
        other = lax.ppermute(total.astype(send_type), axis, pairs)
        total = total.astype(send_type).astype(jnp.float32) + other.astype(jnp.float32)
        step *= 2
    return total


def entries_pass(stacked, probe_now, amp_in, meta_in, tables):
    table_re, table_im, table_neg = tables
    length = probe_now.shape[-1]
    rows_all, size = stacked.shape[1], stacked.shape[2]
    within = jnp.arange(length, dtype=jnp.int32)
    row_at, col_at, valid = meta_in[:, 0], meta_in[:, 1], meta_in[:, 2]
    pick_rows = (
        (row_at[:, None, None] + within[None, :, None])
        == jnp.arange(rows_all, dtype=jnp.int32)[None, None, :]
    ) & (valid[:, None, None] > 0)
    pick_rows = pick_rows.astype(jnp.bfloat16)
    pick_cols = (
        (col_at[:, None, None] + within[None, None, :])
        == jnp.arange(size, dtype=jnp.int32)[None, :, None]
    ).astype(jnp.bfloat16)
    rows = jnp.einsum(
        "skq,xqc->xskc", pick_rows, stacked, preferred_element_type=jnp.float32
    ).astype(jnp.bfloat16)
    patch = jnp.einsum("xskc,scl->xskl", rows, pick_cols, preferred_element_type=jnp.float32)
    left, right = block_tables(tables[0], tables[1])
    held = (valid > 0).astype(jnp.int32)
    count = jnp.sum(held)
    place = jnp.where(held > 0, jnp.cumsum(held) - 1, count + jnp.cumsum(1 - held) - 1)
    slots = valid.shape[0]
    order = jnp.sum(
        (place[:, None] == jnp.arange(slots, dtype=jnp.int32)[None, :])
        * jnp.arange(slots, dtype=jnp.int32)[:, None],
        axis=0,
    )
    order = jnp.concatenate([order, count[None]]).astype(jnp.int32)
    update, probe_grad = entries_kernel(
        order, patch.astype(jnp.bfloat16), amp_in, probe_now, left, right
    )
    spread = jnp.einsum(
        "xskl,scl->xskc", update, pick_cols, preferred_element_type=jnp.float32
    ).astype(jnp.bfloat16)
    local_sum = jnp.einsum("skq,xskc->xqc", pick_rows, spread, preferred_element_type=jnp.float32)
    return local_sum, probe_grad


def one_step(tiles_now, probe_now, amp_in, meta_in, tables, batch_total):
    tiles_here, size = tiles_now.shape[1], tiles_now.shape[2]
    slots, length = amp_in.shape[0], amp_in.shape[-1]
    stacked = tiles_now.astype(jnp.bfloat16).reshape(2, tiles_here * size, size)
    chunk = max(d for d in range(1, min(slots, 24) + 1) if slots % d == 0)
    if chunk == slots:
        local_sum, probe_grad = entries_pass(stacked, probe_now, amp_in, meta_in, tables)
    else:

        def body(carry, piece):
            part_sum, part_grad = entries_pass(stacked, probe_now, piece[0], piece[1], tables)
            return (carry[0] + part_sum, carry[1] + part_grad), None

        start = (jnp.zeros(stacked.shape, jnp.float32), jnp.zeros(probe_now.shape, jnp.float32))
        pieces = (
            amp_in.reshape(slots // chunk, chunk, length + 8, length),
            meta_in.reshape(slots // chunk, chunk, 3),
        )
        (local_sum, probe_grad), _ = lax.scan(body, start, pieces)
    local_sum = local_sum.reshape(tiles_now.shape)
    probe_re = probe_now[:, 0]
    probe_im = probe_now[:, 1]
    peak_power = jnp.max(jnp.sum(probe_re * probe_re + probe_im * probe_im, axis=0))
    summed = all_sum_pairs(local_sum, "pat", jnp.bfloat16)
    tiles_next = tiles_now + summed / peak_power
    grad_sum = all_sum_a2a(probe_grad, ("tile", "pat"))
    probe_next = probe_now + probe_rate * grad_sum / batch_total
    return (tiles_next, probe_next, probe_grad)


def on_device(amplitudes, batch_ids, scan_tile, scan_offset, object_tiles, probe):
    tables = dft_tables(probe.shape[-1])
    tiles_here, size = object_tiles.shape[1], object_tiles.shape[2]
    batch_total = batch_ids.shape[1] * lax.axis_size("tile") * lax.axis_size("pat")
    payload = route(amplitudes, batch_ids, scan_tile, scan_offset, tiles_here)
    tiles_now = object_tiles
    probe_now = probe
    for step_no in range(batch_ids.shape[0]):
        amp_in, meta_in = exchange(payload[step_no], size)
        tiles_now, probe_now, _ = one_step(tiles_now, probe_now, amp_in, meta_in, tables, batch_total)
    return (tiles_now, probe_now)


def solution(mesh):
    in_specs = (
        P(("tile", "pat"), None, None),
        P(None, ("tile", "pat")),
        P(None, ("tile", "pat"), None),
        P(None, ("tile", "pat"), None),
        P(None, "tile", None, None),
        P(),
    )
    out_specs = (P(None, "tile", None, None), P())
    return jax.shard_map(
        on_device, mesh=mesh, in_specs=in_specs, out_specs=out_specs, check_vma=False
    )
```

```python
import math

import jax
import jax.numpy as jnp
from jax import lax
from jax.experimental import pallas as pl
from jax.experimental.pallas import tpu as pltpu
from jax.sharding import PartitionSpec as P

probe_rate = 8.0


def dft_tables(length):
    counter = jnp.arange(length, dtype=jnp.int32)
    product = counter[:, None] * counter[None, :] % length
    angle_table = 2.0 * math.pi / length * product.astype(jnp.float32)
    norm_factor = 1.0 / math.sqrt(length)
    table_re = (jnp.cos(angle_table) * norm_factor).astype(jnp.bfloat16)
    table_im = (-jnp.sin(angle_table) * norm_factor).astype(jnp.bfloat16)
    return (table_re, table_im, -table_im)


def transform(src_re, src_im, table_re, table_im):
    half_re = jnp.einsum(
        "kj,bmjc->bmkc", table_re, src_re, preferred_element_type=jnp.float32
    ) - jnp.einsum("kj,bmjc->bmkc", table_im, src_im, preferred_element_type=jnp.float32)
    half_im = jnp.einsum(
        "kj,bmjc->bmkc", table_re, src_im, preferred_element_type=jnp.float32
    ) + jnp.einsum("kj,bmjc->bmkc", table_im, src_re, preferred_element_type=jnp.float32)
    half_re = half_re.astype(jnp.bfloat16)
    half_im = half_im.astype(jnp.bfloat16)
    out_re = jnp.einsum(
        "bmkc,cl->bmkl", half_re, table_re, preferred_element_type=jnp.float32
    ) - jnp.einsum("bmkc,cl->bmkl", half_im, table_im, preferred_element_type=jnp.float32)
    out_im = jnp.einsum(
        "bmkc,cl->bmkl", half_re, table_im, preferred_element_type=jnp.float32
    ) + jnp.einsum("bmkc,cl->bmkl", half_im, table_re, preferred_element_type=jnp.float32)
    return (out_re, out_im)


def block_tables(table_re, table_im):
    left = jnp.concatenate(
        [jnp.concatenate([table_re, -table_im], 1), jnp.concatenate([table_im, table_re], 1)], 0
    )
    right = jnp.concatenate(
        [jnp.concatenate([table_re, table_im], 1), jnp.concatenate([-table_im, table_re], 1)], 0
    )
    return left, right


def entry_kernel(order_ref, patch_ref, amp_ref, probe_ref, left_ref, right_ref, update_ref, grad_ref):
    slots = order_ref.shape[0] - 1
    count = order_ref[slots]
    group = 2 if slots % 2 == 0 else 1
    grad_ref[...] = jnp.zeros(grad_ref.shape, grad_ref.dtype)
    update_ref[...] = jnp.zeros(update_ref.shape, update_ref.dtype)

    def one_group(index, carry):
        chosen = [order_ref[index * group + g] for g in range(group)]
        entry_body(chosen, patch_ref, amp_ref, probe_ref, left_ref, right_ref, update_ref, grad_ref)
        return carry

    lax.fori_loop(0, (count + group - 1) // group, one_group, 0)


def entry_body(chosen, patch_ref, amp_ref, probe_ref, left_ref, right_ref, update_ref, grad_ref):
    modes, length = probe_ref.shape[0], probe_ref.shape[-1]
    blocks = len(chosen) * modes
    patches = [
        (patch_ref[0, slot].astype(jnp.float32), patch_ref[1, slot].astype(jnp.float32))
        for slot in chosen
    ]
    left = left_ref[...]
    right = right_ref[...]
    exits_re, exits_im = [], []
    for patch_re, patch_im in patches:
        for m in range(modes):
            probe_re = probe_ref[m, 0]
            probe_im = probe_ref[m, 1]
            exits_re.append((probe_re * patch_re - probe_im * patch_im).astype(jnp.bfloat16))
            exits_im.append((probe_re * patch_im + probe_im * patch_re).astype(jnp.bfloat16))
    stacked = jnp.concatenate(
        [jnp.concatenate(exits_re, 1), jnp.concatenate(exits_im, 1)], 0
    )
    half = jnp.dot(left, stacked, preferred_element_type=jnp.float32).astype(jnp.bfloat16)

    def by_mode(wide):
        return jnp.concatenate(
            [
                jnp.concatenate(
                    [
                        wide[:length, j * length : (j + 1) * length],
                        wide[length:, j * length : (j + 1) * length],
                    ],
                    1,
                )
                for j in range(blocks)
            ],
            0,
        )

    def by_part(tall):
        return jnp.concatenate(
            [
                jnp.concatenate(
                    [tall[j * length : (j + 1) * length, :length] for j in range(blocks)], 1
                ),
                jnp.concatenate(
                    [tall[j * length : (j + 1) * length, length:] for j in range(blocks)], 1
                ),
            ],
            0,
        )

    far = jnp.dot(by_mode(half), right, preferred_element_type=jnp.float32)
    factors = []
    for g, slot in enumerate(chosen):
        intensity = jnp.zeros((length, length), jnp.float32)
        for m in range(modes):
            j = g * modes + m
            far_re = far[j * length : (j + 1) * length, :length]
            far_im = far[j * length : (j + 1) * length, length:]
            intensity = intensity + (far_re * far_re + far_im * far_im)
        measured = amp_ref[slot, :length, :].astype(jnp.float32)
        factor = measured / jnp.sqrt(jnp.maximum(intensity, 1.0)) - 1.0
        factors.extend([jnp.concatenate([factor, factor], 1)] * modes)
    scaled = (jnp.concatenate(factors, 0) * far).astype(jnp.bfloat16)
    back = jnp.dot(right, by_part(scaled), preferred_element_type=jnp.float32).astype(
        jnp.bfloat16
    )
    change = jnp.dot(by_mode(back), left, preferred_element_type=jnp.float32)
    grads = [[None, None] for _ in range(modes)]
    for g, slot in enumerate(chosen):
        patch_re, patch_im = patches[g]
        update_re = jnp.zeros((length, length), jnp.float32)
        update_im = jnp.zeros((length, length), jnp.float32)
        for m in range(modes):
            j = g * modes + m
            change_re = change[j * length : (j + 1) * length, :length]
            change_im = change[j * length : (j + 1) * length, length:]
            probe_re = probe_ref[m, 0]
            probe_im = probe_ref[m, 1]
            update_re = update_re + (probe_re * change_re + probe_im * change_im)
            update_im = update_im + (probe_re * change_im - probe_im * change_re)
            grad_re = patch_re * change_re + patch_im * change_im
            grad_im = patch_re * change_im - patch_im * change_re
            if g == 0:
                grads[m] = [grad_re, grad_im]
            else:
                grads[m] = [grads[m][0] + grad_re, grads[m][1] + grad_im]
        update_ref[0, slot] = update_re.astype(update_ref.dtype)
        update_ref[1, slot] = update_im.astype(update_ref.dtype)
    for m in range(modes):
        grad_ref[m, 0] += grads[m][0]
        grad_ref[m, 1] += grads[m][1]


def entries_kernel(order, patch, amp_in, probe_now, left, right):
    slots, length = amp_in.shape[0], amp_in.shape[-1]
    modes = probe_now.shape[0]
    flops = slots * 4 * 2 * (2 * length) * (2 * length) * (modes * length)
    whole = pl.BlockSpec(memory_space=pltpu.VMEM)
    grid_spec = pltpu.PrefetchScalarGridSpec(
        num_scalar_prefetch=1,
        grid=(1,),
        in_specs=[whole] * 5,
        out_specs=[whole] * 2,
    )
    return pl.pallas_call(
        entry_kernel,
        grid_spec=grid_spec,
        out_shape=[
            jax.ShapeDtypeStruct((2, slots, length, length), jnp.bfloat16),
            jax.ShapeDtypeStruct(probe_now.shape, jnp.float32),
        ],
        compiler_params=pltpu.CompilerParams(dimension_semantics=("arbitrary",)),
        cost_estimate=pl.CostEstimate(
            flops=flops,
            transcendentals=slots * length * length,
            bytes_accessed=slots * length * length * 10 + probe_now.size * 8,
        ),
    )(order, patch, amp_in, probe_now, left, right)


def route(amplitudes, batch_ids, scan_tile, scan_offset, tiles_here):
    tile_count = lax.axis_size("tile")
    steps, batch_rows = batch_ids.shape
    capacity = max(2, 2 * batch_rows // tile_count)
    slots = tile_count * capacity
    length = amplitudes.shape[-1]
    target = scan_tile[:, :, 0]
    owner = target // tiles_here
    local_tile = target - owner * tiles_here
    onehot = (owner[:, :, None] == jnp.arange(tile_count, dtype=jnp.int32)).astype(jnp.int32)
    place_in = jnp.sum((jnp.cumsum(onehot, axis=1) - 1) * onehot, axis=2)
    slot_of = owner * capacity + place_in
    chosen = (slot_of[:, None, :] == jnp.arange(slots, dtype=jnp.int32)[None, :, None]).astype(
        jnp.int32
    )
    fields = jnp.stack(
        [local_tile, scan_offset[:, :, 0], scan_offset[:, :, 1], jnp.ones_like(local_tile)], axis=2
    )
    meta = jnp.sum(chosen[:, :, :, None] * fields[:, None, :, :], axis=2).astype(jnp.bfloat16)
    meta = jnp.pad(meta[:, :, None, :], ((0, 0), (0, 0), (0, 7), (0, length - 4)))
    ids = jnp.sum(chosen * batch_ids[:, None, :], axis=2)
    amp_send = amplitudes[ids.reshape(-1)].reshape(steps, slots, length, length)
    payload = jnp.concatenate([amp_send, meta], axis=2)
    return payload.reshape(steps, tile_count, capacity, length + 8, length)


def unpack(arrived, size):
    tile_count, capacity, rows, length = arrived.shape
    arrived = arrived.reshape(tile_count * capacity, rows, length)
    meta = arrived[:, length, :4].astype(jnp.int32)
    meta_in = jnp.stack([meta[:, 0] * size + meta[:, 1], meta[:, 2], meta[:, 3]], axis=1)
    return arrived, meta_in


def group_size(axes):
    count = 1
    for axis in axes:
        count *= lax.axis_size(axis)
    return count


def sum_over(value, axes, send_type):
    count = group_size(axes)
    parts = lax.all_to_all(value.astype(send_type).reshape(count, -1), axes, 0, 0, tiled=True)
    total = jnp.sum(parts.astype(jnp.float32), axis=0, keepdims=True).astype(send_type)
    return total, count


def all_sum_a2a(value, axes):
    total, count = sum_over(value, axes, value.dtype)
    spread = lax.all_to_all(jnp.broadcast_to(total, (count, total.shape[1])), axes, 0, 0, tiled=True)
    return spread.reshape(value.shape)


def all_sum_pairs(value, axis, send_type):
    count = lax.axis_size(axis)
    if count & (count - 1):
        return lax.psum(value.astype(send_type), axis).astype(jnp.float32)
    total = value.astype(send_type).astype(jnp.float32)
    step = 1
    while step < count:
        pairs = [(i, i ^ step) for i in range(count)]
        other = lax.ppermute(total.astype(send_type), axis, pairs)
        total = total.astype(send_type).astype(jnp.float32) + other.astype(jnp.float32)
        step *= 2
    return total


def entries_pass(stacked, probe_now, amp_in, meta_in, tables):
    table_re, table_im, table_neg = tables
    length = probe_now.shape[-1]
    rows_all, size = stacked.shape[1], stacked.shape[2]
    within = jnp.arange(length, dtype=jnp.int32)
    row_at, col_at, valid = meta_in[:, 0], meta_in[:, 1], meta_in[:, 2]
    pick_rows = (
        (row_at[:, None, None] + within[None, :, None])
        == jnp.arange(rows_all, dtype=jnp.int32)[None, None, :]
    ) & (valid[:, None, None] > 0)
    pick_rows = pick_rows.astype(jnp.bfloat16)
    pick_cols = (
        (col_at[:, None, None] + within[None, None, :])
        == jnp.arange(size, dtype=jnp.int32)[None, :, None]
    ).astype(jnp.bfloat16)
    rows = jnp.einsum(
        "skq,xqc->xskc", pick_rows, stacked, preferred_element_type=jnp.float32
    ).astype(jnp.bfloat16)
    patch = jnp.einsum("xskc,scl->xskl", rows, pick_cols, preferred_element_type=jnp.float32)
    left, right = block_tables(tables[0], tables[1])
    held = (valid > 0).astype(jnp.int32)
    count = jnp.sum(held)
    place = jnp.where(held > 0, jnp.cumsum(held) - 1, count + jnp.cumsum(1 - held) - 1)
    slots = valid.shape[0]
    order = jnp.sum(
        (place[:, None] == jnp.arange(slots, dtype=jnp.int32)[None, :])
        * jnp.arange(slots, dtype=jnp.int32)[:, None],
        axis=0,
    )
    order = jnp.concatenate([order, count[None]]).astype(jnp.int32)
    update, probe_grad = entries_kernel(
        order, patch.astype(jnp.bfloat16), amp_in, probe_now, left, right
    )
    spread = jnp.einsum(
        "xskl,scl->xskc", update, pick_cols, preferred_element_type=jnp.float32
    ).astype(jnp.bfloat16)
    local_sum = jnp.einsum("skq,xskc->xqc", pick_rows, spread, preferred_element_type=jnp.float32)
    return local_sum, probe_grad


def one_step(tiles_now, probe_now, amp_in, meta_in, tables, batch_total):
    tiles_here, size = tiles_now.shape[1], tiles_now.shape[2]
    slots, length = amp_in.shape[0], amp_in.shape[-1]
    stacked = tiles_now.astype(jnp.bfloat16).reshape(2, tiles_here * size, size)
    chunk = max(d for d in range(1, min(slots, 24) + 1) if slots % d == 0)
    if chunk == slots:
        local_sum, probe_grad = entries_pass(stacked, probe_now, amp_in, meta_in, tables)
    else:

        def body(carry, piece):
            part_sum, part_grad = entries_pass(stacked, probe_now, piece[0], piece[1], tables)
            return (carry[0] + part_sum, carry[1] + part_grad), None

        start = (jnp.zeros(stacked.shape, jnp.float32), jnp.zeros(probe_now.shape, jnp.float32))
        pieces = (
            amp_in.reshape(slots // chunk, chunk, length + 8, length),
            meta_in.reshape(slots // chunk, chunk, 3),
        )
        (local_sum, probe_grad), _ = lax.scan(body, start, pieces)
    local_sum = local_sum.reshape(tiles_now.shape)
    probe_re = probe_now[:, 0]
    probe_im = probe_now[:, 1]
    peak_power = jnp.max(jnp.sum(probe_re * probe_re + probe_im * probe_im, axis=0))
    summed = all_sum_pairs(local_sum, "pat", jnp.bfloat16)
    tiles_next = tiles_now + summed / peak_power
    grad_sum = all_sum_a2a(probe_grad, ("tile", "pat"))
    probe_next = probe_now + probe_rate * grad_sum / batch_total
    return (tiles_next, probe_next, probe_grad)


def on_device(amplitudes, batch_ids, scan_tile, scan_offset, object_tiles, probe):
    tables = dft_tables(probe.shape[-1])
    tiles_here, size = object_tiles.shape[1], object_tiles.shape[2]
    batch_total = batch_ids.shape[1] * lax.axis_size("tile") * lax.axis_size("pat")
    payload = route(amplitudes, batch_ids, scan_tile, scan_offset, tiles_here)
    tiles_now = object_tiles
    probe_now = probe
    arrived = lax.all_to_all(jnp.swapaxes(payload, 0, 1), "tile", 0, 0, tiled=True)
    for step_no in range(batch_ids.shape[0]):
        amp_in, meta_in = unpack(arrived[:, step_no], size)
        tiles_now, probe_now, _ = one_step(tiles_now, probe_now, amp_in, meta_in, tables, batch_total)
    return (tiles_now, probe_now)


def solution(mesh):
    in_specs = (
        P(("tile", "pat"), None, None),
        P(None, ("tile", "pat")),
        P(None, ("tile", "pat"), None),
        P(None, ("tile", "pat"), None),
        P(None, "tile", None, None),
        P(),
    )
    out_specs = (P(None, "tile", None, None), P())
    return jax.shard_map(
        on_device, mesh=mesh, in_specs=in_specs, out_specs=out_specs, check_vma=False
    )
```

```python
import math

import jax
import jax.numpy as jnp
from jax import lax
from jax.experimental import pallas as pl
from jax.experimental.pallas import tpu as pltpu
from jax.sharding import PartitionSpec as P

probe_rate = 8.0


def dft_tables(length):
    counter = jnp.arange(length, dtype=jnp.int32)
    product = counter[:, None] * counter[None, :] % length
    angle_table = 2.0 * math.pi / length * product.astype(jnp.float32)
    norm_factor = 1.0 / math.sqrt(length)
    table_re = (jnp.cos(angle_table) * norm_factor).astype(jnp.bfloat16)
    table_im = (-jnp.sin(angle_table) * norm_factor).astype(jnp.bfloat16)
    return (table_re, table_im, -table_im)


def transform(src_re, src_im, table_re, table_im):
    half_re = jnp.einsum(
        "kj,bmjc->bmkc", table_re, src_re, preferred_element_type=jnp.float32
    ) - jnp.einsum("kj,bmjc->bmkc", table_im, src_im, preferred_element_type=jnp.float32)
    half_im = jnp.einsum(
        "kj,bmjc->bmkc", table_re, src_im, preferred_element_type=jnp.float32
    ) + jnp.einsum("kj,bmjc->bmkc", table_im, src_re, preferred_element_type=jnp.float32)
    half_re = half_re.astype(jnp.bfloat16)
    half_im = half_im.astype(jnp.bfloat16)
    out_re = jnp.einsum(
        "bmkc,cl->bmkl", half_re, table_re, preferred_element_type=jnp.float32
    ) - jnp.einsum("bmkc,cl->bmkl", half_im, table_im, preferred_element_type=jnp.float32)
    out_im = jnp.einsum(
        "bmkc,cl->bmkl", half_re, table_im, preferred_element_type=jnp.float32
    ) + jnp.einsum("bmkc,cl->bmkl", half_im, table_re, preferred_element_type=jnp.float32)
    return (out_re, out_im)


def block_tables(table_re, table_im):
    left = jnp.concatenate(
        [jnp.concatenate([table_re, -table_im], 1), jnp.concatenate([table_im, table_re], 1)], 0
    )
    right = jnp.concatenate(
        [jnp.concatenate([table_re, table_im], 1), jnp.concatenate([-table_im, table_re], 1)], 0
    )
    return left, right


def entry_kernel(table_ref, tile_ref, amp_ref, probe_ref, left_ref, right_ref, sum_ref, grad_ref):
    slots = amp_ref.shape[0]
    count = table_ref[slots]
    group = 2 if slots % 2 == 0 else 1
    grad_ref[...] = jnp.zeros(grad_ref.shape, grad_ref.dtype)
    sum_ref[...] = jnp.zeros(sum_ref.shape, sum_ref.dtype)

    def one_group(index, carry):
        chosen = [table_ref[index * group + g] for g in range(group)]
        entry_body(chosen, table_ref, tile_ref, amp_ref, probe_ref, left_ref, right_ref, sum_ref, grad_ref)
        return carry

    lax.fori_loop(0, (count + group - 1) // group, one_group, 0)


def one_hot(shape, offset, keep=None):
    rows = lax.broadcasted_iota(jnp.int32, shape, 0)
    cols = lax.broadcasted_iota(jnp.int32, shape, 1)
    hit = cols - rows == offset
    if keep is not None:
        hit = hit & keep
    return jnp.where(hit, 1.0, 0.0).astype(jnp.bfloat16)


def entry_body(chosen, table_ref, tile_ref, amp_ref, probe_ref, left_ref, right_ref, sum_ref, grad_ref):
    modes, length = probe_ref.shape[0], probe_ref.shape[-1]
    slots = amp_ref.shape[0]
    rows_all, size = tile_ref.shape[1], tile_ref.shape[2]
    window = length + 16
    blocks = len(chosen) * modes
    places, patches = [], []
    for slot in chosen:
        row = table_ref[slots + 1 + slot]
        col = table_ref[2 * slots + 1 + slot]
        keep = table_ref[3 * slots + 1 + slot] != 0
        base = jnp.minimum((row // 8) * 8, rows_all - window)
        shift = row - base
        pick_rows = one_hot((length, window), shift, keep)
        pick_cols = one_hot((size, length), -col)
        spread_cols = one_hot((length, size), col)
        spread_rows = one_hot((window, length), -shift, keep)
        start = pl.multiple_of(base, 8)
        parts = []
        for x in range(2):
            near = tile_ref[x, pl.ds(start, window), :].astype(jnp.bfloat16)
            rows = jnp.dot(pick_rows, near, preferred_element_type=jnp.float32).astype(jnp.bfloat16)
            parts.append(jnp.dot(rows, pick_cols, preferred_element_type=jnp.float32))
        places.append((start, spread_cols, spread_rows))
        patches.append(tuple(parts))
    left = left_ref[...]
    right = right_ref[...]
    exits_re, exits_im = [], []
    for patch_re, patch_im in patches:
        for m in range(modes):
            probe_re = probe_ref[m, 0]
            probe_im = probe_ref[m, 1]
            exits_re.append((probe_re * patch_re - probe_im * patch_im).astype(jnp.bfloat16))
            exits_im.append((probe_re * patch_im + probe_im * patch_re).astype(jnp.bfloat16))
    stacked = jnp.concatenate(
        [jnp.concatenate(exits_re, 1), jnp.concatenate(exits_im, 1)], 0
    )
    half = jnp.dot(left, stacked, preferred_element_type=jnp.float32).astype(jnp.bfloat16)

    def by_mode(wide):
        return jnp.concatenate(
            [
                jnp.concatenate(
                    [
                        wide[:length, j * length : (j + 1) * length],
                        wide[length:, j * length : (j + 1) * length],
                    ],
                    1,
                )
                for j in range(blocks)
            ],
            0,
        )

    def by_part(tall):
        return jnp.concatenate(
            [
                jnp.concatenate(
                    [tall[j * length : (j + 1) * length, :length] for j in range(blocks)], 1
                ),
                jnp.concatenate(
                    [tall[j * length : (j + 1) * length, length:] for j in range(blocks)], 1
                ),
            ],
            0,
        )

    far = jnp.dot(by_mode(half), right, preferred_element_type=jnp.float32)
    factors = []
    for g, slot in enumerate(chosen):
        intensity = jnp.zeros((length, length), jnp.float32)
        for m in range(modes):
            j = g * modes + m
            far_re = far[j * length : (j + 1) * length, :length]
            far_im = far[j * length : (j + 1) * length, length:]
            intensity = intensity + (far_re * far_re + far_im * far_im)
        measured = amp_ref[slot, :length, :].astype(jnp.float32)
        factor = measured / jnp.sqrt(jnp.maximum(intensity, 1.0)) - 1.0
        factors.extend([jnp.concatenate([factor, factor], 1)] * modes)
    scaled = (jnp.concatenate(factors, 0) * far).astype(jnp.bfloat16)
    back = jnp.dot(right, by_part(scaled), preferred_element_type=jnp.float32).astype(
        jnp.bfloat16
    )
    change = jnp.dot(by_mode(back), left, preferred_element_type=jnp.float32)
    grads = [[None, None] for _ in range(modes)]
    for g, slot in enumerate(chosen):
        patch_re, patch_im = patches[g]
        update_re = jnp.zeros((length, length), jnp.float32)
        update_im = jnp.zeros((length, length), jnp.float32)
        for m in range(modes):
            j = g * modes + m
            change_re = change[j * length : (j + 1) * length, :length]
            change_im = change[j * length : (j + 1) * length, length:]
            probe_re = probe_ref[m, 0]
            probe_im = probe_ref[m, 1]
            update_re = update_re + (probe_re * change_re + probe_im * change_im)
            update_im = update_im + (probe_re * change_im - probe_im * change_re)
            grad_re = patch_re * change_re + patch_im * change_im
            grad_im = patch_re * change_im - patch_im * change_re
            if g == 0:
                grads[m] = [grad_re, grad_im]
            else:
                grads[m] = [grads[m][0] + grad_re, grads[m][1] + grad_im]
        start, spread_cols, spread_rows = places[g]
        for x, update in enumerate((update_re, update_im)):
            wide = jnp.dot(
                update.astype(jnp.bfloat16), spread_cols, preferred_element_type=jnp.float32
            ).astype(jnp.bfloat16)
            sum_ref[x, pl.ds(start, window), :] += jnp.dot(
                spread_rows, wide, preferred_element_type=jnp.float32
            )
    for m in range(modes):
        grad_ref[m, 0] += grads[m][0]
        grad_ref[m, 1] += grads[m][1]


def entries_kernel(table, tile, amp_in, probe_now, left, right):
    slots, length = amp_in.shape[0], amp_in.shape[-1]
    modes = probe_now.shape[0]
    rows_all, size = tile.shape[1], tile.shape[2]
    flops = slots * 4 * 2 * (2 * length) * (2 * length) * (modes * length)
    flops += slots * 8 * 2 * length * (length + 16) * size
    whole = pl.BlockSpec(memory_space=pltpu.VMEM)
    grid_spec = pltpu.PrefetchScalarGridSpec(
        num_scalar_prefetch=1,
        grid=(1,),
        in_specs=[whole] * 5,
        out_specs=[whole] * 2,
    )
    return pl.pallas_call(
        entry_kernel,
        grid_spec=grid_spec,
        out_shape=[
            jax.ShapeDtypeStruct(tile.shape, jnp.float32),
            jax.ShapeDtypeStruct(probe_now.shape, jnp.float32),
        ],
        compiler_params=pltpu.CompilerParams(dimension_semantics=("arbitrary",)),
        cost_estimate=pl.CostEstimate(
            flops=flops,
            transcendentals=slots * length * length,
            bytes_accessed=slots * length * length * 2 + tile.size * 8 + probe_now.size * 8,
        ),
    )(table, tile, amp_in, probe_now, left, right)


def route(amplitudes, batch_ids, scan_tile, scan_offset, tiles_here):
    tile_count = lax.axis_size("tile")
    steps, batch_rows = batch_ids.shape
    capacity = max(2, 2 * batch_rows // tile_count)
    slots = tile_count * capacity
    length = amplitudes.shape[-1]
    target = scan_tile[:, :, 0]
    owner = target // tiles_here
    local_tile = target - owner * tiles_here
    onehot = (owner[:, :, None] == jnp.arange(tile_count, dtype=jnp.int32)).astype(jnp.int32)
    place_in = jnp.sum((jnp.cumsum(onehot, axis=1) - 1) * onehot, axis=2)
    slot_of = owner * capacity + place_in
    chosen = (slot_of[:, None, :] == jnp.arange(slots, dtype=jnp.int32)[None, :, None]).astype(
        jnp.int32
    )
    fields = jnp.stack(
        [local_tile, scan_offset[:, :, 0], scan_offset[:, :, 1], jnp.ones_like(local_tile)], axis=2
    )
    meta = jnp.sum(chosen[:, :, :, None] * fields[:, None, :, :], axis=2).astype(jnp.bfloat16)
    meta = jnp.pad(meta[:, :, None, :], ((0, 0), (0, 0), (0, 7), (0, length - 4)))
    ids = jnp.sum(chosen * batch_ids[:, None, :], axis=2)
    amp_send = amplitudes[ids.reshape(-1)].reshape(steps, slots, length, length)
    payload = jnp.concatenate([amp_send, meta], axis=2)
    return payload.reshape(steps, tile_count, capacity, length + 8, length)


def unpack(arrived, size):
    tile_count, capacity, rows, length = arrived.shape
    arrived = arrived.reshape(tile_count * capacity, rows, length)
    meta = arrived[:, length, :4].astype(jnp.int32)
    meta_in = jnp.stack([meta[:, 0] * size + meta[:, 1], meta[:, 2], meta[:, 3]], axis=1)
    return arrived, meta_in


def group_size(axes):
    count = 1
    for axis in axes:
        count *= lax.axis_size(axis)
    return count


def sum_over(value, axes, send_type):
    count = group_size(axes)
    parts = lax.all_to_all(value.astype(send_type).reshape(count, -1), axes, 0, 0, tiled=True)
    total = jnp.sum(parts.astype(jnp.float32), axis=0, keepdims=True).astype(send_type)
    return total, count


def all_sum_a2a(value, axes):
    total, count = sum_over(value, axes, value.dtype)
    spread = lax.all_to_all(jnp.broadcast_to(total, (count, total.shape[1])), axes, 0, 0, tiled=True)
    return spread.reshape(value.shape)


def all_sum_pairs(value, axis, send_type):
    count = lax.axis_size(axis)
    if count & (count - 1):
        return lax.psum(value.astype(send_type), axis).astype(jnp.float32)
    total = value.astype(send_type).astype(jnp.float32)
    step = 1
    while step < count:
        pairs = [(i, i ^ step) for i in range(count)]
        other = lax.ppermute(total.astype(send_type), axis, pairs)
        total = total.astype(send_type).astype(jnp.float32) + other.astype(jnp.float32)
        step *= 2
    return total


def entries_pass(stacked, probe_now, amp_in, meta_in, tables):
    row_at, col_at, valid = meta_in[:, 0], meta_in[:, 1], meta_in[:, 2]
    left, right = block_tables(tables[0], tables[1])
    held = (valid > 0).astype(jnp.int32)
    count = jnp.sum(held)
    place = jnp.where(held > 0, jnp.cumsum(held) - 1, count + jnp.cumsum(1 - held) - 1)
    slots = valid.shape[0]
    order = jnp.sum(
        (place[:, None] == jnp.arange(slots, dtype=jnp.int32)[None, :])
        * jnp.arange(slots, dtype=jnp.int32)[:, None],
        axis=0,
    )
    table = jnp.concatenate([order, count[None], row_at, col_at, held]).astype(jnp.int32)
    return entries_kernel(table, stacked, amp_in, probe_now, left, right)


def one_step(tiles_now, probe_now, amp_in, meta_in, tables, batch_total):
    tiles_here, size = tiles_now.shape[1], tiles_now.shape[2]
    slots, length = amp_in.shape[0], amp_in.shape[-1]
    stacked = tiles_now.reshape(2, tiles_here * size, size)
    chunk = max(d for d in range(1, min(slots, 24) + 1) if slots % d == 0)
    if chunk == slots:
        local_sum, probe_grad = entries_pass(stacked, probe_now, amp_in, meta_in, tables)
    else:

        def body(carry, piece):
            part_sum, part_grad = entries_pass(stacked, probe_now, piece[0], piece[1], tables)
            return (carry[0] + part_sum, carry[1] + part_grad), None

        start = (jnp.zeros(stacked.shape, jnp.float32), jnp.zeros(probe_now.shape, jnp.float32))
        pieces = (
            amp_in.reshape(slots // chunk, chunk, length + 8, length),
            meta_in.reshape(slots // chunk, chunk, 3),
        )
        (local_sum, probe_grad), _ = lax.scan(body, start, pieces)
    local_sum = local_sum.reshape(tiles_now.shape)
    probe_re = probe_now[:, 0]
    probe_im = probe_now[:, 1]
    peak_power = jnp.max(jnp.sum(probe_re * probe_re + probe_im * probe_im, axis=0))
    summed = all_sum_pairs(local_sum, "pat", jnp.bfloat16)
    tiles_next = tiles_now + summed / peak_power
    grad_sum = all_sum_a2a(probe_grad, ("tile", "pat"))
    probe_next = probe_now + probe_rate * grad_sum / batch_total
    return (tiles_next, probe_next, probe_grad)


def on_device(amplitudes, batch_ids, scan_tile, scan_offset, object_tiles, probe):
    tables = dft_tables(probe.shape[-1])
    tiles_here, size = object_tiles.shape[1], object_tiles.shape[2]
    batch_total = batch_ids.shape[1] * lax.axis_size("tile") * lax.axis_size("pat")
    payload = route(amplitudes, batch_ids, scan_tile, scan_offset, tiles_here)
    tiles_now = object_tiles
    probe_now = probe
    arrived = lax.all_to_all(jnp.swapaxes(payload, 0, 1), "tile", 0, 0, tiled=True)
    for step_no in range(batch_ids.shape[0]):
        amp_in, meta_in = unpack(arrived[:, step_no], size)
        tiles_now, probe_now, _ = one_step(tiles_now, probe_now, amp_in, meta_in, tables, batch_total)
    return (tiles_now, probe_now)


def solution(mesh):
    in_specs = (
        P(("tile", "pat"), None, None),
        P(None, ("tile", "pat")),
        P(None, ("tile", "pat"), None),
        P(None, ("tile", "pat"), None),
        P(None, "tile", None, None),
        P(),
    )
    out_specs = (P(None, "tile", None, None), P())
    return jax.shard_map(
        on_device, mesh=mesh, in_specs=in_specs, out_specs=out_specs, check_vma=False
    )
```

```python
import math

import jax
import jax.numpy as jnp
from jax import lax
from jax.experimental import pallas as pl
from jax.experimental.pallas import tpu as pltpu
from jax.sharding import PartitionSpec as P

probe_rate = 8.0


def dft_tables(length):
    counter = jnp.arange(length, dtype=jnp.int32)
    product = counter[:, None] * counter[None, :] % length
    angle_table = 2.0 * math.pi / length * product.astype(jnp.float32)
    norm_factor = 1.0 / math.sqrt(length)
    table_re = (jnp.cos(angle_table) * norm_factor).astype(jnp.bfloat16)
    table_im = (-jnp.sin(angle_table) * norm_factor).astype(jnp.bfloat16)
    return (table_re, table_im, -table_im)


def transform(src_re, src_im, table_re, table_im):
    half_re = jnp.einsum(
        "kj,bmjc->bmkc", table_re, src_re, preferred_element_type=jnp.float32
    ) - jnp.einsum("kj,bmjc->bmkc", table_im, src_im, preferred_element_type=jnp.float32)
    half_im = jnp.einsum(
        "kj,bmjc->bmkc", table_re, src_im, preferred_element_type=jnp.float32
    ) + jnp.einsum("kj,bmjc->bmkc", table_im, src_re, preferred_element_type=jnp.float32)
    half_re = half_re.astype(jnp.bfloat16)
    half_im = half_im.astype(jnp.bfloat16)
    out_re = jnp.einsum(
        "bmkc,cl->bmkl", half_re, table_re, preferred_element_type=jnp.float32
    ) - jnp.einsum("bmkc,cl->bmkl", half_im, table_im, preferred_element_type=jnp.float32)
    out_im = jnp.einsum(
        "bmkc,cl->bmkl", half_re, table_im, preferred_element_type=jnp.float32
    ) + jnp.einsum("bmkc,cl->bmkl", half_im, table_re, preferred_element_type=jnp.float32)
    return (out_re, out_im)


def block_tables(table_re, table_im):
    left = jnp.concatenate(
        [jnp.concatenate([table_re, -table_im], 1), jnp.concatenate([table_im, table_re], 1)], 0
    )
    right = jnp.concatenate(
        [jnp.concatenate([table_re, table_im], 1), jnp.concatenate([-table_im, table_re], 1)], 0
    )
    return left, right


def entry_kernel(order_ref, patch_ref, amp_ref, probe_ref, left_ref, right_ref, update_ref, grad_ref):
    slots = order_ref.shape[0] - 1
    count = order_ref[slots]
    group = next(size for size in (4, 2, 1) if slots % size == 0)
    grad_ref[...] = jnp.zeros(grad_ref.shape, grad_ref.dtype)
    update_ref[...] = jnp.zeros(update_ref.shape, update_ref.dtype)

    def one_group(index, carry):
        chosen = [order_ref[index * group + g] for g in range(group)]
        entry_body(chosen, patch_ref, amp_ref, probe_ref, left_ref, right_ref, update_ref, grad_ref)
        return carry

    lax.fori_loop(0, (count + group - 1) // group, one_group, 0)


def entry_body(chosen, patch_ref, amp_ref, probe_ref, left_ref, right_ref, update_ref, grad_ref):
    modes, length = probe_ref.shape[0], probe_ref.shape[-1]
    blocks = len(chosen) * modes
    patches = [
        (patch_ref[0, slot].astype(jnp.float32), patch_ref[1, slot].astype(jnp.float32))
        for slot in chosen
    ]
    left = left_ref[...]
    right = right_ref[...]
    exits_re, exits_im = [], []
    for patch_re, patch_im in patches:
        for m in range(modes):
            probe_re = probe_ref[m, 0]
            probe_im = probe_ref[m, 1]
            exits_re.append((probe_re * patch_re - probe_im * patch_im).astype(jnp.bfloat16))
            exits_im.append((probe_re * patch_im + probe_im * patch_re).astype(jnp.bfloat16))
    stacked = jnp.concatenate(
        [jnp.concatenate(exits_re, 1), jnp.concatenate(exits_im, 1)], 0
    )
    half = jnp.dot(left, stacked, preferred_element_type=jnp.float32).astype(jnp.bfloat16)

    def by_mode(wide):
        return jnp.concatenate(
            [
                jnp.concatenate(
                    [
                        wide[:length, j * length : (j + 1) * length],
                        wide[length:, j * length : (j + 1) * length],
                    ],
                    1,
                )
                for j in range(blocks)
            ],
            0,
        )

    def by_part(tall):
        return jnp.concatenate(
            [
                jnp.concatenate(
                    [tall[j * length : (j + 1) * length, :length] for j in range(blocks)], 1
                ),
                jnp.concatenate(
                    [tall[j * length : (j + 1) * length, length:] for j in range(blocks)], 1
                ),
            ],
            0,
        )

    far = jnp.dot(by_mode(half), right, preferred_element_type=jnp.float32)
    factors = []
    for g, slot in enumerate(chosen):
        intensity = jnp.zeros((length, length), jnp.float32)
        for m in range(modes):
            j = g * modes + m
            far_re = far[j * length : (j + 1) * length, :length]
            far_im = far[j * length : (j + 1) * length, length:]
            intensity = intensity + (far_re * far_re + far_im * far_im)
        measured = amp_ref[slot, :length, :].astype(jnp.float32)
        factor = measured / jnp.sqrt(jnp.maximum(intensity, 1.0)) - 1.0
        factors.extend([jnp.concatenate([factor, factor], 1)] * modes)
    scaled = (jnp.concatenate(factors, 0) * far).astype(jnp.bfloat16)
    back = jnp.dot(right, by_part(scaled), preferred_element_type=jnp.float32).astype(
        jnp.bfloat16
    )
    change = jnp.dot(by_mode(back), left, preferred_element_type=jnp.float32)
    grads = [[None, None] for _ in range(modes)]
    for g, slot in enumerate(chosen):
        patch_re, patch_im = patches[g]
        update_re = jnp.zeros((length, length), jnp.float32)
        update_im = jnp.zeros((length, length), jnp.float32)
        for m in range(modes):
            j = g * modes + m
            change_re = change[j * length : (j + 1) * length, :length]
            change_im = change[j * length : (j + 1) * length, length:]
            probe_re = probe_ref[m, 0]
            probe_im = probe_ref[m, 1]
            update_re = update_re + (probe_re * change_re + probe_im * change_im)
            update_im = update_im + (probe_re * change_im - probe_im * change_re)
            grad_re = patch_re * change_re + patch_im * change_im
            grad_im = patch_re * change_im - patch_im * change_re
            if g == 0:
                grads[m] = [grad_re, grad_im]
            else:
                grads[m] = [grads[m][0] + grad_re, grads[m][1] + grad_im]
        update_ref[0, slot] = update_re.astype(update_ref.dtype)
        update_ref[1, slot] = update_im.astype(update_ref.dtype)
    for m in range(modes):
        grad_ref[m, 0] += grads[m][0]
        grad_ref[m, 1] += grads[m][1]


def entries_kernel(order, patch, amp_in, probe_now, left, right):
    slots, length = amp_in.shape[0], amp_in.shape[-1]
    modes = probe_now.shape[0]
    flops = slots * 4 * 2 * (2 * length) * (2 * length) * (modes * length)
    whole = pl.BlockSpec(memory_space=pltpu.VMEM)
    grid_spec = pltpu.PrefetchScalarGridSpec(
        num_scalar_prefetch=1,
        grid=(1,),
        in_specs=[whole] * 5,
        out_specs=[whole] * 2,
    )
    return pl.pallas_call(
        entry_kernel,
        grid_spec=grid_spec,
        out_shape=[
            jax.ShapeDtypeStruct((2, slots, length, length), jnp.bfloat16),
            jax.ShapeDtypeStruct(probe_now.shape, jnp.float32),
        ],
        compiler_params=pltpu.CompilerParams(dimension_semantics=("arbitrary",)),
        cost_estimate=pl.CostEstimate(
            flops=flops,
            transcendentals=slots * length * length,
            bytes_accessed=slots * length * length * 10 + probe_now.size * 8,
        ),
    )(order, patch, amp_in, probe_now, left, right)


def route(amplitudes, batch_ids, scan_tile, scan_offset, tiles_here):
    tile_count = lax.axis_size("tile")
    steps, batch_rows = batch_ids.shape
    capacity = max(2, 2 * batch_rows // tile_count)
    slots = tile_count * capacity
    length = amplitudes.shape[-1]
    target = scan_tile[:, :, 0]
    owner = target // tiles_here
    local_tile = target - owner * tiles_here
    onehot = (owner[:, :, None] == jnp.arange(tile_count, dtype=jnp.int32)).astype(jnp.int32)
    place_in = jnp.sum((jnp.cumsum(onehot, axis=1) - 1) * onehot, axis=2)
    slot_of = owner * capacity + place_in
    chosen = (slot_of[:, None, :] == jnp.arange(slots, dtype=jnp.int32)[None, :, None]).astype(
        jnp.int32
    )
    fields = jnp.stack(
        [local_tile, scan_offset[:, :, 0], scan_offset[:, :, 1], jnp.ones_like(local_tile)], axis=2
    )
    meta = jnp.sum(chosen[:, :, :, None] * fields[:, None, :, :], axis=2).astype(jnp.bfloat16)
    meta = jnp.pad(meta[:, :, None, :], ((0, 0), (0, 0), (0, 7), (0, length - 4)))
    ids = jnp.sum(chosen * batch_ids[:, None, :], axis=2)
    amp_send = amplitudes[ids.reshape(-1)].reshape(steps, slots, length, length)
    payload = jnp.concatenate([amp_send, meta], axis=2)
    return payload.reshape(steps, tile_count, capacity, length + 8, length)


def unpack(arrived, size):
    tile_count, capacity, rows, length = arrived.shape
    arrived = arrived.reshape(tile_count * capacity, rows, length)
    meta = arrived[:, length, :4].astype(jnp.int32)
    meta_in = jnp.stack([meta[:, 0] * size + meta[:, 1], meta[:, 2], meta[:, 3]], axis=1)
    return arrived, meta_in


def group_size(axes):
    count = 1
    for axis in axes:
        count *= lax.axis_size(axis)
    return count


def sum_over(value, axes, send_type):
    count = group_size(axes)
    parts = lax.all_to_all(value.astype(send_type).reshape(count, -1), axes, 0, 0, tiled=True)
    total = jnp.sum(parts.astype(jnp.float32), axis=0, keepdims=True).astype(send_type)
    return total, count


def all_sum_a2a(value, axes):
    total, count = sum_over(value, axes, value.dtype)
    spread = lax.all_to_all(jnp.broadcast_to(total, (count, total.shape[1])), axes, 0, 0, tiled=True)
    return spread.reshape(value.shape)


def all_sum_pairs(value, axis, send_type):
    count = lax.axis_size(axis)
    if count & (count - 1):
        return lax.psum(value.astype(send_type), axis).astype(jnp.float32)
    total = value.astype(send_type).astype(jnp.float32)
    step = 1
    while step < count:
        pairs = [(i, i ^ step) for i in range(count)]
        other = lax.ppermute(total.astype(send_type), axis, pairs)
        total = total.astype(send_type).astype(jnp.float32) + other.astype(jnp.float32)
        step *= 2
    return total


def entries_pass(stacked, probe_now, amp_in, meta_in, tables):
    table_re, table_im, table_neg = tables
    length = probe_now.shape[-1]
    rows_all, size = stacked.shape[1], stacked.shape[2]
    within = jnp.arange(length, dtype=jnp.int32)
    row_at, col_at, valid = meta_in[:, 0], meta_in[:, 1], meta_in[:, 2]
    pick_rows = (
        (row_at[:, None, None] + within[None, :, None])
        == jnp.arange(rows_all, dtype=jnp.int32)[None, None, :]
    ) & (valid[:, None, None] > 0)
    pick_rows = pick_rows.astype(jnp.bfloat16)
    pick_cols = (
        (col_at[:, None, None] + within[None, None, :])
        == jnp.arange(size, dtype=jnp.int32)[None, :, None]
    ).astype(jnp.bfloat16)
    rows = jnp.einsum(
        "skq,xqc->xskc", pick_rows, stacked, preferred_element_type=jnp.float32
    ).astype(jnp.bfloat16)
    patch = jnp.einsum("xskc,scl->xskl", rows, pick_cols, preferred_element_type=jnp.float32)
    left, right = block_tables(tables[0], tables[1])
    held = (valid > 0).astype(jnp.int32)
    count = jnp.sum(held)
    place = jnp.where(held > 0, jnp.cumsum(held) - 1, count + jnp.cumsum(1 - held) - 1)
    slots = valid.shape[0]
    order = jnp.sum(
        (place[:, None] == jnp.arange(slots, dtype=jnp.int32)[None, :])
        * jnp.arange(slots, dtype=jnp.int32)[:, None],
        axis=0,
    )
    order = jnp.concatenate([order, count[None]]).astype(jnp.int32)
    update, probe_grad = entries_kernel(
        order, patch.astype(jnp.bfloat16), amp_in, probe_now, left, right
    )
    spread = jnp.einsum(
        "xskl,scl->xskc", update, pick_cols, preferred_element_type=jnp.float32
    ).astype(jnp.bfloat16)
    local_sum = jnp.einsum("skq,xskc->xqc", pick_rows, spread, preferred_element_type=jnp.float32)
    return local_sum, probe_grad


def one_step(tiles_now, probe_now, amp_in, meta_in, tables, batch_total):
    tiles_here, size = tiles_now.shape[1], tiles_now.shape[2]
    slots, length = amp_in.shape[0], amp_in.shape[-1]
    stacked = tiles_now.astype(jnp.bfloat16).reshape(2, tiles_here * size, size)
    chunk = max(d for d in range(1, min(slots, 24) + 1) if slots % d == 0)
    if chunk == slots:
        local_sum, probe_grad = entries_pass(stacked, probe_now, amp_in, meta_in, tables)
    else:

        def body(carry, piece):
            part_sum, part_grad = entries_pass(stacked, probe_now, piece[0], piece[1], tables)
            return (carry[0] + part_sum, carry[1] + part_grad), None

        start = (jnp.zeros(stacked.shape, jnp.float32), jnp.zeros(probe_now.shape, jnp.float32))
        pieces = (
            amp_in.reshape(slots // chunk, chunk, length + 8, length),
            meta_in.reshape(slots // chunk, chunk, 3),
        )
        (local_sum, probe_grad), _ = lax.scan(body, start, pieces)
    local_sum = local_sum.reshape(tiles_now.shape)
    probe_re = probe_now[:, 0]
    probe_im = probe_now[:, 1]
    peak_power = jnp.max(jnp.sum(probe_re * probe_re + probe_im * probe_im, axis=0))
    summed = all_sum_pairs(local_sum, "pat", jnp.bfloat16)
    tiles_next = tiles_now + summed / peak_power
    grad_sum = all_sum_a2a(probe_grad, ("tile", "pat"))
    probe_next = probe_now + probe_rate * grad_sum / batch_total
    return (tiles_next, probe_next, probe_grad)


def on_device(amplitudes, batch_ids, scan_tile, scan_offset, object_tiles, probe):
    tables = dft_tables(probe.shape[-1])
    tiles_here, size = object_tiles.shape[1], object_tiles.shape[2]
    batch_total = batch_ids.shape[1] * lax.axis_size("tile") * lax.axis_size("pat")
    payload = route(amplitudes, batch_ids, scan_tile, scan_offset, tiles_here)
    tiles_now = object_tiles
    probe_now = probe
    arrived = lax.all_to_all(jnp.swapaxes(payload, 0, 1), "tile", 0, 0, tiled=True)
    for step_no in range(batch_ids.shape[0]):
        amp_in, meta_in = unpack(arrived[:, step_no], size)
        tiles_now, probe_now, _ = one_step(tiles_now, probe_now, amp_in, meta_in, tables, batch_total)
    return (tiles_now, probe_now)


def solution(mesh):
    in_specs = (
        P(("tile", "pat"), None, None),
        P(None, ("tile", "pat")),
        P(None, ("tile", "pat"), None),
        P(None, ("tile", "pat"), None),
        P(None, "tile", None, None),
        P(),
    )
    out_specs = (P(None, "tile", None, None), P())
    return jax.shard_map(
        on_device, mesh=mesh, in_specs=in_specs, out_specs=out_specs, check_vma=False
    )
```

```python
import math

import jax
import jax.numpy as jnp
from jax import lax
from jax.experimental import pallas as pl
from jax.experimental.pallas import tpu as pltpu
from jax.sharding import PartitionSpec as P

probe_rate = 8.0


def dft_tables(length):
    counter = jnp.arange(length, dtype=jnp.int32)
    product = counter[:, None] * counter[None, :] % length
    angle_table = 2.0 * math.pi / length * product.astype(jnp.float32)
    norm_factor = 1.0 / math.sqrt(length)
    table_re = (jnp.cos(angle_table) * norm_factor).astype(jnp.bfloat16)
    table_im = (-jnp.sin(angle_table) * norm_factor).astype(jnp.bfloat16)
    return (table_re, table_im, -table_im)


def transform(src_re, src_im, table_re, table_im):
    half_re = jnp.einsum(
        "kj,bmjc->bmkc", table_re, src_re, preferred_element_type=jnp.float32
    ) - jnp.einsum("kj,bmjc->bmkc", table_im, src_im, preferred_element_type=jnp.float32)
    half_im = jnp.einsum(
        "kj,bmjc->bmkc", table_re, src_im, preferred_element_type=jnp.float32
    ) + jnp.einsum("kj,bmjc->bmkc", table_im, src_re, preferred_element_type=jnp.float32)
    half_re = half_re.astype(jnp.bfloat16)
    half_im = half_im.astype(jnp.bfloat16)
    out_re = jnp.einsum(
        "bmkc,cl->bmkl", half_re, table_re, preferred_element_type=jnp.float32
    ) - jnp.einsum("bmkc,cl->bmkl", half_im, table_im, preferred_element_type=jnp.float32)
    out_im = jnp.einsum(
        "bmkc,cl->bmkl", half_re, table_im, preferred_element_type=jnp.float32
    ) + jnp.einsum("bmkc,cl->bmkl", half_im, table_re, preferred_element_type=jnp.float32)
    return (out_re, out_im)


def block_tables(table_re, table_im):
    left = jnp.concatenate(
        [jnp.concatenate([table_re, -table_im], 1), jnp.concatenate([table_im, table_re], 1)], 0
    )
    right = jnp.concatenate(
        [jnp.concatenate([table_re, table_im], 1), jnp.concatenate([-table_im, table_re], 1)], 0
    )
    return left, right


def entry_kernel(order_ref, patch_ref, amp_ref, probe_ref, left_ref, right_ref, update_ref, grad_ref):
    slots = order_ref.shape[0] - 1
    count = order_ref[slots]
    group = next(size for size in (8, 4, 2, 1) if slots % size == 0)
    grad_ref[...] = jnp.zeros(grad_ref.shape, grad_ref.dtype)
    update_ref[...] = jnp.zeros(update_ref.shape, update_ref.dtype)

    def one_group(index, carry):
        chosen = [order_ref[index * group + g] for g in range(group)]
        entry_body(chosen, patch_ref, amp_ref, probe_ref, left_ref, right_ref, update_ref, grad_ref)
        return carry

    lax.fori_loop(0, (count + group - 1) // group, one_group, 0)


def entry_body(chosen, patch_ref, amp_ref, probe_ref, left_ref, right_ref, update_ref, grad_ref):
    modes, length = probe_ref.shape[0], probe_ref.shape[-1]
    blocks = len(chosen) * modes
    patches = [
        (patch_ref[0, slot].astype(jnp.float32), patch_ref[1, slot].astype(jnp.float32))
        for slot in chosen
    ]
    left = left_ref[...]
    right = right_ref[...]
    exits_re, exits_im = [], []
    for patch_re, patch_im in patches:
        for m in range(modes):
            probe_re = probe_ref[m, 0]
            probe_im = probe_ref[m, 1]
            exits_re.append((probe_re * patch_re - probe_im * patch_im).astype(jnp.bfloat16))
            exits_im.append((probe_re * patch_im + probe_im * patch_re).astype(jnp.bfloat16))
    stacked = jnp.concatenate(
        [jnp.concatenate(exits_re, 1), jnp.concatenate(exits_im, 1)], 0
    )
    half = jnp.dot(left, stacked, preferred_element_type=jnp.float32).astype(jnp.bfloat16)

    def by_mode(wide):
        return jnp.concatenate(
            [
                jnp.concatenate(
                    [
                        wide[:length, j * length : (j + 1) * length],
                        wide[length:, j * length : (j + 1) * length],
                    ],
                    1,
                )
                for j in range(blocks)
            ],
            0,
        )

    def by_part(tall):
        return jnp.concatenate(
            [
                jnp.concatenate(
                    [tall[j * length : (j + 1) * length, :length] for j in range(blocks)], 1
                ),
                jnp.concatenate(
                    [tall[j * length : (j + 1) * length, length:] for j in range(blocks)], 1
                ),
            ],
            0,
        )

    far = jnp.dot(by_mode(half), right, preferred_element_type=jnp.float32)
    factors = []
    for g, slot in enumerate(chosen):
        intensity = jnp.zeros((length, length), jnp.float32)
        for m in range(modes):
            j = g * modes + m
            far_re = far[j * length : (j + 1) * length, :length]
            far_im = far[j * length : (j + 1) * length, length:]
            intensity = intensity + (far_re * far_re + far_im * far_im)
        measured = amp_ref[slot, :length, :].astype(jnp.float32)
        factor = measured / jnp.sqrt(jnp.maximum(intensity, 1.0)) - 1.0
        factors.extend([jnp.concatenate([factor, factor], 1)] * modes)
    scaled = (jnp.concatenate(factors, 0) * far).astype(jnp.bfloat16)
    back = jnp.dot(right, by_part(scaled), preferred_element_type=jnp.float32).astype(
        jnp.bfloat16
    )
    change = jnp.dot(by_mode(back), left, preferred_element_type=jnp.float32)
    grads = [[None, None] for _ in range(modes)]
    for g, slot in enumerate(chosen):
        patch_re, patch_im = patches[g]
        update_re = jnp.zeros((length, length), jnp.float32)
        update_im = jnp.zeros((length, length), jnp.float32)
        for m in range(modes):
            j = g * modes + m
            change_re = change[j * length : (j + 1) * length, :length]
            change_im = change[j * length : (j + 1) * length, length:]
            probe_re = probe_ref[m, 0]
            probe_im = probe_ref[m, 1]
            update_re = update_re + (probe_re * change_re + probe_im * change_im)
            update_im = update_im + (probe_re * change_im - probe_im * change_re)
            grad_re = patch_re * change_re + patch_im * change_im
            grad_im = patch_re * change_im - patch_im * change_re
            if g == 0:
                grads[m] = [grad_re, grad_im]
            else:
                grads[m] = [grads[m][0] + grad_re, grads[m][1] + grad_im]
        update_ref[0, slot] = update_re.astype(update_ref.dtype)
        update_ref[1, slot] = update_im.astype(update_ref.dtype)
    for m in range(modes):
        grad_ref[m, 0] += grads[m][0]
        grad_ref[m, 1] += grads[m][1]


def entries_kernel(order, patch, amp_in, probe_now, left, right):
    slots, length = amp_in.shape[0], amp_in.shape[-1]
    modes = probe_now.shape[0]
    flops = slots * 4 * 2 * (2 * length) * (2 * length) * (modes * length)
    whole = pl.BlockSpec(memory_space=pltpu.VMEM)
    grid_spec = pltpu.PrefetchScalarGridSpec(
        num_scalar_prefetch=1,
        grid=(1,),
        in_specs=[whole] * 5,
        out_specs=[whole] * 2,
    )
    return pl.pallas_call(
        entry_kernel,
        grid_spec=grid_spec,
        out_shape=[
            jax.ShapeDtypeStruct((2, slots, length, length), jnp.bfloat16),
            jax.ShapeDtypeStruct(probe_now.shape, jnp.float32),
        ],
        compiler_params=pltpu.CompilerParams(dimension_semantics=("arbitrary",)),
        cost_estimate=pl.CostEstimate(
            flops=flops,
            transcendentals=slots * length * length,
            bytes_accessed=slots * length * length * 10 + probe_now.size * 8,
        ),
    )(order, patch, amp_in, probe_now, left, right)


def route(amplitudes, batch_ids, scan_tile, scan_offset, tiles_here):
    tile_count = lax.axis_size("tile")
    steps, batch_rows = batch_ids.shape
    capacity = max(2, 2 * batch_rows // tile_count)
    slots = tile_count * capacity
    length = amplitudes.shape[-1]
    target = scan_tile[:, :, 0]
    owner = target // tiles_here
    local_tile = target - owner * tiles_here
    onehot = (owner[:, :, None] == jnp.arange(tile_count, dtype=jnp.int32)).astype(jnp.int32)
    place_in = jnp.sum((jnp.cumsum(onehot, axis=1) - 1) * onehot, axis=2)
    slot_of = owner * capacity + place_in
    chosen = (slot_of[:, None, :] == jnp.arange(slots, dtype=jnp.int32)[None, :, None]).astype(
        jnp.int32
    )
    fields = jnp.stack(
        [local_tile, scan_offset[:, :, 0], scan_offset[:, :, 1], jnp.ones_like(local_tile)], axis=2
    )
    meta = jnp.sum(chosen[:, :, :, None] * fields[:, None, :, :], axis=2).astype(jnp.bfloat16)
    meta = jnp.pad(meta[:, :, None, :], ((0, 0), (0, 0), (0, 7), (0, length - 4)))
    ids = jnp.sum(chosen * batch_ids[:, None, :], axis=2)
    amp_send = amplitudes[ids.reshape(-1)].reshape(steps, slots, length, length)
    payload = jnp.concatenate([amp_send, meta], axis=2)
    return payload.reshape(steps, tile_count, capacity, length + 8, length)


def unpack(arrived, size):
    tile_count, capacity, rows, length = arrived.shape
    arrived = arrived.reshape(tile_count * capacity, rows, length)
    meta = arrived[:, length, :4].astype(jnp.int32)
    meta_in = jnp.stack([meta[:, 0] * size + meta[:, 1], meta[:, 2], meta[:, 3]], axis=1)
    return arrived, meta_in


def group_size(axes):
    count = 1
    for axis in axes:
        count *= lax.axis_size(axis)
    return count


def sum_over(value, axes, send_type):
    count = group_size(axes)
    parts = lax.all_to_all(value.astype(send_type).reshape(count, -1), axes, 0, 0, tiled=True)
    total = jnp.sum(parts.astype(jnp.float32), axis=0, keepdims=True).astype(send_type)
    return total, count


def all_sum_a2a(value, axes):
    total, count = sum_over(value, axes, value.dtype)
    spread = lax.all_to_all(jnp.broadcast_to(total, (count, total.shape[1])), axes, 0, 0, tiled=True)
    return spread.reshape(value.shape)


def all_sum_pairs(value, axis, send_type):
    count = lax.axis_size(axis)
    if count & (count - 1):
        return lax.psum(value.astype(send_type), axis).astype(jnp.float32)
    total = value.astype(send_type).astype(jnp.float32)
    step = 1
    while step < count:
        pairs = [(i, i ^ step) for i in range(count)]
        other = lax.ppermute(total.astype(send_type), axis, pairs)
        total = total.astype(send_type).astype(jnp.float32) + other.astype(jnp.float32)
        step *= 2
    return total


def entries_pass(stacked, probe_now, amp_in, meta_in, tables):
    table_re, table_im, table_neg = tables
    length = probe_now.shape[-1]
    rows_all, size = stacked.shape[1], stacked.shape[2]
    within = jnp.arange(length, dtype=jnp.int32)
    row_at, col_at, valid = meta_in[:, 0], meta_in[:, 1], meta_in[:, 2]
    pick_rows = (
        (row_at[:, None, None] + within[None, :, None])
        == jnp.arange(rows_all, dtype=jnp.int32)[None, None, :]
    ) & (valid[:, None, None] > 0)
    pick_rows = pick_rows.astype(jnp.bfloat16)
    pick_cols = (
        (col_at[:, None, None] + within[None, None, :])
        == jnp.arange(size, dtype=jnp.int32)[None, :, None]
    ).astype(jnp.bfloat16)
    rows = jnp.einsum(
        "skq,xqc->xskc", pick_rows, stacked, preferred_element_type=jnp.float32
    ).astype(jnp.bfloat16)
    patch = jnp.einsum("xskc,scl->xskl", rows, pick_cols, preferred_element_type=jnp.float32)
    left, right = block_tables(tables[0], tables[1])
    held = (valid > 0).astype(jnp.int32)
    count = jnp.sum(held)
    place = jnp.where(held > 0, jnp.cumsum(held) - 1, count + jnp.cumsum(1 - held) - 1)
    slots = valid.shape[0]
    order = jnp.sum(
        (place[:, None] == jnp.arange(slots, dtype=jnp.int32)[None, :])
        * jnp.arange(slots, dtype=jnp.int32)[:, None],
        axis=0,
    )
    order = jnp.concatenate([order, count[None]]).astype(jnp.int32)
    update, probe_grad = entries_kernel(
        order, patch.astype(jnp.bfloat16), amp_in, probe_now, left, right
    )
    spread = jnp.einsum(
        "xskl,scl->xskc", update, pick_cols, preferred_element_type=jnp.float32
    ).astype(jnp.bfloat16)
    local_sum = jnp.einsum("skq,xskc->xqc", pick_rows, spread, preferred_element_type=jnp.float32)
    return local_sum, probe_grad


def one_step(tiles_now, probe_now, amp_in, meta_in, tables, batch_total):
    tiles_here, size = tiles_now.shape[1], tiles_now.shape[2]
    slots, length = amp_in.shape[0], amp_in.shape[-1]
    stacked = tiles_now.astype(jnp.bfloat16).reshape(2, tiles_here * size, size)
    chunk = max(d for d in range(1, min(slots, 24) + 1) if slots % d == 0)
    if chunk == slots:
        local_sum, probe_grad = entries_pass(stacked, probe_now, amp_in, meta_in, tables)
    else:

        def body(carry, piece):
            part_sum, part_grad = entries_pass(stacked, probe_now, piece[0], piece[1], tables)
            return (carry[0] + part_sum, carry[1] + part_grad), None

        start = (jnp.zeros(stacked.shape, jnp.float32), jnp.zeros(probe_now.shape, jnp.float32))
        pieces = (
            amp_in.reshape(slots // chunk, chunk, length + 8, length),
            meta_in.reshape(slots // chunk, chunk, 3),
        )
        (local_sum, probe_grad), _ = lax.scan(body, start, pieces)
    local_sum = local_sum.reshape(tiles_now.shape)
    probe_re = probe_now[:, 0]
    probe_im = probe_now[:, 1]
    peak_power = jnp.max(jnp.sum(probe_re * probe_re + probe_im * probe_im, axis=0))
    summed = all_sum_pairs(local_sum, "pat", jnp.bfloat16)
    tiles_next = tiles_now + summed / peak_power
    grad_sum = all_sum_a2a(probe_grad, ("tile", "pat"))
    probe_next = probe_now + probe_rate * grad_sum / batch_total
    return (tiles_next, probe_next, probe_grad)


def on_device(amplitudes, batch_ids, scan_tile, scan_offset, object_tiles, probe):
    tables = dft_tables(probe.shape[-1])
    tiles_here, size = object_tiles.shape[1], object_tiles.shape[2]
    batch_total = batch_ids.shape[1] * lax.axis_size("tile") * lax.axis_size("pat")
    payload = route(amplitudes, batch_ids, scan_tile, scan_offset, tiles_here)
    tiles_now = object_tiles
    probe_now = probe
    arrived = lax.all_to_all(jnp.swapaxes(payload, 0, 1), "tile", 0, 0, tiled=True)
    for step_no in range(batch_ids.shape[0]):
        amp_in, meta_in = unpack(arrived[:, step_no], size)
        tiles_now, probe_now, _ = one_step(tiles_now, probe_now, amp_in, meta_in, tables, batch_total)
    return (tiles_now, probe_now)


def solution(mesh):
    in_specs = (
        P(("tile", "pat"), None, None),
        P(None, ("tile", "pat")),
        P(None, ("tile", "pat"), None),
        P(None, ("tile", "pat"), None),
        P(None, "tile", None, None),
        P(),
    )
    out_specs = (P(None, "tile", None, None), P())
    return jax.shard_map(
        on_device, mesh=mesh, in_specs=in_specs, out_specs=out_specs, check_vma=False
    )
```

```python
import math

import jax
import jax.numpy as jnp
from jax import lax
from jax.experimental import pallas as pl
from jax.experimental.pallas import tpu as pltpu
from jax.sharding import PartitionSpec as P

probe_rate = 8.0


def dft_tables(length):
    counter = jnp.arange(length, dtype=jnp.int32)
    product = counter[:, None] * counter[None, :] % length
    angle_table = 2.0 * math.pi / length * product.astype(jnp.float32)
    norm_factor = 1.0 / math.sqrt(length)
    table_re = (jnp.cos(angle_table) * norm_factor).astype(jnp.bfloat16)
    table_im = (-jnp.sin(angle_table) * norm_factor).astype(jnp.bfloat16)
    return (table_re, table_im, -table_im)


def transform(src_re, src_im, table_re, table_im):
    half_re = jnp.einsum(
        "kj,bmjc->bmkc", table_re, src_re, preferred_element_type=jnp.float32
    ) - jnp.einsum("kj,bmjc->bmkc", table_im, src_im, preferred_element_type=jnp.float32)
    half_im = jnp.einsum(
        "kj,bmjc->bmkc", table_re, src_im, preferred_element_type=jnp.float32
    ) + jnp.einsum("kj,bmjc->bmkc", table_im, src_re, preferred_element_type=jnp.float32)
    half_re = half_re.astype(jnp.bfloat16)
    half_im = half_im.astype(jnp.bfloat16)
    out_re = jnp.einsum(
        "bmkc,cl->bmkl", half_re, table_re, preferred_element_type=jnp.float32
    ) - jnp.einsum("bmkc,cl->bmkl", half_im, table_im, preferred_element_type=jnp.float32)
    out_im = jnp.einsum(
        "bmkc,cl->bmkl", half_re, table_im, preferred_element_type=jnp.float32
    ) + jnp.einsum("bmkc,cl->bmkl", half_im, table_re, preferred_element_type=jnp.float32)
    return (out_re, out_im)


def block_tables(table_re, table_im):
    left = jnp.concatenate(
        [jnp.concatenate([table_re, -table_im], 1), jnp.concatenate([table_im, table_re], 1)], 0
    )
    right = jnp.concatenate(
        [jnp.concatenate([table_re, table_im], 1), jnp.concatenate([-table_im, table_re], 1)], 0
    )
    return left, right


def entry_kernel(order_ref, patch_ref, amp_ref, probe_ref, left_ref, right_ref, update_ref, grad_ref):
    slots = order_ref.shape[0] - 1
    count = order_ref[slots]
    group = next(size for size in (4, 2, 1) if slots % size == 0)
    grad_ref[...] = jnp.zeros(grad_ref.shape, grad_ref.dtype)
    update_ref[...] = jnp.zeros(update_ref.shape, update_ref.dtype)

    def one_group(index, carry):
        chosen = [order_ref[index * group + g] for g in range(group)]
        entry_body(chosen, patch_ref, amp_ref, probe_ref, left_ref, right_ref, update_ref, grad_ref)
        return carry

    lax.fori_loop(0, (count + group - 1) // group, one_group, 0)


def entry_body(chosen, patch_ref, amp_ref, probe_ref, left_ref, right_ref, update_ref, grad_ref):
    modes, length = probe_ref.shape[0], probe_ref.shape[-1]
    blocks = len(chosen) * modes
    patches = [
        (patch_ref[0, slot].astype(jnp.float32), patch_ref[1, slot].astype(jnp.float32))
        for slot in chosen
    ]
    left = left_ref[...]
    right = right_ref[...]
    exits_re, exits_im = [], []
    for patch_re, patch_im in patches:
        for m in range(modes):
            probe_re = probe_ref[m, 0]
            probe_im = probe_ref[m, 1]
            exits_re.append((probe_re * patch_re - probe_im * patch_im).astype(jnp.bfloat16))
            exits_im.append((probe_re * patch_im + probe_im * patch_re).astype(jnp.bfloat16))
    stacked = jnp.concatenate(
        [jnp.concatenate(exits_re, 1), jnp.concatenate(exits_im, 1)], 0
    )
    half = jnp.dot(left, stacked, preferred_element_type=jnp.float32).astype(jnp.bfloat16)

    def by_mode(wide):
        return jnp.concatenate(
            [
                jnp.concatenate(
                    [
                        wide[:length, j * length : (j + 1) * length],
                        wide[length:, j * length : (j + 1) * length],
                    ],
                    1,
                )
                for j in range(blocks)
            ],
            0,
        )

    def by_part(tall):
        return jnp.concatenate(
            [
                jnp.concatenate(
                    [tall[j * length : (j + 1) * length, :length] for j in range(blocks)], 1
                ),
                jnp.concatenate(
                    [tall[j * length : (j + 1) * length, length:] for j in range(blocks)], 1
                ),
            ],
            0,
        )

    far = jnp.dot(by_mode(half), right, preferred_element_type=jnp.float32)
    factors = []
    for g, slot in enumerate(chosen):
        intensity = jnp.zeros((length, length), jnp.float32)
        for m in range(modes):
            j = g * modes + m
            far_re = far[j * length : (j + 1) * length, :length]
            far_im = far[j * length : (j + 1) * length, length:]
            intensity = intensity + (far_re * far_re + far_im * far_im)
        measured = amp_ref[slot, :length, :].astype(jnp.float32)
        factor = measured / jnp.sqrt(jnp.maximum(intensity, 1.0)) - 1.0
        factors.extend([jnp.concatenate([factor, factor], 1)] * modes)
    scaled = (jnp.concatenate(factors, 0) * far).astype(jnp.bfloat16)
    back = jnp.dot(right, by_part(scaled), preferred_element_type=jnp.float32).astype(
        jnp.bfloat16
    )
    change = jnp.dot(by_mode(back), left, preferred_element_type=jnp.float32)
    grads = [[None, None] for _ in range(modes)]
    for g, slot in enumerate(chosen):
        patch_re, patch_im = patches[g]
        update_re = jnp.zeros((length, length), jnp.float32)
        update_im = jnp.zeros((length, length), jnp.float32)
        for m in range(modes):
            j = g * modes + m
            change_re = change[j * length : (j + 1) * length, :length]
            change_im = change[j * length : (j + 1) * length, length:]
            probe_re = probe_ref[m, 0]
            probe_im = probe_ref[m, 1]
            update_re = update_re + (probe_re * change_re + probe_im * change_im)
            update_im = update_im + (probe_re * change_im - probe_im * change_re)
            grad_re = patch_re * change_re + patch_im * change_im
            grad_im = patch_re * change_im - patch_im * change_re
            if g == 0:
                grads[m] = [grad_re, grad_im]
            else:
                grads[m] = [grads[m][0] + grad_re, grads[m][1] + grad_im]
        update_ref[0, slot] = update_re.astype(update_ref.dtype)
        update_ref[1, slot] = update_im.astype(update_ref.dtype)
    for m in range(modes):
        grad_ref[m, 0] += grads[m][0]
        grad_ref[m, 1] += grads[m][1]


def entries_kernel(order, patch, amp_in, probe_now, left, right):
    slots, length = amp_in.shape[0], amp_in.shape[-1]
    modes = probe_now.shape[0]
    flops = slots * 4 * 2 * (2 * length) * (2 * length) * (modes * length)
    whole = pl.BlockSpec(memory_space=pltpu.VMEM)
    grid_spec = pltpu.PrefetchScalarGridSpec(
        num_scalar_prefetch=1,
        grid=(1,),
        in_specs=[whole] * 5,
        out_specs=[whole] * 2,
    )
    return pl.pallas_call(
        entry_kernel,
        grid_spec=grid_spec,
        out_shape=[
            jax.ShapeDtypeStruct((2, slots, length, length), jnp.bfloat16),
            jax.ShapeDtypeStruct(probe_now.shape, jnp.float32),
        ],
        compiler_params=pltpu.CompilerParams(dimension_semantics=("arbitrary",)),
        cost_estimate=pl.CostEstimate(
            flops=flops,
            transcendentals=slots * length * length,
            bytes_accessed=slots * length * length * 10 + probe_now.size * 8,
        ),
    )(order, patch, amp_in, probe_now, left, right)


def route(amplitudes, batch_ids, scan_tile, scan_offset, tiles_here):
    tile_count = lax.axis_size("tile")
    steps, batch_rows = batch_ids.shape
    capacity = max(2, 2 * batch_rows // tile_count)
    slots = tile_count * capacity
    length = amplitudes.shape[-1]
    target = scan_tile[:, :, 0]
    owner = target // tiles_here
    local_tile = target - owner * tiles_here
    onehot = (owner[:, :, None] == jnp.arange(tile_count, dtype=jnp.int32)).astype(jnp.int32)
    place_in = jnp.sum((jnp.cumsum(onehot, axis=1) - 1) * onehot, axis=2)
    slot_of = owner * capacity + place_in
    chosen = (slot_of[:, None, :] == jnp.arange(slots, dtype=jnp.int32)[None, :, None]).astype(
        jnp.int32
    )
    fields = jnp.stack(
        [local_tile, scan_offset[:, :, 0], scan_offset[:, :, 1], jnp.ones_like(local_tile)], axis=2
    )
    meta = jnp.sum(chosen[:, :, :, None] * fields[:, None, :, :], axis=2).astype(jnp.bfloat16)
    meta = jnp.pad(meta[:, :, None, :], ((0, 0), (0, 0), (0, 7), (0, length - 4)))
    ids = jnp.sum(chosen * batch_ids[:, None, :], axis=2)
    amp_send = amplitudes[ids.reshape(-1)].reshape(steps, slots, length, length)
    payload = jnp.concatenate([amp_send, meta], axis=2)
    return payload.reshape(steps, tile_count, capacity, length + 8, length)


def unpack(arrived, size):
    tile_count, capacity, rows, length = arrived.shape
    arrived = arrived.reshape(tile_count * capacity, rows, length)
    meta = arrived[:, length, :4].astype(jnp.int32)
    meta_in = jnp.stack([meta[:, 0] * size + meta[:, 1], meta[:, 2], meta[:, 3]], axis=1)
    return arrived, meta_in


def group_size(axes):
    count = 1
    for axis in axes:
        count *= lax.axis_size(axis)
    return count


def sum_over(value, axes, send_type):
    count = group_size(axes)
    parts = lax.all_to_all(value.astype(send_type).reshape(count, -1), axes, 0, 0, tiled=True)
    total = jnp.sum(parts.astype(jnp.float32), axis=0, keepdims=True).astype(send_type)
    return total, count


def all_sum_a2a(value, axes):
    total, count = sum_over(value, axes, value.dtype)
    spread = lax.all_to_all(jnp.broadcast_to(total, (count, total.shape[1])), axes, 0, 0, tiled=True)
    return spread.reshape(value.shape)


def all_sum_pairs(value, axis, send_type):
    count = lax.axis_size(axis)
    if count & (count - 1):
        return lax.psum(value.astype(send_type), axis).astype(jnp.float32)
    total = value.astype(send_type).astype(jnp.float32)
    step = 1
    while step < count:
        pairs = [(i, i ^ step) for i in range(count)]
        other = lax.ppermute(total.astype(send_type), axis, pairs)
        total = total.astype(send_type).astype(jnp.float32) + other.astype(jnp.float32)
        step *= 2
    return total


def entries_pass(stacked, probe_now, amp_in, meta_in, tables):
    table_re, table_im, table_neg = tables
    length = probe_now.shape[-1]
    rows_all, size = stacked.shape[1], stacked.shape[2]
    within = jnp.arange(length, dtype=jnp.int32)
    row_at, col_at, valid = meta_in[:, 0], meta_in[:, 1], meta_in[:, 2]
    pick_rows = (
        (row_at[:, None, None] + within[None, :, None])
        == jnp.arange(rows_all, dtype=jnp.int32)[None, None, :]
    ) & (valid[:, None, None] > 0)
    pick_rows = pick_rows.astype(jnp.bfloat16)
    pick_cols = (
        (col_at[:, None, None] + within[None, None, :])
        == jnp.arange(size, dtype=jnp.int32)[None, :, None]
    ).astype(jnp.bfloat16)
    rows = jnp.einsum(
        "skq,xqc->xskc", pick_rows, stacked, preferred_element_type=jnp.float32
    ).astype(jnp.bfloat16)
    patch = jnp.einsum("xskc,scl->xskl", rows, pick_cols, preferred_element_type=jnp.float32)
    left, right = block_tables(tables[0], tables[1])
    held = (valid > 0).astype(jnp.int32)
    count = jnp.sum(held)
    place = jnp.where(held > 0, jnp.cumsum(held) - 1, count + jnp.cumsum(1 - held) - 1)
    slots = valid.shape[0]
    order = jnp.sum(
        (place[:, None] == jnp.arange(slots, dtype=jnp.int32)[None, :])
        * jnp.arange(slots, dtype=jnp.int32)[:, None],
        axis=0,
    )
    order = jnp.concatenate([order, count[None]]).astype(jnp.int32)
    update, probe_grad = entries_kernel(
        order, patch.astype(jnp.bfloat16), amp_in, probe_now, left, right
    )
    spread = jnp.einsum(
        "xskl,scl->xskc", update, pick_cols, preferred_element_type=jnp.float32
    ).astype(jnp.bfloat16)
    local_sum = jnp.stack(
        [
            jnp.dot(
                pick_rows.reshape(-1, pick_rows.shape[-1]).T,
                spread[x].reshape(-1, spread.shape[-1]),
                preferred_element_type=jnp.float32,
            )
            for x in range(2)
        ]
    )
    return local_sum, probe_grad


def one_step(tiles_now, probe_now, amp_in, meta_in, tables, batch_total):
    tiles_here, size = tiles_now.shape[1], tiles_now.shape[2]
    slots, length = amp_in.shape[0], amp_in.shape[-1]
    stacked = tiles_now.astype(jnp.bfloat16).reshape(2, tiles_here * size, size)
    chunk = max(d for d in range(1, min(slots, 24) + 1) if slots % d == 0)
    if chunk == slots:
        local_sum, probe_grad = entries_pass(stacked, probe_now, amp_in, meta_in, tables)
    else:

        def body(carry, piece):
            part_sum, part_grad = entries_pass(stacked, probe_now, piece[0], piece[1], tables)
            return (carry[0] + part_sum, carry[1] + part_grad), None

        start = (jnp.zeros(stacked.shape, jnp.float32), jnp.zeros(probe_now.shape, jnp.float32))
        pieces = (
            amp_in.reshape(slots // chunk, chunk, length + 8, length),
            meta_in.reshape(slots // chunk, chunk, 3),
        )
        (local_sum, probe_grad), _ = lax.scan(body, start, pieces)
    local_sum = local_sum.reshape(tiles_now.shape)
    probe_re = probe_now[:, 0]
    probe_im = probe_now[:, 1]
    peak_power = jnp.max(jnp.sum(probe_re * probe_re + probe_im * probe_im, axis=0))
    summed = all_sum_pairs(local_sum, "pat", jnp.bfloat16)
    tiles_next = tiles_now + summed / peak_power
    grad_sum = all_sum_a2a(probe_grad, ("tile", "pat"))
    probe_next = probe_now + probe_rate * grad_sum / batch_total
    return (tiles_next, probe_next, probe_grad)


def on_device(amplitudes, batch_ids, scan_tile, scan_offset, object_tiles, probe):
    tables = dft_tables(probe.shape[-1])
    tiles_here, size = object_tiles.shape[1], object_tiles.shape[2]
    batch_total = batch_ids.shape[1] * lax.axis_size("tile") * lax.axis_size("pat")
    payload = route(amplitudes, batch_ids, scan_tile, scan_offset, tiles_here)
    tiles_now = object_tiles
    probe_now = probe
    arrived = lax.all_to_all(jnp.swapaxes(payload, 0, 1), "tile", 0, 0, tiled=True)
    for step_no in range(batch_ids.shape[0]):
        amp_in, meta_in = unpack(arrived[:, step_no], size)
        tiles_now, probe_now, _ = one_step(tiles_now, probe_now, amp_in, meta_in, tables, batch_total)
    return (tiles_now, probe_now)


def solution(mesh):
    in_specs = (
        P(("tile", "pat"), None, None),
        P(None, ("tile", "pat")),
        P(None, ("tile", "pat"), None),
        P(None, ("tile", "pat"), None),
        P(None, "tile", None, None),
        P(),
    )
    out_specs = (P(None, "tile", None, None), P())
    return jax.shard_map(
        on_device, mesh=mesh, in_specs=in_specs, out_specs=out_specs, check_vma=False
    )
```

```python
import math

import jax
import jax.numpy as jnp
from jax import lax
from jax.experimental import pallas as pl
from jax.experimental.pallas import tpu as pltpu
from jax.sharding import PartitionSpec as P

probe_rate = 8.0


def dft_tables(length):
    counter = jnp.arange(length, dtype=jnp.int32)
    product = counter[:, None] * counter[None, :] % length
    angle_table = 2.0 * math.pi / length * product.astype(jnp.float32)
    norm_factor = 1.0 / math.sqrt(length)
    table_re = (jnp.cos(angle_table) * norm_factor).astype(jnp.bfloat16)
    table_im = (-jnp.sin(angle_table) * norm_factor).astype(jnp.bfloat16)
    return (table_re, table_im, -table_im)


def transform(src_re, src_im, table_re, table_im):
    half_re = jnp.einsum(
        "kj,bmjc->bmkc", table_re, src_re, preferred_element_type=jnp.float32
    ) - jnp.einsum("kj,bmjc->bmkc", table_im, src_im, preferred_element_type=jnp.float32)
    half_im = jnp.einsum(
        "kj,bmjc->bmkc", table_re, src_im, preferred_element_type=jnp.float32
    ) + jnp.einsum("kj,bmjc->bmkc", table_im, src_re, preferred_element_type=jnp.float32)
    half_re = half_re.astype(jnp.bfloat16)
    half_im = half_im.astype(jnp.bfloat16)
    out_re = jnp.einsum(
        "bmkc,cl->bmkl", half_re, table_re, preferred_element_type=jnp.float32
    ) - jnp.einsum("bmkc,cl->bmkl", half_im, table_im, preferred_element_type=jnp.float32)
    out_im = jnp.einsum(
        "bmkc,cl->bmkl", half_re, table_im, preferred_element_type=jnp.float32
    ) + jnp.einsum("bmkc,cl->bmkl", half_im, table_re, preferred_element_type=jnp.float32)
    return (out_re, out_im)


def block_tables(table_re, table_im):
    left = jnp.concatenate(
        [jnp.concatenate([table_re, -table_im], 1), jnp.concatenate([table_im, table_re], 1)], 0
    )
    right = jnp.concatenate(
        [jnp.concatenate([table_re, table_im], 1), jnp.concatenate([-table_im, table_re], 1)], 0
    )
    return left, right


def entry_kernel(order_ref, patch_ref, amp_ref, probe_ref, left_ref, right_ref, update_ref, grad_ref):
    slots = order_ref.shape[0] - 1
    count = order_ref[slots]
    group = next(size for size in (4, 2, 1) if slots % size == 0)
    grad_ref[...] = jnp.zeros(grad_ref.shape, grad_ref.dtype)
    update_ref[...] = jnp.zeros(update_ref.shape, update_ref.dtype)

    def one_group(index, carry):
        chosen = [order_ref[index * group + g] for g in range(group)]
        entry_body(chosen, patch_ref, amp_ref, probe_ref, left_ref, right_ref, update_ref, grad_ref)
        return carry

    lax.fori_loop(0, (count + group - 1) // group, one_group, 0)


def entry_body(chosen, patch_ref, amp_ref, probe_ref, left_ref, right_ref, update_ref, grad_ref):
    modes, length = probe_ref.shape[0], probe_ref.shape[-1]
    blocks = len(chosen) * modes
    patches = [
        (patch_ref[0, slot].astype(jnp.float32), patch_ref[1, slot].astype(jnp.float32))
        for slot in chosen
    ]
    left = left_ref[...]
    right = right_ref[...]
    exits_re, exits_im = [], []
    for patch_re, patch_im in patches:
        for m in range(modes):
            probe_re = probe_ref[m, 0]
            probe_im = probe_ref[m, 1]
            exits_re.append((probe_re * patch_re - probe_im * patch_im).astype(jnp.bfloat16))
            exits_im.append((probe_re * patch_im + probe_im * patch_re).astype(jnp.bfloat16))
    stacked = jnp.concatenate(
        [jnp.concatenate(exits_re, 1), jnp.concatenate(exits_im, 1)], 0
    )
    half = jnp.dot(left, stacked, preferred_element_type=jnp.float32).astype(jnp.bfloat16)

    def by_mode(wide):
        return jnp.concatenate(
            [
                jnp.concatenate(
                    [
                        wide[:length, j * length : (j + 1) * length],
                        wide[length:, j * length : (j + 1) * length],
                    ],
                    1,
                )
                for j in range(blocks)
            ],
            0,
        )

    def by_part(tall):
        return jnp.concatenate(
            [
                jnp.concatenate(
                    [tall[j * length : (j + 1) * length, :length] for j in range(blocks)], 1
                ),
                jnp.concatenate(
                    [tall[j * length : (j + 1) * length, length:] for j in range(blocks)], 1
                ),
            ],
            0,
        )

    far = jnp.dot(by_mode(half), right, preferred_element_type=jnp.float32)
    factors = []
    for g, slot in enumerate(chosen):
        intensity = jnp.zeros((length, length), jnp.float32)
        for m in range(modes):
            j = g * modes + m
            far_re = far[j * length : (j + 1) * length, :length]
            far_im = far[j * length : (j + 1) * length, length:]
            intensity = intensity + (far_re * far_re + far_im * far_im)
        measured = amp_ref[slot, :length, :].astype(jnp.float32)
        factor = measured / jnp.sqrt(jnp.maximum(intensity, 1.0)) - 1.0
        factors.extend([jnp.concatenate([factor, factor], 1)] * modes)
    scaled = (jnp.concatenate(factors, 0) * far).astype(jnp.bfloat16)
    back = jnp.dot(right, by_part(scaled), preferred_element_type=jnp.float32).astype(
        jnp.bfloat16
    )
    change = jnp.dot(by_mode(back), left, preferred_element_type=jnp.float32)
    grads = [[None, None] for _ in range(modes)]
    for g, slot in enumerate(chosen):
        patch_re, patch_im = patches[g]
        update_re = jnp.zeros((length, length), jnp.float32)
        update_im = jnp.zeros((length, length), jnp.float32)
        for m in range(modes):
            j = g * modes + m
            change_re = change[j * length : (j + 1) * length, :length]
            change_im = change[j * length : (j + 1) * length, length:]
            probe_re = probe_ref[m, 0]
            probe_im = probe_ref[m, 1]
            update_re = update_re + (probe_re * change_re + probe_im * change_im)
            update_im = update_im + (probe_re * change_im - probe_im * change_re)
            grad_re = patch_re * change_re + patch_im * change_im
            grad_im = patch_re * change_im - patch_im * change_re
            if g == 0:
                grads[m] = [grad_re, grad_im]
            else:
                grads[m] = [grads[m][0] + grad_re, grads[m][1] + grad_im]
        update_ref[0, slot] = update_re.astype(update_ref.dtype)
        update_ref[1, slot] = update_im.astype(update_ref.dtype)
    for m in range(modes):
        grad_ref[m, 0] += grads[m][0]
        grad_ref[m, 1] += grads[m][1]


def entries_kernel(order, patch, amp_in, probe_now, left, right):
    slots, length = amp_in.shape[0], amp_in.shape[-1]
    modes = probe_now.shape[0]
    flops = slots * 4 * 2 * (2 * length) * (2 * length) * (modes * length)
    whole = pl.BlockSpec(memory_space=pltpu.VMEM)
    grid_spec = pltpu.PrefetchScalarGridSpec(
        num_scalar_prefetch=1,
        grid=(1,),
        in_specs=[whole] * 5,
        out_specs=[whole] * 2,
    )
    return pl.pallas_call(
        entry_kernel,
        grid_spec=grid_spec,
        out_shape=[
            jax.ShapeDtypeStruct((2, slots, length, length), jnp.bfloat16),
            jax.ShapeDtypeStruct(probe_now.shape, jnp.float32),
        ],
        compiler_params=pltpu.CompilerParams(dimension_semantics=("arbitrary",)),
        cost_estimate=pl.CostEstimate(
            flops=flops,
            transcendentals=slots * length * length,
            bytes_accessed=slots * length * length * 10 + probe_now.size * 8,
        ),
    )(order, patch, amp_in, probe_now, left, right)


def route(amplitudes, batch_ids, scan_tile, scan_offset, tiles_here):
    tile_count = lax.axis_size("tile")
    steps, batch_rows = batch_ids.shape
    capacity = max(2, 2 * batch_rows // tile_count)
    slots = tile_count * capacity
    length = amplitudes.shape[-1]
    target = scan_tile[:, :, 0]
    owner = target // tiles_here
    local_tile = target - owner * tiles_here
    onehot = (owner[:, :, None] == jnp.arange(tile_count, dtype=jnp.int32)).astype(jnp.int32)
    place_in = jnp.sum((jnp.cumsum(onehot, axis=1) - 1) * onehot, axis=2)
    slot_of = owner * capacity + place_in
    chosen = (slot_of[:, None, :] == jnp.arange(slots, dtype=jnp.int32)[None, :, None]).astype(
        jnp.int32
    )
    fields = jnp.stack(
        [local_tile, scan_offset[:, :, 0], scan_offset[:, :, 1], jnp.ones_like(local_tile)], axis=2
    )
    meta = jnp.sum(chosen[:, :, :, None] * fields[:, None, :, :], axis=2)
    ids = jnp.sum(chosen * batch_ids[:, None, :], axis=2)
    amp_send = amplitudes[ids.reshape(-1)].reshape(steps, tile_count, capacity, length, length)
    return amp_send, meta.reshape(steps, tile_count, capacity, 4)


def unpack(arrived, meta, size):
    tile_count, capacity, rows, length = arrived.shape
    arrived = arrived.reshape(tile_count * capacity, rows, length)
    meta = meta.reshape(tile_count * capacity, 4)
    meta_in = jnp.stack([meta[:, 0] * size + meta[:, 1], meta[:, 2], meta[:, 3]], axis=1)
    return arrived, meta_in


def group_size(axes):
    count = 1
    for axis in axes:
        count *= lax.axis_size(axis)
    return count


def sum_over(value, axes, send_type):
    count = group_size(axes)
    parts = lax.all_to_all(value.astype(send_type).reshape(count, -1), axes, 0, 0, tiled=True)
    total = jnp.sum(parts.astype(jnp.float32), axis=0, keepdims=True).astype(send_type)
    return total, count


def all_sum_a2a(value, axes):
    total, count = sum_over(value, axes, value.dtype)
    spread = lax.all_to_all(jnp.broadcast_to(total, (count, total.shape[1])), axes, 0, 0, tiled=True)
    return spread.reshape(value.shape)


def all_sum_pairs(value, axis, send_type):
    count = lax.axis_size(axis)
    if count & (count - 1):
        return lax.psum(value.astype(send_type), axis).astype(jnp.float32)
    total = value.astype(send_type).astype(jnp.float32)
    step = 1
    while step < count:
        pairs = [(i, i ^ step) for i in range(count)]
        other = lax.ppermute(total.astype(send_type), axis, pairs)
        total = total.astype(send_type).astype(jnp.float32) + other.astype(jnp.float32)
        step *= 2
    return total


def entries_pass(stacked, probe_now, amp_in, meta_in, tables):
    table_re, table_im, table_neg = tables
    length = probe_now.shape[-1]
    rows_all, size = stacked.shape[1], stacked.shape[2]
    within = jnp.arange(length, dtype=jnp.int32)
    row_at, col_at, valid = meta_in[:, 0], meta_in[:, 1], meta_in[:, 2]
    pick_rows = (
        (row_at[:, None, None] + within[None, :, None])
        == jnp.arange(rows_all, dtype=jnp.int32)[None, None, :]
    ) & (valid[:, None, None] > 0)
    pick_rows = pick_rows.astype(jnp.bfloat16)
    pick_cols = (
        (col_at[:, None, None] + within[None, None, :])
        == jnp.arange(size, dtype=jnp.int32)[None, :, None]
    ).astype(jnp.bfloat16)
    rows = jnp.einsum(
        "skq,xqc->xskc", pick_rows, stacked, preferred_element_type=jnp.float32
    ).astype(jnp.bfloat16)
    patch = jnp.einsum("xskc,scl->xskl", rows, pick_cols, preferred_element_type=jnp.float32)
    left, right = block_tables(tables[0], tables[1])
    held = (valid > 0).astype(jnp.int32)
    count = jnp.sum(held)
    place = jnp.where(held > 0, jnp.cumsum(held) - 1, count + jnp.cumsum(1 - held) - 1)
    slots = valid.shape[0]
    order = jnp.sum(
        (place[:, None] == jnp.arange(slots, dtype=jnp.int32)[None, :])
        * jnp.arange(slots, dtype=jnp.int32)[:, None],
        axis=0,
    )
    order = jnp.concatenate([order, count[None]]).astype(jnp.int32)
    update, probe_grad = entries_kernel(
        order, patch.astype(jnp.bfloat16), amp_in, probe_now, left, right
    )
    spread = jnp.einsum(
        "xskl,scl->xskc", update, pick_cols, preferred_element_type=jnp.float32
    ).astype(jnp.bfloat16)
    local_sum = jnp.einsum("skq,xskc->xqc", pick_rows, spread, preferred_element_type=jnp.float32)
    return local_sum, probe_grad


def one_step(tiles_now, probe_now, amp_in, meta_in, tables, batch_total):
    tiles_here, size = tiles_now.shape[1], tiles_now.shape[2]
    slots, length = amp_in.shape[0], amp_in.shape[-1]
    stacked = tiles_now.astype(jnp.bfloat16).reshape(2, tiles_here * size, size)
    chunk = max(d for d in range(1, min(slots, 24) + 1) if slots % d == 0)
    if chunk == slots:
        local_sum, probe_grad = entries_pass(stacked, probe_now, amp_in, meta_in, tables)
    else:

        def body(carry, piece):
            part_sum, part_grad = entries_pass(stacked, probe_now, piece[0], piece[1], tables)
            return (carry[0] + part_sum, carry[1] + part_grad), None

        start = (jnp.zeros(stacked.shape, jnp.float32), jnp.zeros(probe_now.shape, jnp.float32))
        pieces = (
            amp_in.reshape(slots // chunk, chunk, length, length),
            meta_in.reshape(slots // chunk, chunk, 3),
        )
        (local_sum, probe_grad), _ = lax.scan(body, start, pieces)
    local_sum = local_sum.reshape(tiles_now.shape)
    probe_re = probe_now[:, 0]
    probe_im = probe_now[:, 1]
    peak_power = jnp.max(jnp.sum(probe_re * probe_re + probe_im * probe_im, axis=0))
    summed = all_sum_pairs(local_sum, "pat", jnp.bfloat16)
    tiles_next = tiles_now + summed / peak_power
    grad_sum = all_sum_a2a(probe_grad, ("tile", "pat"))
    probe_next = probe_now + probe_rate * grad_sum / batch_total
    return (tiles_next, probe_next, probe_grad)


def on_device(amplitudes, batch_ids, scan_tile, scan_offset, object_tiles, probe):
    tables = dft_tables(probe.shape[-1])
    tiles_here, size = object_tiles.shape[1], object_tiles.shape[2]
    batch_total = batch_ids.shape[1] * lax.axis_size("tile") * lax.axis_size("pat")
    payload, meta = route(amplitudes, batch_ids, scan_tile, scan_offset, tiles_here)
    tiles_now = object_tiles
    probe_now = probe
    placed = lax.all_to_all(jnp.swapaxes(meta, 0, 1), "tile", 0, 0, tiled=True)
    arrived = lax.all_to_all(jnp.swapaxes(payload, 0, 1), "tile", 0, 0, tiled=True)
    for step_no in range(batch_ids.shape[0]):
        amp_in, meta_in = unpack(arrived[:, step_no], placed[:, step_no], size)
        tiles_now, probe_now, _ = one_step(tiles_now, probe_now, amp_in, meta_in, tables, batch_total)
    return (tiles_now, probe_now)


def solution(mesh):
    in_specs = (
        P(("tile", "pat"), None, None),
        P(None, ("tile", "pat")),
        P(None, ("tile", "pat"), None),
        P(None, ("tile", "pat"), None),
        P(None, "tile", None, None),
        P(),
    )
    out_specs = (P(None, "tile", None, None), P())
    return jax.shard_map(
        on_device, mesh=mesh, in_specs=in_specs, out_specs=out_specs, check_vma=False
    )
```

```python
import math

import jax
import jax.numpy as jnp
from jax import lax
from jax.experimental import pallas as pl
from jax.experimental.pallas import tpu as pltpu
from jax.sharding import PartitionSpec as P

probe_rate = 8.0


def dft_tables(length):
    counter = jnp.arange(length, dtype=jnp.int32)
    product = counter[:, None] * counter[None, :] % length
    angle_table = 2.0 * math.pi / length * product.astype(jnp.float32)
    norm_factor = 1.0 / math.sqrt(length)
    table_re = (jnp.cos(angle_table) * norm_factor).astype(jnp.bfloat16)
    table_im = (-jnp.sin(angle_table) * norm_factor).astype(jnp.bfloat16)
    return (table_re, table_im, -table_im)


def transform(src_re, src_im, table_re, table_im):
    half_re = jnp.einsum(
        "kj,bmjc->bmkc", table_re, src_re, preferred_element_type=jnp.float32
    ) - jnp.einsum("kj,bmjc->bmkc", table_im, src_im, preferred_element_type=jnp.float32)
    half_im = jnp.einsum(
        "kj,bmjc->bmkc", table_re, src_im, preferred_element_type=jnp.float32
    ) + jnp.einsum("kj,bmjc->bmkc", table_im, src_re, preferred_element_type=jnp.float32)
    half_re = half_re.astype(jnp.bfloat16)
    half_im = half_im.astype(jnp.bfloat16)
    out_re = jnp.einsum(
        "bmkc,cl->bmkl", half_re, table_re, preferred_element_type=jnp.float32
    ) - jnp.einsum("bmkc,cl->bmkl", half_im, table_im, preferred_element_type=jnp.float32)
    out_im = jnp.einsum(
        "bmkc,cl->bmkl", half_re, table_im, preferred_element_type=jnp.float32
    ) + jnp.einsum("bmkc,cl->bmkl", half_im, table_re, preferred_element_type=jnp.float32)
    return (out_re, out_im)


def block_tables(table_re, table_im):
    left = jnp.concatenate(
        [jnp.concatenate([table_re, -table_im], 1), jnp.concatenate([table_im, table_re], 1)], 0
    )
    right = jnp.concatenate(
        [jnp.concatenate([table_re, table_im], 1), jnp.concatenate([-table_im, table_re], 1)], 0
    )
    return left, right


def entry_kernel(order_ref, patch_ref, amp_ref, probe_ref, left_ref, right_ref, update_ref, grad_ref):
    slots = order_ref.shape[0] - 1
    count = order_ref[slots]
    group = next(size for size in (4, 2, 1) if slots % size == 0)
    grad_ref[...] = jnp.zeros(grad_ref.shape, grad_ref.dtype)
    update_ref[...] = jnp.zeros(update_ref.shape, update_ref.dtype)

    def one_group(index, carry):
        chosen = [order_ref[index * group + g] for g in range(group)]
        entry_body(chosen, patch_ref, amp_ref, probe_ref, left_ref, right_ref, update_ref, grad_ref)
        return carry

    lax.fori_loop(0, (count + group - 1) // group, one_group, 0)


def entry_body(chosen, patch_ref, amp_ref, probe_ref, left_ref, right_ref, update_ref, grad_ref):
    modes, length = probe_ref.shape[0], probe_ref.shape[-1]
    blocks = len(chosen) * modes
    patches = [
        (patch_ref[0, slot].astype(jnp.float32), patch_ref[1, slot].astype(jnp.float32))
        for slot in chosen
    ]
    left = left_ref[...]
    right = right_ref[...]
    exits_re, exits_im = [], []
    for patch_re, patch_im in patches:
        for m in range(modes):
            probe_re = probe_ref[m, 0]
            probe_im = probe_ref[m, 1]
            exits_re.append((probe_re * patch_re - probe_im * patch_im).astype(jnp.bfloat16))
            exits_im.append((probe_re * patch_im + probe_im * patch_re).astype(jnp.bfloat16))
    stacked = jnp.concatenate(
        [jnp.concatenate(exits_re, 1), jnp.concatenate(exits_im, 1)], 0
    )
    half = jnp.dot(left, stacked, preferred_element_type=jnp.float32).astype(jnp.bfloat16)

    def by_mode(wide):
        return jnp.concatenate(
            [
                jnp.concatenate(
                    [
                        wide[:length, j * length : (j + 1) * length],
                        wide[length:, j * length : (j + 1) * length],
                    ],
                    1,
                )
                for j in range(blocks)
            ],
            0,
        )

    def by_part(tall):
        return jnp.concatenate(
            [
                jnp.concatenate(
                    [tall[j * length : (j + 1) * length, :length] for j in range(blocks)], 1
                ),
                jnp.concatenate(
                    [tall[j * length : (j + 1) * length, length:] for j in range(blocks)], 1
                ),
            ],
            0,
        )

    far = jnp.dot(by_mode(half), right, preferred_element_type=jnp.float32)
    factors = []
    for g, slot in enumerate(chosen):
        intensity = jnp.zeros((length, length), jnp.float32)
        for m in range(modes):
            j = g * modes + m
            far_re = far[j * length : (j + 1) * length, :length]
            far_im = far[j * length : (j + 1) * length, length:]
            intensity = intensity + (far_re * far_re + far_im * far_im)
        measured = amp_ref[slot, :length, :].astype(jnp.float32)
        factor = measured / jnp.sqrt(jnp.maximum(intensity, 1.0)) - 1.0
        factors.extend([jnp.concatenate([factor, factor], 1)] * modes)
    scaled = (jnp.concatenate(factors, 0) * far).astype(jnp.bfloat16)
    back = jnp.dot(right, by_part(scaled), preferred_element_type=jnp.float32).astype(
        jnp.bfloat16
    )
    change = jnp.dot(by_mode(back), left, preferred_element_type=jnp.float32)
    grads = [[None, None] for _ in range(modes)]
    for g, slot in enumerate(chosen):
        patch_re, patch_im = patches[g]
        update_re = jnp.zeros((length, length), jnp.float32)
        update_im = jnp.zeros((length, length), jnp.float32)
        for m in range(modes):
            j = g * modes + m
            change_re = change[j * length : (j + 1) * length, :length]
            change_im = change[j * length : (j + 1) * length, length:]
            probe_re = probe_ref[m, 0]
            probe_im = probe_ref[m, 1]
            update_re = update_re + (probe_re * change_re + probe_im * change_im)
            update_im = update_im + (probe_re * change_im - probe_im * change_re)
            grad_re = patch_re * change_re + patch_im * change_im
            grad_im = patch_re * change_im - patch_im * change_re
            if g == 0:
                grads[m] = [grad_re, grad_im]
            else:
                grads[m] = [grads[m][0] + grad_re, grads[m][1] + grad_im]
        update_ref[0, slot] = update_re.astype(update_ref.dtype)
        update_ref[1, slot] = update_im.astype(update_ref.dtype)
    for m in range(modes):
        grad_ref[m, 0] += grads[m][0]
        grad_ref[m, 1] += grads[m][1]


def entries_kernel(order, patch, amp_in, probe_now, left, right):
    slots, length = amp_in.shape[0], amp_in.shape[-1]
    modes = probe_now.shape[0]
    flops = slots * 4 * 2 * (2 * length) * (2 * length) * (modes * length)
    whole = pl.BlockSpec(memory_space=pltpu.VMEM)
    grid_spec = pltpu.PrefetchScalarGridSpec(
        num_scalar_prefetch=1,
        grid=(1,),
        in_specs=[whole] * 5,
        out_specs=[whole] * 2,
    )
    return pl.pallas_call(
        entry_kernel,
        grid_spec=grid_spec,
        out_shape=[
            jax.ShapeDtypeStruct((2, slots, length, length), jnp.bfloat16),
            jax.ShapeDtypeStruct(probe_now.shape, jnp.float32),
        ],
        compiler_params=pltpu.CompilerParams(dimension_semantics=("arbitrary",)),
        cost_estimate=pl.CostEstimate(
            flops=flops,
            transcendentals=slots * length * length,
            bytes_accessed=slots * length * length * 10 + probe_now.size * 8,
        ),
    )(order, patch, amp_in, probe_now, left, right)


def route(amplitudes, batch_ids, scan_tile, scan_offset, tiles_here):
    tile_count = lax.axis_size("tile")
    steps, batch_rows = batch_ids.shape
    capacity = max(2, 2 * batch_rows // tile_count)
    slots = tile_count * capacity
    length = amplitudes.shape[-1]
    target = scan_tile[:, :, 0]
    owner = target // tiles_here
    local_tile = target - owner * tiles_here
    onehot = (owner[:, :, None] == jnp.arange(tile_count, dtype=jnp.int32)).astype(jnp.int32)
    place_in = jnp.sum((jnp.cumsum(onehot, axis=1) - 1) * onehot, axis=2)
    slot_of = owner * capacity + place_in
    chosen = (slot_of[:, None, :] == jnp.arange(slots, dtype=jnp.int32)[None, :, None]).astype(
        jnp.int32
    )
    fields = jnp.stack(
        [local_tile, scan_offset[:, :, 0], scan_offset[:, :, 1], jnp.ones_like(local_tile)], axis=2
    )
    meta = jnp.sum(chosen[:, :, :, None] * fields[:, None, :, :], axis=2)
    ids = jnp.sum(chosen * batch_ids[:, None, :], axis=2)
    amp_send = amplitudes[ids.reshape(-1)].reshape(steps, tile_count, capacity, length, length)
    return amp_send, meta.reshape(steps, tile_count, capacity, 4)


def unpack(arrived, meta, size):
    tile_count, capacity, rows, length = arrived.shape
    arrived = arrived.reshape(tile_count * capacity, rows, length)
    meta = meta.reshape(tile_count * capacity, 4)
    meta_in = jnp.stack([meta[:, 0] * size + meta[:, 1], meta[:, 2], meta[:, 3]], axis=1)
    return arrived, meta_in


def group_size(axes):
    count = 1
    for axis in axes:
        count *= lax.axis_size(axis)
    return count


def sum_over(value, axes, send_type):
    count = group_size(axes)
    parts = lax.all_to_all(value.astype(send_type).reshape(count, -1), axes, 0, 0, tiled=True)
    total = jnp.sum(parts.astype(jnp.float32), axis=0, keepdims=True).astype(send_type)
    return total, count


def all_sum_a2a(value, axes):
    total, count = sum_over(value, axes, value.dtype)
    total = total.astype(jnp.bfloat16)
    spread = lax.all_to_all(jnp.broadcast_to(total, (count, total.shape[1])), axes, 0, 0, tiled=True)
    return spread.reshape(value.shape).astype(jnp.float32)


def all_sum_pairs(value, axis, send_type):
    count = lax.axis_size(axis)
    if count & (count - 1):
        return lax.psum(value.astype(send_type), axis).astype(jnp.float32)
    total = value.astype(send_type).astype(jnp.float32)
    step = 1
    while step < count:
        pairs = [(i, i ^ step) for i in range(count)]
        other = lax.ppermute(total.astype(send_type), axis, pairs)
        total = total.astype(send_type).astype(jnp.float32) + other.astype(jnp.float32)
        step *= 2
    return total


def entries_pass(stacked, probe_now, amp_in, meta_in, tables):
    table_re, table_im, table_neg = tables
    length = probe_now.shape[-1]
    rows_all, size = stacked.shape[1], stacked.shape[2]
    within = jnp.arange(length, dtype=jnp.int32)
    row_at, col_at, valid = meta_in[:, 0], meta_in[:, 1], meta_in[:, 2]
    pick_rows = (
        (row_at[:, None, None] + within[None, :, None])
        == jnp.arange(rows_all, dtype=jnp.int32)[None, None, :]
    ) & (valid[:, None, None] > 0)
    pick_rows = pick_rows.astype(jnp.bfloat16)
    pick_cols = (
        (col_at[:, None, None] + within[None, None, :])
        == jnp.arange(size, dtype=jnp.int32)[None, :, None]
    ).astype(jnp.bfloat16)
    rows = jnp.einsum(
        "skq,xqc->xskc", pick_rows, stacked, preferred_element_type=jnp.float32
    ).astype(jnp.bfloat16)
    patch = jnp.einsum("xskc,scl->xskl", rows, pick_cols, preferred_element_type=jnp.float32)
    left, right = block_tables(tables[0], tables[1])
    held = (valid > 0).astype(jnp.int32)
    count = jnp.sum(held)
    place = jnp.where(held > 0, jnp.cumsum(held) - 1, count + jnp.cumsum(1 - held) - 1)
    slots = valid.shape[0]
    order = jnp.sum(
        (place[:, None] == jnp.arange(slots, dtype=jnp.int32)[None, :])
        * jnp.arange(slots, dtype=jnp.int32)[:, None],
        axis=0,
    )
    order = jnp.concatenate([order, count[None]]).astype(jnp.int32)
    update, probe_grad = entries_kernel(
        order, patch.astype(jnp.bfloat16), amp_in, probe_now, left, right
    )
    spread = jnp.einsum(
        "xskl,scl->xskc", update, pick_cols, preferred_element_type=jnp.float32
    ).astype(jnp.bfloat16)
    local_sum = jnp.einsum("skq,xskc->xqc", pick_rows, spread, preferred_element_type=jnp.float32)
    return local_sum, probe_grad


def one_step(tiles_now, probe_now, amp_in, meta_in, tables, batch_total):
    tiles_here, size = tiles_now.shape[1], tiles_now.shape[2]
    slots, length = amp_in.shape[0], amp_in.shape[-1]
    stacked = tiles_now.astype(jnp.bfloat16).reshape(2, tiles_here * size, size)
    chunk = max(d for d in range(1, min(slots, 24) + 1) if slots % d == 0)
    if chunk == slots:
        local_sum, probe_grad = entries_pass(stacked, probe_now, amp_in, meta_in, tables)
    else:

        def body(carry, piece):
            part_sum, part_grad = entries_pass(stacked, probe_now, piece[0], piece[1], tables)
            return (carry[0] + part_sum, carry[1] + part_grad), None

        start = (jnp.zeros(stacked.shape, jnp.float32), jnp.zeros(probe_now.shape, jnp.float32))
        pieces = (
            amp_in.reshape(slots // chunk, chunk, length, length),
            meta_in.reshape(slots // chunk, chunk, 3),
        )
        (local_sum, probe_grad), _ = lax.scan(body, start, pieces)
    local_sum = local_sum.reshape(tiles_now.shape)
    probe_re = probe_now[:, 0]
    probe_im = probe_now[:, 1]
    peak_power = jnp.max(jnp.sum(probe_re * probe_re + probe_im * probe_im, axis=0))
    summed = all_sum_pairs(local_sum, "pat", jnp.bfloat16)
    tiles_next = tiles_now + summed / peak_power
    grad_sum = all_sum_a2a(probe_grad, ("tile", "pat"))
    probe_next = probe_now + probe_rate * grad_sum / batch_total
    return (tiles_next, probe_next, probe_grad)


def on_device(amplitudes, batch_ids, scan_tile, scan_offset, object_tiles, probe):
    tables = dft_tables(probe.shape[-1])
    tiles_here, size = object_tiles.shape[1], object_tiles.shape[2]
    batch_total = batch_ids.shape[1] * lax.axis_size("tile") * lax.axis_size("pat")
    payload, meta = route(amplitudes, batch_ids, scan_tile, scan_offset, tiles_here)
    tiles_now = object_tiles
    probe_now = probe
    placed = lax.all_to_all(jnp.swapaxes(meta, 0, 1), "tile", 0, 0, tiled=True)
    arrived = lax.all_to_all(jnp.swapaxes(payload, 0, 1), "tile", 0, 0, tiled=True)
    for step_no in range(batch_ids.shape[0]):
        amp_in, meta_in = unpack(arrived[:, step_no], placed[:, step_no], size)
        tiles_now, probe_now, _ = one_step(tiles_now, probe_now, amp_in, meta_in, tables, batch_total)
    return (tiles_now, probe_now)


def solution(mesh):
    in_specs = (
        P(("tile", "pat"), None, None),
        P(None, ("tile", "pat")),
        P(None, ("tile", "pat"), None),
        P(None, ("tile", "pat"), None),
        P(None, "tile", None, None),
        P(),
    )
    out_specs = (P(None, "tile", None, None), P())
    return jax.shard_map(
        on_device, mesh=mesh, in_specs=in_specs, out_specs=out_specs, check_vma=False
    )
```

```python
import math

import jax
import jax.numpy as jnp
from jax import lax
from jax.experimental import pallas as pl
from jax.experimental.pallas import tpu as pltpu
from jax.sharding import PartitionSpec as P

probe_rate = 8.0


def dft_tables(length):
    counter = jnp.arange(length, dtype=jnp.int32)
    product = counter[:, None] * counter[None, :] % length
    angle_table = 2.0 * math.pi / length * product.astype(jnp.float32)
    norm_factor = 1.0 / math.sqrt(length)
    table_re = (jnp.cos(angle_table) * norm_factor).astype(jnp.bfloat16)
    table_im = (-jnp.sin(angle_table) * norm_factor).astype(jnp.bfloat16)
    return (table_re, table_im, -table_im)


def transform(src_re, src_im, table_re, table_im):
    half_re = jnp.einsum(
        "kj,bmjc->bmkc", table_re, src_re, preferred_element_type=jnp.float32
    ) - jnp.einsum("kj,bmjc->bmkc", table_im, src_im, preferred_element_type=jnp.float32)
    half_im = jnp.einsum(
        "kj,bmjc->bmkc", table_re, src_im, preferred_element_type=jnp.float32
    ) + jnp.einsum("kj,bmjc->bmkc", table_im, src_re, preferred_element_type=jnp.float32)
    half_re = half_re.astype(jnp.bfloat16)
    half_im = half_im.astype(jnp.bfloat16)
    out_re = jnp.einsum(
        "bmkc,cl->bmkl", half_re, table_re, preferred_element_type=jnp.float32
    ) - jnp.einsum("bmkc,cl->bmkl", half_im, table_im, preferred_element_type=jnp.float32)
    out_im = jnp.einsum(
        "bmkc,cl->bmkl", half_re, table_im, preferred_element_type=jnp.float32
    ) + jnp.einsum("bmkc,cl->bmkl", half_im, table_re, preferred_element_type=jnp.float32)
    return (out_re, out_im)


def block_tables(table_re, table_im):
    left = jnp.concatenate(
        [jnp.concatenate([table_re, -table_im], 1), jnp.concatenate([table_im, table_re], 1)], 0
    )
    right = jnp.concatenate(
        [jnp.concatenate([table_re, table_im], 1), jnp.concatenate([-table_im, table_re], 1)], 0
    )
    return left, right


def entry_kernel(order_ref, patch_ref, amp_ref, probe_ref, left_ref, right_ref, update_ref, grad_ref):
    slots = order_ref.shape[0] - 1
    count = order_ref[slots]
    group = next(size for size in (4, 2, 1) if slots % size == 0)
    grad_ref[...] = jnp.zeros(grad_ref.shape, grad_ref.dtype)
    update_ref[...] = jnp.zeros(update_ref.shape, update_ref.dtype)

    def one_group(index, carry):
        chosen = [order_ref[index * group + g] for g in range(group)]
        entry_body(chosen, patch_ref, amp_ref, probe_ref, left_ref, right_ref, update_ref, grad_ref)
        return carry

    lax.fori_loop(0, (count + group - 1) // group, one_group, 0)


def entry_body(chosen, patch_ref, amp_ref, probe_ref, left_ref, right_ref, update_ref, grad_ref):
    modes, length = probe_ref.shape[0], probe_ref.shape[-1]
    blocks = len(chosen) * modes
    patches = [
        (patch_ref[0, slot].astype(jnp.float32), patch_ref[1, slot].astype(jnp.float32))
        for slot in chosen
    ]
    left = left_ref[...]
    right = right_ref[...]
    exits_re, exits_im = [], []
    for patch_re, patch_im in patches:
        for m in range(modes):
            probe_re = probe_ref[m, 0]
            probe_im = probe_ref[m, 1]
            exits_re.append((probe_re * patch_re - probe_im * patch_im).astype(jnp.bfloat16))
            exits_im.append((probe_re * patch_im + probe_im * patch_re).astype(jnp.bfloat16))
    stacked = jnp.concatenate(
        [jnp.concatenate(exits_re, 1), jnp.concatenate(exits_im, 1)], 0
    )
    half = jnp.dot(left, stacked, preferred_element_type=jnp.float32).astype(jnp.bfloat16)

    def by_mode(wide):
        return jnp.concatenate(
            [
                jnp.concatenate(
                    [
                        wide[:length, j * length : (j + 1) * length],
                        wide[length:, j * length : (j + 1) * length],
                    ],
                    1,
                )
                for j in range(blocks)
            ],
            0,
        )

    def by_part(tall):
        return jnp.concatenate(
            [
                jnp.concatenate(
                    [tall[j * length : (j + 1) * length, :length] for j in range(blocks)], 1
                ),
                jnp.concatenate(
                    [tall[j * length : (j + 1) * length, length:] for j in range(blocks)], 1
                ),
            ],
            0,
        )

    far = jnp.dot(by_mode(half), right, preferred_element_type=jnp.float32)
    factors = []
    for g, slot in enumerate(chosen):
        intensity = jnp.zeros((length, length), jnp.float32)
        for m in range(modes):
            j = g * modes + m
            far_re = far[j * length : (j + 1) * length, :length]
            far_im = far[j * length : (j + 1) * length, length:]
            intensity = intensity + (far_re * far_re + far_im * far_im)
        measured = amp_ref[slot, :length, :].astype(jnp.float32)
        factor = measured / jnp.sqrt(jnp.maximum(intensity, 1.0)) - 1.0
        factors.extend([jnp.concatenate([factor, factor], 1)] * modes)
    scaled = (jnp.concatenate(factors, 0) * far).astype(jnp.bfloat16)
    back = jnp.dot(right, by_part(scaled), preferred_element_type=jnp.float32).astype(
        jnp.bfloat16
    )
    change = jnp.dot(by_mode(back), left, preferred_element_type=jnp.float32)
    grads = [[None, None] for _ in range(modes)]
    for g, slot in enumerate(chosen):
        patch_re, patch_im = patches[g]
        update_re = jnp.zeros((length, length), jnp.float32)
        update_im = jnp.zeros((length, length), jnp.float32)
        for m in range(modes):
            j = g * modes + m
            change_re = change[j * length : (j + 1) * length, :length]
            change_im = change[j * length : (j + 1) * length, length:]
            probe_re = probe_ref[m, 0]
            probe_im = probe_ref[m, 1]
            update_re = update_re + (probe_re * change_re + probe_im * change_im)
            update_im = update_im + (probe_re * change_im - probe_im * change_re)
            grad_re = patch_re * change_re + patch_im * change_im
            grad_im = patch_re * change_im - patch_im * change_re
            if g == 0:
                grads[m] = [grad_re, grad_im]
            else:
                grads[m] = [grads[m][0] + grad_re, grads[m][1] + grad_im]
        update_ref[0, slot] = update_re.astype(update_ref.dtype)
        update_ref[1, slot] = update_im.astype(update_ref.dtype)
    for m in range(modes):
        grad_ref[m, 0] += grads[m][0]
        grad_ref[m, 1] += grads[m][1]


def entries_kernel(order, patch, amp_in, probe_now, left, right):
    slots, length = amp_in.shape[0], amp_in.shape[-1]
    modes = probe_now.shape[0]
    flops = slots * 4 * 2 * (2 * length) * (2 * length) * (modes * length)
    whole = pl.BlockSpec(memory_space=pltpu.VMEM)
    grid_spec = pltpu.PrefetchScalarGridSpec(
        num_scalar_prefetch=1,
        grid=(1,),
        in_specs=[whole] * 5,
        out_specs=[whole] * 2,
    )
    return pl.pallas_call(
        entry_kernel,
        grid_spec=grid_spec,
        out_shape=[
            jax.ShapeDtypeStruct((2, slots, length, length), jnp.bfloat16),
            jax.ShapeDtypeStruct(probe_now.shape, jnp.float32),
        ],
        compiler_params=pltpu.CompilerParams(dimension_semantics=("arbitrary",)),
        cost_estimate=pl.CostEstimate(
            flops=flops,
            transcendentals=slots * length * length,
            bytes_accessed=slots * length * length * 10 + probe_now.size * 8,
        ),
    )(order, patch, amp_in, probe_now, left, right)


def route(amplitudes, batch_ids, scan_tile, scan_offset, tiles_here):
    tile_count = lax.axis_size("tile")
    steps, batch_rows = batch_ids.shape
    capacity = max(2, 2 * batch_rows // tile_count)
    slots = tile_count * capacity
    length = amplitudes.shape[-1]
    target = scan_tile[:, :, 0]
    owner = target // tiles_here
    local_tile = target - owner * tiles_here
    onehot = (owner[:, :, None] == jnp.arange(tile_count, dtype=jnp.int32)).astype(jnp.int32)
    place_in = jnp.sum((jnp.cumsum(onehot, axis=1) - 1) * onehot, axis=2)
    slot_of = owner * capacity + place_in
    chosen = (slot_of[:, None, :] == jnp.arange(slots, dtype=jnp.int32)[None, :, None]).astype(
        jnp.int32
    )
    fields = jnp.stack(
        [local_tile, scan_offset[:, :, 0], scan_offset[:, :, 1], jnp.ones_like(local_tile)], axis=2
    )
    meta = jnp.sum(chosen[:, :, :, None] * fields[:, None, :, :], axis=2)
    ids = jnp.sum(chosen * batch_ids[:, None, :], axis=2)
    amp_send = amplitudes[ids.reshape(-1)].reshape(steps, tile_count, capacity, length, length)
    return amp_send, meta.reshape(steps, tile_count, capacity, 4)


def unpack(arrived, meta, size):
    tile_count, capacity, rows, length = arrived.shape
    arrived = arrived.reshape(tile_count * capacity, rows, length)
    meta = meta.reshape(tile_count * capacity, 4)
    meta_in = jnp.stack([meta[:, 0] * size + meta[:, 1], meta[:, 2], meta[:, 3]], axis=1)
    return arrived, meta_in


def group_size(axes):
    count = 1
    for axis in axes:
        count *= lax.axis_size(axis)
    return count


def sum_over(value, axes, send_type):
    count = group_size(axes)
    parts = lax.all_to_all(value.astype(send_type).reshape(count, -1), axes, 0, 0, tiled=True)
    total = jnp.sum(parts.astype(jnp.float32), axis=0, keepdims=True).astype(send_type)
    return total, count


def all_sum_a2a(value, axes):
    total, count = sum_over(value, axes, value.dtype)
    spread = lax.all_to_all(jnp.broadcast_to(total, (count, total.shape[1])), axes, 0, 0, tiled=True)
    return spread.reshape(value.shape)


def all_sum_pairs(value, axis, send_type):
    count = lax.axis_size(axis)
    if count & (count - 1):
        return lax.psum(value.astype(send_type), axis).astype(jnp.float32)
    total = value.astype(send_type).astype(jnp.float32)
    step = count // 2
    while step >= 1:
        pairs = [(i, i ^ step) for i in range(count)]
        other = lax.ppermute(total.astype(send_type), axis, pairs)
        total = total.astype(send_type).astype(jnp.float32) + other.astype(jnp.float32)
        step //= 2
    return total


def entries_pass(stacked, probe_now, amp_in, meta_in, tables):
    table_re, table_im, table_neg = tables
    length = probe_now.shape[-1]
    rows_all, size = stacked.shape[1], stacked.shape[2]
    within = jnp.arange(length, dtype=jnp.int32)
    row_at, col_at, valid = meta_in[:, 0], meta_in[:, 1], meta_in[:, 2]
    pick_rows = (
        (row_at[:, None, None] + within[None, :, None])
        == jnp.arange(rows_all, dtype=jnp.int32)[None, None, :]
    ) & (valid[:, None, None] > 0)
    pick_rows = pick_rows.astype(jnp.bfloat16)
    pick_cols = (
        (col_at[:, None, None] + within[None, None, :])
        == jnp.arange(size, dtype=jnp.int32)[None, :, None]
    ).astype(jnp.bfloat16)
    rows = jnp.einsum(
        "skq,xqc->xskc", pick_rows, stacked, preferred_element_type=jnp.float32
    ).astype(jnp.bfloat16)
    patch = jnp.einsum("xskc,scl->xskl", rows, pick_cols, preferred_element_type=jnp.float32)
    left, right = block_tables(tables[0], tables[1])
    held = (valid > 0).astype(jnp.int32)
    count = jnp.sum(held)
    place = jnp.where(held > 0, jnp.cumsum(held) - 1, count + jnp.cumsum(1 - held) - 1)
    slots = valid.shape[0]
    order = jnp.sum(
        (place[:, None] == jnp.arange(slots, dtype=jnp.int32)[None, :])
        * jnp.arange(slots, dtype=jnp.int32)[:, None],
        axis=0,
    )
    order = jnp.concatenate([order, count[None]]).astype(jnp.int32)
    update, probe_grad = entries_kernel(
        order, patch.astype(jnp.bfloat16), amp_in, probe_now, left, right
    )
    spread = jnp.einsum(
        "xskl,scl->xskc", update, pick_cols, preferred_element_type=jnp.float32
    ).astype(jnp.bfloat16)
    local_sum = jnp.einsum("skq,xskc->xqc", pick_rows, spread, preferred_element_type=jnp.float32)
    return local_sum, probe_grad


def one_step(tiles_now, probe_now, amp_in, meta_in, tables, batch_total):
    tiles_here, size = tiles_now.shape[1], tiles_now.shape[2]
    slots, length = amp_in.shape[0], amp_in.shape[-1]
    stacked = tiles_now.astype(jnp.bfloat16).reshape(2, tiles_here * size, size)
    chunk = max(d for d in range(1, min(slots, 24) + 1) if slots % d == 0)
    if chunk == slots:
        local_sum, probe_grad = entries_pass(stacked, probe_now, amp_in, meta_in, tables)
    else:

        def body(carry, piece):
            part_sum, part_grad = entries_pass(stacked, probe_now, piece[0], piece[1], tables)
            return (carry[0] + part_sum, carry[1] + part_grad), None

        start = (jnp.zeros(stacked.shape, jnp.float32), jnp.zeros(probe_now.shape, jnp.float32))
        pieces = (
            amp_in.reshape(slots // chunk, chunk, length, length),
            meta_in.reshape(slots // chunk, chunk, 3),
        )
        (local_sum, probe_grad), _ = lax.scan(body, start, pieces)
    local_sum = local_sum.reshape(tiles_now.shape)
    probe_re = probe_now[:, 0]
    probe_im = probe_now[:, 1]
    peak_power = jnp.max(jnp.sum(probe_re * probe_re + probe_im * probe_im, axis=0))
    summed = all_sum_pairs(local_sum, "pat", jnp.bfloat16)
    tiles_next = tiles_now + summed / peak_power
    grad_sum = all_sum_a2a(probe_grad, ("tile", "pat"))
    probe_next = probe_now + probe_rate * grad_sum / batch_total
    return (tiles_next, probe_next, probe_grad)


def on_device(amplitudes, batch_ids, scan_tile, scan_offset, object_tiles, probe):
    tables = dft_tables(probe.shape[-1])
    tiles_here, size = object_tiles.shape[1], object_tiles.shape[2]
    batch_total = batch_ids.shape[1] * lax.axis_size("tile") * lax.axis_size("pat")
    payload, meta = route(amplitudes, batch_ids, scan_tile, scan_offset, tiles_here)
    tiles_now = object_tiles
    probe_now = probe
    placed = lax.all_to_all(jnp.swapaxes(meta, 0, 1), "tile", 0, 0, tiled=True)
    arrived = lax.all_to_all(jnp.swapaxes(payload, 0, 1), "tile", 0, 0, tiled=True)
    for step_no in range(batch_ids.shape[0]):
        amp_in, meta_in = unpack(arrived[:, step_no], placed[:, step_no], size)
        tiles_now, probe_now, _ = one_step(tiles_now, probe_now, amp_in, meta_in, tables, batch_total)
    return (tiles_now, probe_now)


def solution(mesh):
    in_specs = (
        P(("tile", "pat"), None, None),
        P(None, ("tile", "pat")),
        P(None, ("tile", "pat"), None),
        P(None, ("tile", "pat"), None),
        P(None, "tile", None, None),
        P(),
    )
    out_specs = (P(None, "tile", None, None), P())
    return jax.shard_map(
        on_device, mesh=mesh, in_specs=in_specs, out_specs=out_specs, check_vma=False
    )
```

```python
import math

import jax
import jax.numpy as jnp
from jax import lax
from jax.experimental import pallas as pl
from jax.experimental.pallas import tpu as pltpu
from jax.sharding import PartitionSpec as P

probe_rate = 8.0


def dft_tables(length):
    counter = jnp.arange(length, dtype=jnp.int32)
    product = counter[:, None] * counter[None, :] % length
    angle_table = 2.0 * math.pi / length * product.astype(jnp.float32)
    norm_factor = 1.0 / math.sqrt(length)
    table_re = (jnp.cos(angle_table) * norm_factor).astype(jnp.bfloat16)
    table_im = (-jnp.sin(angle_table) * norm_factor).astype(jnp.bfloat16)
    return (table_re, table_im, -table_im)


def transform(src_re, src_im, table_re, table_im):
    half_re = jnp.einsum(
        "kj,bmjc->bmkc", table_re, src_re, preferred_element_type=jnp.float32
    ) - jnp.einsum("kj,bmjc->bmkc", table_im, src_im, preferred_element_type=jnp.float32)
    half_im = jnp.einsum(
        "kj,bmjc->bmkc", table_re, src_im, preferred_element_type=jnp.float32
    ) + jnp.einsum("kj,bmjc->bmkc", table_im, src_re, preferred_element_type=jnp.float32)
    half_re = half_re.astype(jnp.bfloat16)
    half_im = half_im.astype(jnp.bfloat16)
    out_re = jnp.einsum(
        "bmkc,cl->bmkl", half_re, table_re, preferred_element_type=jnp.float32
    ) - jnp.einsum("bmkc,cl->bmkl", half_im, table_im, preferred_element_type=jnp.float32)
    out_im = jnp.einsum(
        "bmkc,cl->bmkl", half_re, table_im, preferred_element_type=jnp.float32
    ) + jnp.einsum("bmkc,cl->bmkl", half_im, table_re, preferred_element_type=jnp.float32)
    return (out_re, out_im)


def block_tables(table_re, table_im):
    left = jnp.concatenate(
        [jnp.concatenate([table_re, -table_im], 1), jnp.concatenate([table_im, table_re], 1)], 0
    )
    right = jnp.concatenate(
        [jnp.concatenate([table_re, table_im], 1), jnp.concatenate([-table_im, table_re], 1)], 0
    )
    return left, right


def entry_kernel(order_ref, patch_ref, amp_ref, probe_ref, left_ref, right_ref, update_ref, grad_ref):
    slots = order_ref.shape[0] - 1
    count = order_ref[slots]
    group = next(size for size in (4, 2, 1) if slots % size == 0)
    grad_ref[...] = jnp.zeros(grad_ref.shape, grad_ref.dtype)

    def clear(index, carry):
        update_ref[:, order_ref[index]] = jnp.zeros((2,) + update_ref.shape[2:], update_ref.dtype)
        return carry

    lax.fori_loop(count, slots, clear, 0)

    def one_group(index, carry):
        chosen = [order_ref[index * group + g] for g in range(group)]
        entry_body(chosen, patch_ref, amp_ref, probe_ref, left_ref, right_ref, update_ref, grad_ref)
        return carry

    lax.fori_loop(0, (count + group - 1) // group, one_group, 0)


def entry_body(chosen, patch_ref, amp_ref, probe_ref, left_ref, right_ref, update_ref, grad_ref):
    modes, length = probe_ref.shape[0], probe_ref.shape[-1]
    blocks = len(chosen) * modes
    patches = [
        (patch_ref[0, slot].astype(jnp.float32), patch_ref[1, slot].astype(jnp.float32))
        for slot in chosen
    ]
    left = left_ref[...]
    right = right_ref[...]
    exits_re, exits_im = [], []
    for patch_re, patch_im in patches:
        for m in range(modes):
            probe_re = probe_ref[m, 0]
            probe_im = probe_ref[m, 1]
            exits_re.append((probe_re * patch_re - probe_im * patch_im).astype(jnp.bfloat16))
            exits_im.append((probe_re * patch_im + probe_im * patch_re).astype(jnp.bfloat16))
    stacked = jnp.concatenate(
        [jnp.concatenate(exits_re, 1), jnp.concatenate(exits_im, 1)], 0
    )
    half = jnp.dot(left, stacked, preferred_element_type=jnp.float32).astype(jnp.bfloat16)

    def by_mode(wide):
        return jnp.concatenate(
            [
                jnp.concatenate(
                    [
                        wide[:length, j * length : (j + 1) * length],
                        wide[length:, j * length : (j + 1) * length],
                    ],
                    1,
                )
                for j in range(blocks)
            ],
            0,
        )

    def by_part(tall):
        return jnp.concatenate(
            [
                jnp.concatenate(
                    [tall[j * length : (j + 1) * length, :length] for j in range(blocks)], 1
                ),
                jnp.concatenate(
                    [tall[j * length : (j + 1) * length, length:] for j in range(blocks)], 1
                ),
            ],
            0,
        )

    far = jnp.dot(by_mode(half), right, preferred_element_type=jnp.float32)
    factors = []
    for g, slot in enumerate(chosen):
        intensity = jnp.zeros((length, length), jnp.float32)
        for m in range(modes):
            j = g * modes + m
            far_re = far[j * length : (j + 1) * length, :length]
            far_im = far[j * length : (j + 1) * length, length:]
            intensity = intensity + (far_re * far_re + far_im * far_im)
        measured = amp_ref[slot, :length, :].astype(jnp.float32)
        factor = measured / jnp.sqrt(jnp.maximum(intensity, 1.0)) - 1.0
        factors.extend([jnp.concatenate([factor, factor], 1)] * modes)
    scaled = (jnp.concatenate(factors, 0) * far).astype(jnp.bfloat16)
    back = jnp.dot(right, by_part(scaled), preferred_element_type=jnp.float32).astype(
        jnp.bfloat16
    )
    change = jnp.dot(by_mode(back), left, preferred_element_type=jnp.float32)
    grads = [[None, None] for _ in range(modes)]
    for g, slot in enumerate(chosen):
        patch_re, patch_im = patches[g]
        update_re = jnp.zeros((length, length), jnp.float32)
        update_im = jnp.zeros((length, length), jnp.float32)
        for m in range(modes):
            j = g * modes + m
            change_re = change[j * length : (j + 1) * length, :length]
            change_im = change[j * length : (j + 1) * length, length:]
            probe_re = probe_ref[m, 0]
            probe_im = probe_ref[m, 1]
            update_re = update_re + (probe_re * change_re + probe_im * change_im)
            update_im = update_im + (probe_re * change_im - probe_im * change_re)
            grad_re = patch_re * change_re + patch_im * change_im
            grad_im = patch_re * change_im - patch_im * change_re
            if g == 0:
                grads[m] = [grad_re, grad_im]
            else:
                grads[m] = [grads[m][0] + grad_re, grads[m][1] + grad_im]
        update_ref[0, slot] = update_re.astype(update_ref.dtype)
        update_ref[1, slot] = update_im.astype(update_ref.dtype)
    for m in range(modes):
        grad_ref[m, 0] += grads[m][0]
        grad_ref[m, 1] += grads[m][1]


def entries_kernel(order, patch, amp_in, probe_now, left, right):
    slots, length = amp_in.shape[0], amp_in.shape[-1]
    modes = probe_now.shape[0]
    flops = slots * 4 * 2 * (2 * length) * (2 * length) * (modes * length)
    whole = pl.BlockSpec(memory_space=pltpu.VMEM)
    grid_spec = pltpu.PrefetchScalarGridSpec(
        num_scalar_prefetch=1,
        grid=(1,),
        in_specs=[whole] * 5,
        out_specs=[whole] * 2,
    )
    return pl.pallas_call(
        entry_kernel,
        grid_spec=grid_spec,
        out_shape=[
            jax.ShapeDtypeStruct((2, slots, length, length), jnp.bfloat16),
            jax.ShapeDtypeStruct(probe_now.shape, jnp.float32),
        ],
        compiler_params=pltpu.CompilerParams(dimension_semantics=("arbitrary",)),
        cost_estimate=pl.CostEstimate(
            flops=flops,
            transcendentals=slots * length * length,
            bytes_accessed=slots * length * length * 10 + probe_now.size * 8,
        ),
    )(order, patch, amp_in, probe_now, left, right)


def route(amplitudes, batch_ids, scan_tile, scan_offset, tiles_here):
    tile_count = lax.axis_size("tile")
    steps, batch_rows = batch_ids.shape
    capacity = max(2, 2 * batch_rows // tile_count)
    slots = tile_count * capacity
    length = amplitudes.shape[-1]
    target = scan_tile[:, :, 0]
    owner = target // tiles_here
    local_tile = target - owner * tiles_here
    onehot = (owner[:, :, None] == jnp.arange(tile_count, dtype=jnp.int32)).astype(jnp.int32)
    place_in = jnp.sum((jnp.cumsum(onehot, axis=1) - 1) * onehot, axis=2)
    slot_of = owner * capacity + place_in
    chosen = (slot_of[:, None, :] == jnp.arange(slots, dtype=jnp.int32)[None, :, None]).astype(
        jnp.int32
    )
    fields = jnp.stack(
        [local_tile, scan_offset[:, :, 0], scan_offset[:, :, 1], jnp.ones_like(local_tile)], axis=2
    )
    meta = jnp.sum(chosen[:, :, :, None] * fields[:, None, :, :], axis=2)
    ids = jnp.sum(chosen * batch_ids[:, None, :], axis=2)
    amp_send = amplitudes[ids.reshape(-1)].reshape(steps, tile_count, capacity, length, length)
    return amp_send, meta.reshape(steps, tile_count, capacity, 4)


def unpack(arrived, meta, size):
    tile_count, capacity, rows, length = arrived.shape
    arrived = arrived.reshape(tile_count * capacity, rows, length)
    meta = meta.reshape(tile_count * capacity, 4)
    meta_in = jnp.stack([meta[:, 0] * size + meta[:, 1], meta[:, 2], meta[:, 3]], axis=1)
    return arrived, meta_in


def group_size(axes):
    count = 1
    for axis in axes:
        count *= lax.axis_size(axis)
    return count


def sum_over(value, axes, send_type):
    count = group_size(axes)
    parts = lax.all_to_all(value.astype(send_type).reshape(count, -1), axes, 0, 0, tiled=True)
    total = jnp.sum(parts.astype(jnp.float32), axis=0, keepdims=True).astype(send_type)
    return total, count


def all_sum_a2a(value, axes):
    total, count = sum_over(value, axes, value.dtype)
    spread = lax.all_to_all(jnp.broadcast_to(total, (count, total.shape[1])), axes, 0, 0, tiled=True)
    return spread.reshape(value.shape)


def all_sum_pairs(value, axis, send_type):
    count = lax.axis_size(axis)
    if count & (count - 1):
        return lax.psum(value.astype(send_type), axis).astype(jnp.float32)
    total = value.astype(send_type).astype(jnp.float32)
    step = 1
    while step < count:
        pairs = [(i, i ^ step) for i in range(count)]
        other = lax.ppermute(total.astype(send_type), axis, pairs)
        total = total.astype(send_type).astype(jnp.float32) + other.astype(jnp.float32)
        step *= 2
    return total


def entries_pass(stacked, probe_now, amp_in, meta_in, tables):
    table_re, table_im, table_neg = tables
    length = probe_now.shape[-1]
    rows_all, size = stacked.shape[1], stacked.shape[2]
    within = jnp.arange(length, dtype=jnp.int32)
    row_at, col_at, valid = meta_in[:, 0], meta_in[:, 1], meta_in[:, 2]
    pick_rows = (
        (row_at[:, None, None] + within[None, :, None])
        == jnp.arange(rows_all, dtype=jnp.int32)[None, None, :]
    ) & (valid[:, None, None] > 0)
    pick_rows = pick_rows.astype(jnp.bfloat16)
    pick_cols = (
        (col_at[:, None, None] + within[None, None, :])
        == jnp.arange(size, dtype=jnp.int32)[None, :, None]
    ).astype(jnp.bfloat16)
    rows = jnp.einsum(
        "skq,xqc->xskc", pick_rows, stacked, preferred_element_type=jnp.float32
    ).astype(jnp.bfloat16)
    patch = jnp.einsum("xskc,scl->xskl", rows, pick_cols, preferred_element_type=jnp.float32)
    left, right = block_tables(tables[0], tables[1])
    held = (valid > 0).astype(jnp.int32)
    count = jnp.sum(held)
    place = jnp.where(held > 0, jnp.cumsum(held) - 1, count + jnp.cumsum(1 - held) - 1)
    slots = valid.shape[0]
    order = jnp.sum(
        (place[:, None] == jnp.arange(slots, dtype=jnp.int32)[None, :])
        * jnp.arange(slots, dtype=jnp.int32)[:, None],
        axis=0,
    )
    order = jnp.concatenate([order, count[None]]).astype(jnp.int32)
    update, probe_grad = entries_kernel(
        order, patch.astype(jnp.bfloat16), amp_in, probe_now, left, right
    )
    spread = jnp.einsum(
        "xskl,scl->xskc", update, pick_cols, preferred_element_type=jnp.float32
    ).astype(jnp.bfloat16)
    local_sum = jnp.einsum("skq,xskc->xqc", pick_rows, spread, preferred_element_type=jnp.float32)
    return local_sum, probe_grad


def one_step(tiles_now, probe_now, amp_in, meta_in, tables, batch_total):
    tiles_here, size = tiles_now.shape[1], tiles_now.shape[2]
    slots, length = amp_in.shape[0], amp_in.shape[-1]
    stacked = tiles_now.astype(jnp.bfloat16).reshape(2, tiles_here * size, size)
    chunk = max(d for d in range(1, min(slots, 24) + 1) if slots % d == 0)
    if chunk == slots:
        local_sum, probe_grad = entries_pass(stacked, probe_now, amp_in, meta_in, tables)
    else:

        def body(carry, piece):
            part_sum, part_grad = entries_pass(stacked, probe_now, piece[0], piece[1], tables)
            return (carry[0] + part_sum, carry[1] + part_grad), None

        start = (jnp.zeros(stacked.shape, jnp.float32), jnp.zeros(probe_now.shape, jnp.float32))
        pieces = (
            amp_in.reshape(slots // chunk, chunk, length, length),
            meta_in.reshape(slots // chunk, chunk, 3),
        )
        (local_sum, probe_grad), _ = lax.scan(body, start, pieces)
    local_sum = local_sum.reshape(tiles_now.shape)
    probe_re = probe_now[:, 0]
    probe_im = probe_now[:, 1]
    peak_power = jnp.max(jnp.sum(probe_re * probe_re + probe_im * probe_im, axis=0))
    summed = all_sum_pairs(local_sum, "pat", jnp.bfloat16)
    tiles_next = tiles_now + summed / peak_power
    grad_sum = all_sum_a2a(probe_grad, ("tile", "pat"))
    probe_next = probe_now + probe_rate * grad_sum / batch_total
    return (tiles_next, probe_next, probe_grad)


def on_device(amplitudes, batch_ids, scan_tile, scan_offset, object_tiles, probe):
    tables = dft_tables(probe.shape[-1])
    tiles_here, size = object_tiles.shape[1], object_tiles.shape[2]
    batch_total = batch_ids.shape[1] * lax.axis_size("tile") * lax.axis_size("pat")
    payload, meta = route(amplitudes, batch_ids, scan_tile, scan_offset, tiles_here)
    tiles_now = object_tiles
    probe_now = probe
    placed = lax.all_to_all(jnp.swapaxes(meta, 0, 1), "tile", 0, 0, tiled=True)
    arrived = lax.all_to_all(jnp.swapaxes(payload, 0, 1), "tile", 0, 0, tiled=True)
    for step_no in range(batch_ids.shape[0]):
        amp_in, meta_in = unpack(arrived[:, step_no], placed[:, step_no], size)
        tiles_now, probe_now, _ = one_step(tiles_now, probe_now, amp_in, meta_in, tables, batch_total)
    return (tiles_now, probe_now)


def solution(mesh):
    in_specs = (
        P(("tile", "pat"), None, None),
        P(None, ("tile", "pat")),
        P(None, ("tile", "pat"), None),
        P(None, ("tile", "pat"), None),
        P(None, "tile", None, None),
        P(),
    )
    out_specs = (P(None, "tile", None, None), P())
    return jax.shard_map(
        on_device, mesh=mesh, in_specs=in_specs, out_specs=out_specs, check_vma=False
    )
```
